128 devices in a mesh: dp: 32 (over y, z_lo, x), tensor: 4 (over z_hi, core).
Axes of the slice: x: 4, y: 4, z: 4 (z_hi: 2, z_lo: 2; z = z_hi * 2 + z_lo), core: 2. Of those that a mesh axis runs over, the one named last changes fastest.
Arguments:
- tokens: bfloat16 [32768, 4096], P('dp'), may hold values from -6 to 6
- grad_out: bfloat16 [32768, 2048], P('dp', 'tensor'), may hold values from -12 to 12
- w_query: bfloat16 [4096, 2048], P('dp', 'tensor'), may hold values from -2 to 2
- w_key: bfloat16 [4096, 512], P('dp', 'tensor'), may hold values from -2 to 2
- value_matrix: bfloat16 [4096, 512], P('dp', 'tensor'), may hold values from -0.09375 to 0.09375
Outputs:
- grad_tokens: bfloat16 [32768, 4096], P('dp', 'tensor')
- grad_query: bfloat16 [4096, 2048], P('dp', 'tensor')
- grad_key: bfloat16 [4096, 512], P('dp', 'tensor')
- grad_value: bfloat16 [4096, 512], P('dp', 'tensor')
The draws below stay inside these ranges and needn't reach their ends.
All inputs are finite; a program needn't handle non-finite values.
Results may differ from the reference program's by a relative error of at most 0.03.
The reference program's roundings to bfloat16 on the way (of `weights_b`, `dscore` and `part`) count: a program that leaves them out, or rounds other values in their place, can miss the bound.
Values may be sent and summed in bfloat16 or wider, within the bound.
No kernel may reach another device: no remote copies, remote signals or barrier semaphores. Data moves between devices by JAX's collectives and lax.ppermute only.
A program may use at most 192 MiB of HBM per device.

```python
import math
import jax
import jax.numpy as jnp
from jax import lax

MODEL_WIDTH = 4096
QUERY_HEADS = 16
KEY_VALUE_HEADS = 4
HEAD_SIZE = 128
LEN = 1024
TOKEN_COUNT = 32768
N_DP = 32
N_TENSOR = 4


def draw_w_key(key, part):
    drawn = jax.random.normal(jax.random.fold_in(key, 13), (MODEL_WIDTH, KEY_VALUE_HEADS * HEAD_SIZE), jnp.float32) / math.sqrt(MODEL_WIDTH)
    return jnp.clip(drawn, -2.0, 2.0).astype(jnp.bfloat16)


def draw_w_query(key, part):
    own_part = jax.random.normal(jax.random.fold_in(key, 11), (MODEL_WIDTH, QUERY_HEADS * HEAD_SIZE), jnp.float32) / math.sqrt(MODEL_WIDTH)
    return jnp.clip(own_part, -2.0, 2.0).astype(jnp.bfloat16)


def raised(result, stream_key, source, target, shards_of, factor):
    owner, partner = [(jnp.arange(result.shape[axis_at]) // (result.shape[axis_at] // shards_of)).reshape([-1 if axis == axis_at else 1 for axis in range(result.ndim)]) for axis_at in (source, target)]
    chosen = jax.random.permutation(stream_key, shards_of)[partner]
    strong = (owner == chosen) | (owner == (partner + shards_of // 2) % shards_of)
    return jnp.where(strong, factor * result, result)


def steps_of(rng, shape, pieces, low, high):
    level, own = 1.0, jax.random.fold_in(rng, 6)
    for position, parts in pieces:
        draws = jnp.exp(jax.random.uniform(jax.random.fold_in(own, position), (parts,), jnp.float32, low / len(pieces), high / len(pieces)))
        level = level * jnp.repeat(draws, shape[position] // parts).reshape([-1 if axis == position else 1 for axis in range(len(shape))])
    return level


def normal_values(own_key, extent, spread, reach, shards=(), held_as=jnp.bfloat16):
    entries = spread * jax.random.normal(own_key, extent, jnp.float32)
    if shards:
        entries = entries * steps_of(own_key, extent, shards, -0.22, 0.18)
    return jnp.clip(entries, -reach, reach).astype(held_as)


def noise_with(own_key, shape, spread, most, cuts, heavy, kind=jnp.bfloat16):
    array = spread * jax.random.normal(own_key, shape, jnp.float32)
    if cuts:
        array = array * steps_of(own_key, shape, cuts, -0.22, 0.18)
    return jnp.clip(raised(array, jax.random.fold_in(own_key, 3), *heavy), -most, most).astype(kind)


def setup_inputs(seed: int = 0) -> dict:
    key_list = jax.random.split(jax.random.key(seed), 6)
    tokens = noise_with(key_list[0], (TOKEN_COUNT, MODEL_WIDTH), 1.0, 6.0, ((0, 32),), (0, 1, 32, 2.75))
    grad_out = normal_values(key_list[1], (TOKEN_COUNT, QUERY_HEADS * HEAD_SIZE), 2.0, 12.0, ((0, 32), (1, 4)))
    w_query = draw_w_query(jax.random.fold_in(key_list[5], 71), 0)
    w_key = draw_w_key(jax.random.fold_in(key_list[5], 71), 0)
    value_matrix = normal_values(key_list[4], (MODEL_WIDTH, KEY_VALUE_HEADS * HEAD_SIZE), MODEL_WIDTH ** -0.5, 0.09375, ((0, 32), (1, 4)))
    return dict(tokens=tokens, grad_out=grad_out, w_query=w_query, w_key=w_key, value_matrix=value_matrix)


rope_base = 500000.0

def position_tables(length, head_dim):
    half_dim = head_dim // 2
    positions = jnp.arange(length, dtype=jnp.float32)
    inverse = jnp.power(jnp.float32(rope_base), -2.0 * jnp.arange(half_dim, dtype=jnp.float32) / head_dim)
    angles = positions[:, None] * inverse[None, :]
    cosine = jnp.concatenate([jnp.cos(angles), jnp.cos(angles)], axis=-1)[:, None, :]
    sine_table = jnp.concatenate([jnp.sin(angles), jnp.sin(angles)], axis=-1)[:, None, :]
    return (cosine, sine_table)

def half_turn(values):
    lower, upper = jnp.split(values, 2, axis=-1)
    return jnp.concatenate([-upper, lower], axis=-1)

def rotate_forward(values, cosine, sine_table):
    return values * cosine + half_turn(values) * sine_table

def rotate_back(grads, cosine, sine_table):
    return grads * cosine - half_turn(grads * sine_table)

def attention_backward(unrotated_query, unrotated_key, projected_value, upstream_flat, kv_heads):
    length = unrotated_query.shape[0]
    heads = unrotated_query.shape[1] // HEAD_SIZE
    group_size = heads // kv_heads
    cosine, sine_table = position_tables(length, HEAD_SIZE)
    query = rotate_forward(unrotated_query.reshape(length, heads, HEAD_SIZE), cosine, sine_table).astype(jnp.bfloat16)
    key = rotate_forward(unrotated_key.reshape(length, kv_heads, HEAD_SIZE), cosine, sine_table).astype(jnp.bfloat16)
    value = projected_value.reshape(length, kv_heads, HEAD_SIZE).astype(jnp.bfloat16)
    query_f = query.astype(jnp.float32).reshape(length, kv_heads, group_size, HEAD_SIZE)
    key_f = key.astype(jnp.float32)
    value_f = value.astype(jnp.float32)
    upstream = upstream_flat.astype(jnp.float32).reshape(length, kv_heads, group_size, HEAD_SIZE)
    scale = 1.0 / jnp.sqrt(jnp.float32(HEAD_SIZE))
    scores = jnp.einsum('ikgd,jkd->kgij', query_f, key_f) * scale
    positions = jnp.arange(length, dtype=jnp.int32)
    causal = positions[:, None] >= positions[None, :]
    scores = jnp.where(causal, scores, -jnp.inf)
    row_max = lax.optimization_barrier(jnp.max(scores, axis=-1, keepdims=True))
    weights = jnp.exp(scores - row_max)
    weights = weights / lax.optimization_barrier(jnp.sum(weights, axis=-1, keepdims=True))
    weights_b = weights.astype(jnp.bfloat16).astype(jnp.float32)
    dprob = jnp.einsum('ikgd,jkd->kgij', upstream, value_f)
    rowdot = lax.optimization_barrier(jnp.sum(weights * dprob, axis=-1, keepdims=True))
    dscore = (weights * (dprob - rowdot) * scale).astype(jnp.bfloat16).astype(jnp.float32)
    dquery = jnp.einsum('kgij,jkd->ikgd', dscore, key_f).reshape(length, heads, HEAD_SIZE)
    dkey = jnp.einsum('kgij,ikgd->jkd', dscore, query_f)
    dvalue = jnp.einsum('kgij,ikgd->jkd', weights_b, upstream)
    query_gradient = rotate_back(dquery, cosine, sine_table).astype(jnp.bfloat16).reshape(length, heads * HEAD_SIZE)
    key_gradient = rotate_back(dkey, cosine, sine_table).astype(jnp.bfloat16).reshape(length, kv_heads * HEAD_SIZE)
    value_gradient = dvalue.astype(jnp.bfloat16).reshape(length, kv_heads * HEAD_SIZE)
    return (query_gradient, key_gradient, value_gradient)

def reference(tokens, grad_out, w_query, w_key, value_matrix):
    query_cols = QUERY_HEADS * HEAD_SIZE // N_TENSOR
    key_value_columns = KEY_VALUE_HEADS * HEAD_SIZE // N_TENSOR

    def one_sequence(inputs):
        seq_tokens, sequence_gradients = inputs
        unrotated_query = jnp.dot(seq_tokens, w_query, preferred_element_type=jnp.float32)
        unrotated_key = jnp.dot(seq_tokens, w_key, preferred_element_type=jnp.float32)
        projected_value = jnp.dot(seq_tokens, value_matrix, preferred_element_type=jnp.float32)
        query_gradient, key_gradient, value_gradient = attention_backward(unrotated_query, unrotated_key, projected_value, sequence_gradients, KEY_VALUE_HEADS)
        summed = jnp.zeros((LEN, MODEL_WIDTH), jnp.float32)
        for group in range(N_TENSOR):
            q_lo = group * query_cols
            k_lo = group * key_value_columns
            part_sum = jnp.dot(query_gradient[:, q_lo:q_lo + query_cols], w_query[:, q_lo:q_lo + query_cols].T, preferred_element_type=jnp.float32)
            part_sum = part_sum + jnp.dot(key_gradient[:, k_lo:k_lo + key_value_columns], w_key[:, k_lo:k_lo + key_value_columns].T, preferred_element_type=jnp.float32)
            part_sum = part_sum + jnp.dot(value_gradient[:, k_lo:k_lo + key_value_columns], value_matrix[:, k_lo:k_lo + key_value_columns].T, preferred_element_type=jnp.float32)
            rounded = lax.optimization_barrier(part_sum.astype(jnp.bfloat16))
            summed = summed + rounded.astype(jnp.float32)
        return (query_gradient, key_gradient, value_gradient, summed.astype(jnp.bfloat16))
    seq_tokens = tokens.reshape(N_DP, LEN, MODEL_WIDTH)
    sequence_gradients = grad_out.reshape(N_DP, LEN, QUERY_HEADS * HEAD_SIZE)
    query_gradient, key_gradient, value_gradient, grad_tokens = lax.map(one_sequence, (seq_tokens, sequence_gradients))
    query_gradient = query_gradient.reshape(TOKEN_COUNT, QUERY_HEADS * HEAD_SIZE)
    key_gradient = key_gradient.reshape(TOKEN_COUNT, KEY_VALUE_HEADS * HEAD_SIZE)
    value_gradient = value_gradient.reshape(TOKEN_COUNT, KEY_VALUE_HEADS * HEAD_SIZE)
    grad_tokens = grad_tokens.reshape(TOKEN_COUNT, MODEL_WIDTH)
    tokens_t = tokens.T
    grad_query = jnp.dot(tokens_t, query_gradient, preferred_element_type=jnp.float32).astype(jnp.bfloat16)
    grad_key = jnp.dot(tokens_t, key_gradient, preferred_element_type=jnp.float32).astype(jnp.bfloat16)
    grad_value = jnp.dot(tokens_t, value_gradient, preferred_element_type=jnp.float32).astype(jnp.bfloat16)
    return (grad_tokens, grad_query, grad_key, grad_value)
```

```python
import jax
import jax.numpy as jnp
from jax import lax
from jax.sharding import Mesh
from jax.sharding import PartitionSpec as P

MODEL_WIDTH = 4096
HEAD_SIZE = 128


rope_base = 500000.0


def position_tables(length, head_dim):
    half_dim = head_dim // 2
    positions = jnp.arange(length, dtype=jnp.float32)
    inverse = jnp.power(
        jnp.float32(rope_base), -2.0 * jnp.arange(half_dim, dtype=jnp.float32) / head_dim
    )
    angles = positions[:, None] * inverse[None, :]
    cosine = jnp.concatenate([jnp.cos(angles), jnp.cos(angles)], axis=-1)[:, None, :]
    sine_table = jnp.concatenate([jnp.sin(angles), jnp.sin(angles)], axis=-1)[:, None, :]
    return (cosine, sine_table)


def half_turn(values):
    lower, upper = jnp.split(values, 2, axis=-1)
    return jnp.concatenate([-upper, lower], axis=-1)


def rotate_forward(values, cosine, sine_table):
    return values * cosine + half_turn(values) * sine_table


def rotate_back(grads, cosine, sine_table):
    return grads * cosine - half_turn(grads * sine_table)


def attention_backward(unrotated_query, unrotated_key, projected_value, upstream_flat, kv_heads):
    length = unrotated_query.shape[0]
    heads = unrotated_query.shape[1] // HEAD_SIZE
    group_size = heads // kv_heads
    cosine, sine_table = position_tables(length, HEAD_SIZE)
    query = rotate_forward(
        unrotated_query.reshape(length, heads, HEAD_SIZE), cosine, sine_table
    ).astype(jnp.bfloat16)
    key = rotate_forward(
        unrotated_key.reshape(length, kv_heads, HEAD_SIZE), cosine, sine_table
    ).astype(jnp.bfloat16)
    value = projected_value.reshape(length, kv_heads, HEAD_SIZE).astype(jnp.bfloat16)
    query_grouped = query.reshape(length, kv_heads, group_size, HEAD_SIZE)
    upstream = upstream_flat.reshape(length, kv_heads, group_size, HEAD_SIZE)
    scale = 1.0 / jnp.sqrt(jnp.float32(HEAD_SIZE))
    scores = (
        jnp.einsum("ikgd,jkd->kgij", query_grouped, key, preferred_element_type=jnp.float32) * scale
    )
    positions = jnp.arange(length, dtype=jnp.int32)
    causal = positions[:, None] >= positions[None, :]
    scores = jnp.where(causal, scores, -jnp.inf)
    row_max = jnp.max(scores, axis=-1, keepdims=True)
    weights = jnp.exp(scores - row_max)
    weights = weights / jnp.sum(weights, axis=-1, keepdims=True)
    weights_b = weights.astype(jnp.bfloat16)
    dprob = jnp.einsum("ikgd,jkd->kgij", upstream, value, preferred_element_type=jnp.float32)
    rowdot = jnp.sum(weights * dprob, axis=-1, keepdims=True)
    dscore = (weights * (dprob - rowdot) * scale).astype(jnp.bfloat16)
    dquery = jnp.einsum("kgij,jkd->ikgd", dscore, key, preferred_element_type=jnp.float32).reshape(
        length, heads, HEAD_SIZE
    )
    dkey = jnp.einsum("kgij,ikgd->jkd", dscore, query_grouped, preferred_element_type=jnp.float32)
    dvalue = jnp.einsum("kgij,ikgd->jkd", weights_b, upstream, preferred_element_type=jnp.float32)
    query_gradient = (
        rotate_back(dquery, cosine, sine_table)
        .astype(jnp.bfloat16)
        .reshape(length, heads * HEAD_SIZE)
    )
    key_gradient = (
        rotate_back(dkey, cosine, sine_table)
        .astype(jnp.bfloat16)
        .reshape(length, kv_heads * HEAD_SIZE)
    )
    value_gradient = dvalue.astype(jnp.bfloat16).reshape(length, kv_heads * HEAD_SIZE)
    return (query_gradient, key_gradient, value_gradient)


DP_AXES = ("y", "zl", "x")
TP_AXES = ("zh", "c")


def gather_rows(block):
    block = lax.all_gather(block, "x", axis=0, tiled=True)
    block = lax.all_gather(block, "zl", axis=0, tiled=True)
    return lax.all_gather(block, "y", axis=0, tiled=True)


def scatter_rows(block):
    block = lax.psum_scatter(block, "y", scatter_dimension=0, tiled=True)
    block = lax.psum_scatter(block, "zl", scatter_dimension=0, tiled=True)
    return lax.psum_scatter(block, "x", scatter_dimension=0, tiled=True)


def body(tokens, grad_out, w_query, w_key, value_matrix):
    query_cols = w_query.shape[1]
    key_value_columns = w_key.shape[1]
    kv_dev = key_value_columns // HEAD_SIZE
    weights_all = gather_rows(jnp.concatenate([w_query, w_key, value_matrix], axis=1))
    projected = jnp.dot(tokens, weights_all, preferred_element_type=jnp.float32)
    unrotated_query = projected[:, :query_cols]
    unrotated_key = projected[:, query_cols : query_cols + key_value_columns]
    projected_value = projected[:, query_cols + key_value_columns :]
    query_gradient, key_gradient, value_gradient = attention_backward(
        unrotated_query, unrotated_key, projected_value, grad_out, kv_dev
    )
    combined = jnp.concatenate([query_gradient, key_gradient, value_gradient], axis=1)
    partial_sum = lax.dot_general(
        combined, weights_all, (((1,), (1,)), ((), ())), preferred_element_type=jnp.float32
    )
    grad_tokens = lax.psum_scatter(
        partial_sum.astype(jnp.bfloat16), TP_AXES, scatter_dimension=1, tiled=True
    )
    grads_all = scatter_rows(
        lax.dot_general(
            tokens, combined, (((0,), (0,)), ((), ())), preferred_element_type=jnp.float32
        ).astype(jnp.bfloat16)
    )
    grad_query = grads_all[:, :query_cols]
    grad_key = grads_all[:, query_cols : query_cols + key_value_columns]
    grad_value = grads_all[:, query_cols + key_value_columns :]
    return (grad_tokens, grad_query, grad_key, grad_value)


def solution(mesh):
    view = Mesh(mesh.devices.reshape(4, 2, 4, 2, 2), DP_AXES + TP_AXES)
    rows = P(DP_AXES, None)
    split = P(DP_AXES, TP_AXES)
    in_specs = (rows, split, split, split, split)
    out_specs = (split, split, split, split)
    return jax.shard_map(body, mesh=view, in_specs=in_specs, out_specs=out_specs, check_vma=False)
```

```python
import jax
import jax.numpy as jnp
from jax import lax
from jax.sharding import Mesh
from jax.sharding import PartitionSpec as P

MODEL_WIDTH = 4096
HEAD_SIZE = 128


rope_base = 500000.0


def position_tables(length, head_dim):
    half_dim = head_dim // 2
    positions = jnp.arange(length, dtype=jnp.float32)
    inverse = jnp.power(
        jnp.float32(rope_base), -2.0 * jnp.arange(half_dim, dtype=jnp.float32) / head_dim
    )
    angles = positions[:, None] * inverse[None, :]
    cosine = jnp.concatenate([jnp.cos(angles), jnp.cos(angles)], axis=-1)[:, None, :]
    sine_table = jnp.concatenate([jnp.sin(angles), jnp.sin(angles)], axis=-1)[:, None, :]
    return (cosine, sine_table)


def half_turn(values):
    lower, upper = jnp.split(values, 2, axis=-1)
    return jnp.concatenate([-upper, lower], axis=-1)


def rotate_forward(values, cosine, sine_table):
    return values * cosine + half_turn(values) * sine_table


def rotate_back(grads, cosine, sine_table):
    return grads * cosine - half_turn(grads * sine_table)


def attention_backward(unrotated_query, unrotated_key, projected_value, upstream_flat, kv_heads):
    length = unrotated_query.shape[0]
    heads = unrotated_query.shape[1] // HEAD_SIZE
    group_size = heads // kv_heads
    cosine, sine_table = position_tables(length, HEAD_SIZE)
    query = rotate_forward(
        unrotated_query.reshape(length, heads, HEAD_SIZE), cosine, sine_table
    ).astype(jnp.bfloat16)
    key = rotate_forward(
        unrotated_key.reshape(length, kv_heads, HEAD_SIZE), cosine, sine_table
    ).astype(jnp.bfloat16)
    value = projected_value.reshape(length, kv_heads, HEAD_SIZE).astype(jnp.bfloat16)
    query_grouped = query.reshape(length, kv_heads, group_size, HEAD_SIZE)
    upstream = upstream_flat.reshape(length, kv_heads, group_size, HEAD_SIZE)
    scale = 1.0 / jnp.sqrt(jnp.float32(HEAD_SIZE))
    scores = (
        jnp.einsum("ikgd,jkd->kgij", query_grouped, key, preferred_element_type=jnp.float32) * scale
    )
    positions = jnp.arange(length, dtype=jnp.int32)
    causal = positions[:, None] >= positions[None, :]
    scores = jnp.where(causal, scores, -jnp.inf)
    row_max = jnp.max(scores, axis=-1, keepdims=True)
    weights = jnp.exp(scores - row_max)
    weights = weights / jnp.sum(weights, axis=-1, keepdims=True)
    weights_b = weights.astype(jnp.bfloat16)
    dprob = jnp.einsum("ikgd,jkd->kgij", upstream, value, preferred_element_type=jnp.float32)
    rowdot = jnp.sum(weights * dprob, axis=-1, keepdims=True)
    dscore = (weights * (dprob - rowdot) * scale).astype(jnp.bfloat16)
    dquery = jnp.einsum("kgij,jkd->ikgd", dscore, key, preferred_element_type=jnp.float32).reshape(
        length, heads, HEAD_SIZE
    )
    dkey = jnp.einsum("kgij,ikgd->jkd", dscore, query_grouped, preferred_element_type=jnp.float32)
    dvalue = jnp.einsum("kgij,ikgd->jkd", weights_b, upstream, preferred_element_type=jnp.float32)
    query_gradient = (
        rotate_back(dquery, cosine, sine_table)
        .astype(jnp.bfloat16)
        .reshape(length, heads * HEAD_SIZE)
    )
    key_gradient = (
        rotate_back(dkey, cosine, sine_table)
        .astype(jnp.bfloat16)
        .reshape(length, kv_heads * HEAD_SIZE)
    )
    value_gradient = dvalue.astype(jnp.bfloat16).reshape(length, kv_heads * HEAD_SIZE)
    return (query_gradient, key_gradient, value_gradient)


DP_AXES = ("y", "zl", "x")
TP_AXES = ("zh", "c")


def _shift(x, axis, n, step):
    return lax.ppermute(x, axis, [(k, (k + step) % n) for k in range(n)])


def _place(parts, idx, n, dim):
    shape = list(parts[0].shape)
    size = shape[dim]
    shape[dim] = size * n
    out = jnp.zeros(shape, parts[0].dtype)
    for o, p in enumerate(parts):
        start = [0] * len(shape)
        start[dim] = ((idx + o) % n) * size
        out = lax.dynamic_update_slice(out, p, start)
    return out


def ring_gather(x, axis, n, dim):
    idx = lax.axis_index(axis)
    if n == 1:
        return x
    if n == 2:
        return _place([x, _shift(x, axis, 2, 1)], idx, 2, dim)
    assert n == 4
    from_left = _shift(x, axis, 4, 1)
    from_right = _shift(x, axis, 4, -1)
    half = x.shape[-1] // 2
    far_a = _shift(from_right[..., :half], axis, 4, -1)
    far_b = _shift(from_left[..., half:], axis, 4, 1)
    far = jnp.concatenate([far_a, far_b], axis=-1)
    return _place([x, from_right, far, from_left], idx, 4, dim)


def _take(x, pos, dim, n):
    size = x.shape[dim] // n
    return lax.dynamic_slice_in_dim(x, pos * size, size, dim)


def _add(a, b):
    return (a.astype(jnp.float32) + b.astype(jnp.float32)).astype(a.dtype)


def ring_scatter(x, axis, n, dim):
    idx = lax.axis_index(axis)
    if n == 1:
        return x
    if n == 2:
        return _add(_take(x, idx, dim, 2), _shift(_take(x, (idx + 1) % 2, dim, 2), axis, 2, 1))
    assert n == 4
    half = x.shape[-1] // 2
    far = _take(x, (idx + 2) % 4, dim, 4)
    to_right = _take(x, (idx + 1) % 4, dim, 4)
    to_left = _take(x, (idx + 3) % 4, dim, 4)
    got_a = _shift(far[..., :half], axis, 4, 1)
    got_b = _shift(far[..., half:], axis, 4, -1)
    to_right = jnp.concatenate([_add(to_right[..., :half], got_a), to_right[..., half:]], axis=-1)
    to_left = jnp.concatenate([to_left[..., :half], _add(to_left[..., half:], got_b)], axis=-1)
    mine = _take(x, idx, dim, 4)
    s = _add(mine, _shift(to_right, axis, 4, 1))
    return _add(s, _shift(to_left, axis, 4, -1))


def dp_gather(w, sizes=(4, 2, 4)):
    ny, nz, nx = sizes
    r, c = w.shape
    a = w.reshape(1, 1, 1, r, c)
    a = ring_gather(a, "zl", nz, 1)
    h = c // 2
    s1 = ring_gather(ring_gather(a[..., :h], "x", nx, 2), "y", ny, 0)
    s2 = ring_gather(ring_gather(a[..., h:], "y", ny, 0), "x", nx, 2)
    return jnp.concatenate([s1, s2], axis=-1).reshape(ny * nz * nx * r, c)


def dp_scatter(g, sizes=(4, 2, 4)):
    ny, nz, nx = sizes
    R, c = g.shape
    r = R // (ny * nz * nx)
    a = g.reshape(ny, nz, nx, r, c)
    h = c // 2
    s1 = ring_scatter(ring_scatter(a[..., :h], "y", ny, 0), "x", nx, 2)
    s2 = ring_scatter(ring_scatter(a[..., h:], "x", nx, 2), "y", ny, 0)
    a = jnp.concatenate([s1, s2], axis=-1)
    a = ring_scatter(a, "zl", nz, 1)
    return a.reshape(r, c)


def tp_scatter(t, sizes=(2, 2)):
    nh, nc = sizes
    rows, wdt = t.shape
    a = t.reshape(rows, nh, nc, wdt // (nh * nc))
    a = ring_scatter(a, "c", nc, 2)
    a = ring_scatter(a, "zh", nh, 1)
    return a.reshape(rows, wdt // (nh * nc))


def body(tokens, grad_out, w_query, w_key, value_matrix):
    query_cols = w_query.shape[1]
    key_value_columns = w_key.shape[1]
    kv_dev = key_value_columns // HEAD_SIZE
    weights_all = dp_gather(jnp.concatenate([w_query, w_key, value_matrix], axis=1))
    projected = jnp.dot(tokens, weights_all, preferred_element_type=jnp.float32)
    unrotated_query = projected[:, :query_cols]
    unrotated_key = projected[:, query_cols : query_cols + key_value_columns]
    projected_value = projected[:, query_cols + key_value_columns :]
    query_gradient, key_gradient, value_gradient = attention_backward(
        unrotated_query, unrotated_key, projected_value, grad_out, kv_dev
    )
    combined = jnp.concatenate([query_gradient, key_gradient, value_gradient], axis=1)
    partial_sum = lax.dot_general(
        combined, weights_all, (((1,), (1,)), ((), ())), preferred_element_type=jnp.float32
    )
    grad_tokens = lax.psum_scatter(
        partial_sum.astype(jnp.bfloat16), TP_AXES, scatter_dimension=1, tiled=True
    )
    grads_all = dp_scatter(
        lax.dot_general(
            tokens, combined, (((0,), (0,)), ((), ())), preferred_element_type=jnp.float32
        ).astype(jnp.bfloat16)
    )
    grad_query = grads_all[:, :query_cols]
    grad_key = grads_all[:, query_cols : query_cols + key_value_columns]
    grad_value = grads_all[:, query_cols + key_value_columns :]
    return (grad_tokens, grad_query, grad_key, grad_value)


def solution(mesh):
    view = Mesh(mesh.devices.reshape(4, 2, 4, 2, 2), DP_AXES + TP_AXES)
    rows = P(DP_AXES, None)
    split = P(DP_AXES, TP_AXES)
    in_specs = (rows, split, split, split, split)
    out_specs = (split, split, split, split)
    return jax.shard_map(body, mesh=view, in_specs=in_specs, out_specs=out_specs, check_vma=False)
```

```python
import jax
import jax.numpy as jnp
from jax import lax
from jax.sharding import Mesh
from jax.sharding import PartitionSpec as P

MODEL_WIDTH = 4096
HEAD_SIZE = 128


rope_base = 500000.0


def position_tables(length, head_dim):
    half_dim = head_dim // 2
    positions = jnp.arange(length, dtype=jnp.float32)
    inverse = jnp.power(
        jnp.float32(rope_base), -2.0 * jnp.arange(half_dim, dtype=jnp.float32) / head_dim
    )
    angles = positions[:, None] * inverse[None, :]
    cosine = jnp.concatenate([jnp.cos(angles), jnp.cos(angles)], axis=-1)[:, None, :]
    sine_table = jnp.concatenate([jnp.sin(angles), jnp.sin(angles)], axis=-1)[:, None, :]
    return (cosine, sine_table)


def half_turn(values):
    lower, upper = jnp.split(values, 2, axis=-1)
    return jnp.concatenate([-upper, lower], axis=-1)


def rotate_forward(values, cosine, sine_table):
    return values * cosine + half_turn(values) * sine_table


def rotate_back(grads, cosine, sine_table):
    return grads * cosine - half_turn(grads * sine_table)


def attention_backward(unrotated_query, unrotated_key, projected_value, upstream_flat, kv_heads):
    length = unrotated_query.shape[0]
    heads = unrotated_query.shape[1] // HEAD_SIZE
    group_size = heads // kv_heads
    cosine, sine_table = position_tables(length, HEAD_SIZE)
    query = rotate_forward(
        unrotated_query.reshape(length, heads, HEAD_SIZE), cosine, sine_table
    ).astype(jnp.bfloat16)
    key = rotate_forward(
        unrotated_key.reshape(length, kv_heads, HEAD_SIZE), cosine, sine_table
    ).astype(jnp.bfloat16)
    value = projected_value.reshape(length, kv_heads, HEAD_SIZE).astype(jnp.bfloat16)
    query_grouped = query.reshape(length, kv_heads, group_size, HEAD_SIZE)
    upstream = upstream_flat.reshape(length, kv_heads, group_size, HEAD_SIZE)
    scale = 1.0 / jnp.sqrt(jnp.float32(HEAD_SIZE))
    scores = (
        jnp.einsum("ikgd,jkd->kgij", query_grouped, key, preferred_element_type=jnp.float32) * scale
    )
    positions = jnp.arange(length, dtype=jnp.int32)
    causal = positions[:, None] >= positions[None, :]
    scores = jnp.where(causal, scores, -jnp.inf)
    row_max = jnp.max(scores, axis=-1, keepdims=True)
    weights = jnp.exp(scores - row_max)
    weights = weights / jnp.sum(weights, axis=-1, keepdims=True)
    weights_b = weights.astype(jnp.bfloat16)
    dprob = jnp.einsum("ikgd,jkd->kgij", upstream, value, preferred_element_type=jnp.float32)
    rowdot = jnp.sum(weights * dprob, axis=-1, keepdims=True)
    dscore = (weights * (dprob - rowdot) * scale).astype(jnp.bfloat16)
    dquery = jnp.einsum("kgij,jkd->ikgd", dscore, key, preferred_element_type=jnp.float32).reshape(
        length, heads, HEAD_SIZE
    )
    dkey = jnp.einsum("kgij,ikgd->jkd", dscore, query_grouped, preferred_element_type=jnp.float32)
    dvalue = jnp.einsum("kgij,ikgd->jkd", weights_b, upstream, preferred_element_type=jnp.float32)
    query_gradient = (
        rotate_back(dquery, cosine, sine_table)
        .astype(jnp.bfloat16)
        .reshape(length, heads * HEAD_SIZE)
    )
    key_gradient = (
        rotate_back(dkey, cosine, sine_table)
        .astype(jnp.bfloat16)
        .reshape(length, kv_heads * HEAD_SIZE)
    )
    value_gradient = dvalue.astype(jnp.bfloat16).reshape(length, kv_heads * HEAD_SIZE)
    return (query_gradient, key_gradient, value_gradient)


DP_AXES = ("y", "zl", "x")
TP_AXES = ("zh", "c")


def _shift(x, axis, n, step):
    return lax.ppermute(x, axis, [(k, (k + step) % n) for k in range(n)])


def _place(parts, idx, n, dim):
    shape = list(parts[0].shape)
    size = shape[dim]
    shape[dim] = size * n
    out = jnp.zeros(shape, parts[0].dtype)
    for o, p in enumerate(parts):
        start = [0] * len(shape)
        start[dim] = ((idx + o) % n) * size
        out = lax.dynamic_update_slice(out, p, start)
    return out


def ring_gather(x, axis, n, dim):
    idx = lax.axis_index(axis)
    if n == 1:
        return x
    if n == 2:
        return _place([x, _shift(x, axis, 2, 1)], idx, 2, dim)
    assert n == 4
    from_left = _shift(x, axis, 4, 1)
    from_right = _shift(x, axis, 4, -1)
    half = x.shape[-1] // 2
    far_a = _shift(from_right[..., :half], axis, 4, -1)
    far_b = _shift(from_left[..., half:], axis, 4, 1)
    far = jnp.concatenate([far_a, far_b], axis=-1)
    return _place([x, from_right, far, from_left], idx, 4, dim)


def _take(x, pos, dim, n):
    size = x.shape[dim] // n
    return lax.dynamic_slice_in_dim(x, pos * size, size, dim)


def _add(a, b):
    return (a.astype(jnp.float32) + b.astype(jnp.float32)).astype(a.dtype)


def _halves(x, hdim):
    half = x.shape[hdim] // 2
    return (lax.slice_in_dim(x, 0, half, axis=hdim), lax.slice_in_dim(x, half, 2 * half, axis=hdim))


def ring_scatter(x, axis, n, take, hdim=0):
    idx = lax.axis_index(axis)
    if n == 2:
        return _add(take(x, idx), _shift(take(x, (idx + 1) % 2), axis, 2, 1))
    assert n == 4
    far_a, far_b = _halves(take(x, (idx + 2) % 4), hdim)
    right_a, right_b = _halves(take(x, (idx + 1) % 4), hdim)
    left_a, left_b = _halves(take(x, (idx + 3) % 4), hdim)
    got_a = _shift(far_a, axis, 4, 1)
    got_b = _shift(far_b, axis, 4, -1)
    to_right = jnp.concatenate([_add(right_a, got_a), right_b], axis=hdim)
    to_left = jnp.concatenate([left_a, _add(left_b, got_b)], axis=hdim)
    mine = take(x, idx)
    s = _add(mine, _shift(to_right, axis, 4, 1))
    return _add(s, _shift(to_left, axis, 4, -1))


def _cols(starts, width):
    def take(x, j):
        runs = [lax.dynamic_slice_in_dim(x, s(j), width, axis=1) for s in starts]
        return runs[0] if len(runs) == 1 else jnp.concatenate(runs, axis=1)

    return take


def dp_gather(w, sizes=(4, 2, 4)):
    ny, nz, nx = sizes
    r, c = w.shape
    a = w.reshape(1, 1, 1, r, c)
    a = ring_gather(a, "zl", nz, 1)
    h = c // 2
    s1 = ring_gather(ring_gather(a[..., :h], "x", nx, 2), "y", ny, 0)
    s2 = ring_gather(ring_gather(a[..., h:], "y", ny, 0), "x", nx, 2)
    return jnp.concatenate([s1, s2], axis=-1).reshape(ny * nz * nx * r, c)


def dp_scatter_t(g, sizes=(4, 2, 4)):
    ny, nz, nx = sizes
    c, R = g.shape
    r = R // (ny * nz * nx)
    h = c // 2
    zx = nz * nx * r
    s1 = ring_scatter(g[:h], "y", ny, _cols([lambda j: j * zx], zx))
    s1 = ring_scatter(s1, "x", nx, _cols([lambda j, z=z: z * nx * r + j * r for z in range(nz)], r))
    s2 = ring_scatter(
        g[h:], "x", nx,
        _cols([lambda j, k=k: k * nx * r + j * r for k in range(ny * nz)], r),
    )
    s2 = ring_scatter(s2, "y", ny, _cols([lambda j: j * nz * r], nz * r))
    a = jnp.concatenate([s1, s2], axis=0)
    a = ring_scatter(a, "zl", nz, _cols([lambda j: j * r], r))
    return a.T


def body(tokens, grad_out, w_query, w_key, value_matrix):
    query_cols = w_query.shape[1]
    key_value_columns = w_key.shape[1]
    kv_dev = key_value_columns // HEAD_SIZE
    weights_all = dp_gather(jnp.concatenate([w_query, w_key, value_matrix], axis=1))
    projected = jnp.dot(tokens, weights_all, preferred_element_type=jnp.float32)
    unrotated_query = projected[:, :query_cols]
    unrotated_key = projected[:, query_cols : query_cols + key_value_columns]
    projected_value = projected[:, query_cols + key_value_columns :]
    query_gradient, key_gradient, value_gradient = attention_backward(
        unrotated_query, unrotated_key, projected_value, grad_out, kv_dev
    )
    combined = jnp.concatenate([query_gradient, key_gradient, value_gradient], axis=1)
    partial_sum = lax.dot_general(
        combined, weights_all, (((1,), (1,)), ((), ())), preferred_element_type=jnp.float32
    )
    grad_tokens = lax.psum_scatter(
        partial_sum.astype(jnp.bfloat16), TP_AXES, scatter_dimension=1, tiled=True
    )
    grads_all = dp_scatter_t(
        lax.dot_general(
            combined, tokens, (((0,), (0,)), ((), ())), preferred_element_type=jnp.float32
        ).astype(jnp.bfloat16)
    )
    grad_query = grads_all[:, :query_cols]
    grad_key = grads_all[:, query_cols : query_cols + key_value_columns]
    grad_value = grads_all[:, query_cols + key_value_columns :]
    return (grad_tokens, grad_query, grad_key, grad_value)


def solution(mesh):
    view = Mesh(mesh.devices.reshape(4, 2, 4, 2, 2), DP_AXES + TP_AXES)
    rows = P(DP_AXES, None)
    split = P(DP_AXES, TP_AXES)
    in_specs = (rows, split, split, split, split)
    out_specs = (split, split, split, split)
    return jax.shard_map(body, mesh=view, in_specs=in_specs, out_specs=out_specs, check_vma=False)
```

```python
import jax
import jax.numpy as jnp
from jax import lax
from jax.sharding import Mesh
from jax.sharding import PartitionSpec as P

MODEL_WIDTH = 4096
HEAD_SIZE = 128


rope_base = 500000.0


def position_tables(length, head_dim):
    half_dim = head_dim // 2
    positions = jnp.arange(length, dtype=jnp.float32)
    inverse = jnp.power(
        jnp.float32(rope_base), -2.0 * jnp.arange(half_dim, dtype=jnp.float32) / head_dim
    )
    angles = positions[:, None] * inverse[None, :]
    cosine = jnp.concatenate([jnp.cos(angles), jnp.cos(angles)], axis=-1)[:, None, :]
    sine_table = jnp.concatenate([jnp.sin(angles), jnp.sin(angles)], axis=-1)[:, None, :]
    return (cosine, sine_table)


def half_turn(values):
    lower, upper = jnp.split(values, 2, axis=-1)
    return jnp.concatenate([-upper, lower], axis=-1)


def rotate_forward(values, cosine, sine_table):
    return values * cosine + half_turn(values) * sine_table


def rotate_back(grads, cosine, sine_table):
    return grads * cosine - half_turn(grads * sine_table)


def attention_part(unrotated_query, key, value, upstream_flat, cosine, sine_table):
    length = unrotated_query.shape[0]
    heads = unrotated_query.shape[1] // HEAD_SIZE
    query = rotate_forward(
        unrotated_query.reshape(length, heads, HEAD_SIZE), cosine, sine_table
    ).astype(jnp.bfloat16)
    query_grouped = query.reshape(length, 1, heads, HEAD_SIZE)
    upstream = upstream_flat.reshape(length, 1, heads, HEAD_SIZE)
    scale = 1.0 / jnp.sqrt(jnp.float32(HEAD_SIZE))
    scores = (
        jnp.einsum("ikgd,jkd->kgij", query_grouped, key, preferred_element_type=jnp.float32) * scale
    )
    positions = jnp.arange(length, dtype=jnp.int32)
    causal = positions[:, None] >= positions[None, :]
    scores = jnp.where(causal, scores, -jnp.inf)
    row_max = jnp.max(scores, axis=-1, keepdims=True)
    weights = jnp.exp(scores - row_max)
    weights = weights / jnp.sum(weights, axis=-1, keepdims=True)
    weights_b = weights.astype(jnp.bfloat16)
    dprob = jnp.einsum("ikgd,jkd->kgij", upstream, value, preferred_element_type=jnp.float32)
    rowdot = jnp.sum(weights * dprob, axis=-1, keepdims=True)
    dscore = (weights * (dprob - rowdot) * scale).astype(jnp.bfloat16)
    dquery = jnp.einsum("kgij,jkd->ikgd", dscore, key, preferred_element_type=jnp.float32).reshape(
        length, heads, HEAD_SIZE
    )
    dkey = jnp.einsum("kgij,ikgd->jkd", dscore, query_grouped, preferred_element_type=jnp.float32)
    dvalue = jnp.einsum("kgij,ikgd->jkd", weights_b, upstream, preferred_element_type=jnp.float32)
    query_gradient = (
        rotate_back(dquery, cosine, sine_table)
        .astype(jnp.bfloat16)
        .reshape(length, heads * HEAD_SIZE)
    )
    return query_gradient, dkey, dvalue


DP_AXES = ("y", "zl", "x")
TP_AXES = ("zh", "c")


def _shift(x, axis, n, step):
    return lax.ppermute(x, axis, [(k, (k + step) % n) for k in range(n)])


def _place(parts, idx, n, dim):
    shape = list(parts[0].shape)
    size = shape[dim]
    shape[dim] = size * n
    out = jnp.zeros(shape, parts[0].dtype)
    for o, p in enumerate(parts):
        start = [0] * len(shape)
        start[dim] = ((idx + o) % n) * size
        out = lax.dynamic_update_slice(out, p, start)
    return out


def ring_gather(x, axis, n, dim):
    idx = lax.axis_index(axis)
    if n == 1:
        return x
    if n == 2:
        return _place([x, _shift(x, axis, 2, 1)], idx, 2, dim)
    assert n == 4
    from_left = _shift(x, axis, 4, 1)
    from_right = _shift(x, axis, 4, -1)
    half = x.shape[-1] // 2
    far_a = _shift(from_right[..., :half], axis, 4, -1)
    far_b = _shift(from_left[..., half:], axis, 4, 1)
    far = jnp.concatenate([far_a, far_b], axis=-1)
    return _place([x, from_right, far, from_left], idx, 4, dim)


def _take(x, pos, dim, n):
    size = x.shape[dim] // n
    return lax.dynamic_slice_in_dim(x, pos * size, size, dim)


def _add(a, b):
    return (a.astype(jnp.float32) + b.astype(jnp.float32)).astype(a.dtype)


def _halves(x, hdim):
    half = x.shape[hdim] // 2
    return (lax.slice_in_dim(x, 0, half, axis=hdim), lax.slice_in_dim(x, half, 2 * half, axis=hdim))


def ring_scatter(x, axis, n, take, hdim=0):
    idx = lax.axis_index(axis)
    if n == 2:
        return _add(take(x, idx), _shift(take(x, (idx + 1) % 2), axis, 2, 1))
    assert n == 4
    far_a, far_b = _halves(take(x, (idx + 2) % 4), hdim)
    right_a, right_b = _halves(take(x, (idx + 1) % 4), hdim)
    left_a, left_b = _halves(take(x, (idx + 3) % 4), hdim)
    got_a = _shift(far_a, axis, 4, 1)
    got_b = _shift(far_b, axis, 4, -1)
    to_right = jnp.concatenate([_add(right_a, got_a), right_b], axis=hdim)
    to_left = jnp.concatenate([left_a, _add(left_b, got_b)], axis=hdim)
    mine = take(x, idx)
    s = _add(mine, _shift(to_right, axis, 4, 1))
    return _add(s, _shift(to_left, axis, 4, -1))


def _cols(starts, width):
    def take(x, j):
        runs = [lax.dynamic_slice_in_dim(x, s(j), width, axis=1) for s in starts]
        return runs[0] if len(runs) == 1 else jnp.concatenate(runs, axis=1)

    return take


def dp_gather(w, sizes=(4, 2, 4)):
    ny, nz, nx = sizes
    r, c = w.shape
    a = w.reshape(1, 1, 1, r, c)
    a = ring_gather(a, "zl", nz, 1)
    h = c // 2
    s1 = ring_gather(ring_gather(a[..., :h], "x", nx, 2), "y", ny, 0)
    s2 = ring_gather(ring_gather(a[..., h:], "y", ny, 0), "x", nx, 2)
    return jnp.concatenate([s1, s2], axis=-1).reshape(ny * nz * nx * r, c)


def dp_scatter_t(g, sizes=(4, 2, 4)):
    ny, nz, nx = sizes
    c, R = g.shape
    r = R // (ny * nz * nx)
    h = c // 2
    zx = nz * nx * r
    s1 = ring_scatter(g[:h], "y", ny, _cols([lambda j: j * zx], zx))
    s1 = ring_scatter(s1, "x", nx, _cols([lambda j, z=z: z * nx * r + j * r for z in range(nz)], r))
    s2 = ring_scatter(
        g[h:], "x", nx,
        _cols([lambda j, k=k: k * nx * r + j * r for k in range(ny * nz)], r),
    )
    s2 = ring_scatter(s2, "y", ny, _cols([lambda j: j * nz * r], nz * r))
    a = jnp.concatenate([s1, s2], axis=0)
    a = ring_scatter(a, "zl", nz, _cols([lambda j: j * r], r))
    return a.T


def tp_scatter(t):
    w = t.shape[1] // 4
    t = ring_scatter(t, "c", 2, _cols([lambda j, z=z: z * 2 * w + j * w for z in range(2)], w))
    return ring_scatter(t, "zh", 2, _cols([lambda j: j * w], w))


def body(tokens, grad_out, w_query, w_key, value_matrix):
    length = tokens.shape[0]
    query_cols = w_query.shape[1]
    kv_cols = w_key.shape[1]
    half = query_cols // 2
    gathered_a = dp_gather(jnp.concatenate([w_key, value_matrix, w_query[:, :half]], axis=1))
    gathered_b = dp_gather(w_query[:, half:])
    cosine, sine_table = position_tables(length, HEAD_SIZE)
    projected_a = jnp.dot(tokens, gathered_a, preferred_element_type=jnp.float32)
    key = rotate_forward(
        projected_a[:, :kv_cols].reshape(length, 1, HEAD_SIZE), cosine, sine_table
    ).astype(jnp.bfloat16)
    value = projected_a[:, kv_cols : 2 * kv_cols].reshape(length, 1, HEAD_SIZE).astype(jnp.bfloat16)
    dq_a, dk_a, dv_a = attention_part(
        projected_a[:, 2 * kv_cols :], key, value, grad_out[:, :half], cosine, sine_table
    )
    grad_query_a = dp_scatter_t(
        lax.dot_general(
            dq_a, tokens, (((0,), (0,)), ((), ())), preferred_element_type=jnp.float32
        ).astype(jnp.bfloat16)
    )
    projected_b = jnp.dot(tokens, gathered_b, preferred_element_type=jnp.float32)
    dq_b, dk_b, dv_b = attention_part(
        projected_b, key, value, grad_out[:, half:], cosine, sine_table
    )
    key_gradient = (
        rotate_back(dk_a + dk_b, cosine, sine_table).astype(jnp.bfloat16).reshape(length, kv_cols)
    )
    value_gradient = (dv_a + dv_b).astype(jnp.bfloat16).reshape(length, kv_cols)
    rest = jnp.concatenate([dq_b, key_gradient, value_gradient], axis=1)
    grads_rest = dp_scatter_t(
        lax.dot_general(
            rest, tokens, (((0,), (0,)), ((), ())), preferred_element_type=jnp.float32
        ).astype(jnp.bfloat16)
    )
    contract = (((1,), (1,)), ((), ()))
    partial_sum = lax.dot_general(
        jnp.concatenate([key_gradient, value_gradient, dq_a], axis=1),
        gathered_a, contract, preferred_element_type=jnp.float32,
    ) + lax.dot_general(dq_b, gathered_b, contract, preferred_element_type=jnp.float32)
    part = partial_sum.astype(jnp.bfloat16)
    rows = length // 2
    grad_tokens = jnp.concatenate(
        [
            lax.psum_scatter(part[:rows], TP_AXES, scatter_dimension=1, tiled=True),
            tp_scatter(part[rows:]),
        ],
        axis=0,
    )
    grad_query = jnp.concatenate([grad_query_a, grads_rest[:, : query_cols - half]], axis=1)
    grad_key = grads_rest[:, query_cols - half : query_cols - half + kv_cols]
    grad_value = grads_rest[:, query_cols - half + kv_cols :]
    return (grad_tokens, grad_query, grad_key, grad_value)


def solution(mesh):
    view = Mesh(mesh.devices.reshape(4, 2, 4, 2, 2), DP_AXES + TP_AXES)
    rows = P(DP_AXES, None)
    split = P(DP_AXES, TP_AXES)
    in_specs = (rows, split, split, split, split)
    out_specs = (split, split, split, split)
    return jax.shard_map(body, mesh=view, in_specs=in_specs, out_specs=out_specs, check_vma=False)
```

```python
import jax
import jax.numpy as jnp
from jax import lax
from jax.experimental import pallas as pl
from jax.experimental.pallas import tpu as pltpu
from jax.sharding import Mesh
from jax.sharding import PartitionSpec as P

MODEL_WIDTH = 4096
HEAD_SIZE = 128


rope_base = 500000.0


def position_tables(length, head_dim):
    half_dim = head_dim // 2
    positions = jnp.arange(length, dtype=jnp.float32)
    inverse = jnp.power(
        jnp.float32(rope_base), -2.0 * jnp.arange(half_dim, dtype=jnp.float32) / head_dim
    )
    angles = positions[:, None] * inverse[None, :]
    cosine = jnp.concatenate([jnp.cos(angles), jnp.cos(angles)], axis=-1)[:, None, :]
    sine_table = jnp.concatenate([jnp.sin(angles), jnp.sin(angles)], axis=-1)[:, None, :]
    return (cosine, sine_table)


def half_turn(values):
    lower, upper = jnp.split(values, 2, axis=-1)
    return jnp.concatenate([-upper, lower], axis=-1)


def rotate_forward(values, cosine, sine_table):
    return values * cosine + half_turn(values) * sine_table


def rotate_back(grads, cosine, sine_table):
    return grads * cosine - half_turn(grads * sine_table)


def _attn_kernel(q_ref, k_ref, v_ref, do_ref, dq_ref, dk_ref, dv_ref):
    h = pl.program_id(0)
    scale = 1.0 / jnp.sqrt(jnp.float32(HEAD_SIZE))
    q = q_ref[...]
    k = k_ref[...]
    v = v_ref[...]
    do = do_ref[...]
    nt = (((1,), (1,)), ((), ()))
    tn = (((0,), (0,)), ((), ()))
    s = lax.dot_general(q, k, nt, preferred_element_type=jnp.float32) * scale
    rows = lax.broadcasted_iota(jnp.int32, s.shape, 0)
    cols = lax.broadcasted_iota(jnp.int32, s.shape, 1)
    s = jnp.where(rows >= cols, s, -jnp.inf)
    m = jnp.max(s, axis=1, keepdims=True)
    e = jnp.exp(s - m)
    w = e / jnp.sum(e, axis=1, keepdims=True)
    dp = lax.dot_general(do, v, nt, preferred_element_type=jnp.float32)
    rd = jnp.sum(w * dp, axis=1, keepdims=True)
    ds = (w * (dp - rd) * scale).astype(jnp.bfloat16)
    dq_ref[...] = jnp.dot(ds, k, preferred_element_type=jnp.float32)
    dk = lax.dot_general(ds, q, tn, preferred_element_type=jnp.float32)
    dv = lax.dot_general(w.astype(jnp.bfloat16), do, tn, preferred_element_type=jnp.float32)

    @pl.when(h == 0)
    def _():
        dk_ref[...] = dk
        dv_ref[...] = dv

    @pl.when(h > 0)
    def _():
        dk_ref[...] += dk
        dv_ref[...] += dv


def attention_kernel(query, key, value, upstream):
    length, width = query.shape
    heads = width // HEAD_SIZE
    per_head = pl.BlockSpec((length, HEAD_SIZE), lambda h: (0, h))
    shared = pl.BlockSpec((length, HEAD_SIZE), lambda h: (0, 0))
    return pl.pallas_call(
        _attn_kernel,
        grid=(heads,),
        in_specs=[per_head, shared, shared, per_head],
        out_specs=[per_head, shared, shared],
        out_shape=[
            jax.ShapeDtypeStruct((length, width), jnp.float32),
            jax.ShapeDtypeStruct((length, HEAD_SIZE), jnp.float32),
            jax.ShapeDtypeStruct((length, HEAD_SIZE), jnp.float32),
        ],
        compiler_params=pltpu.CompilerParams(dimension_semantics=("arbitrary",)),
    )(query, key, value, upstream)


def attention_backward(unrotated_query, unrotated_key, projected_value, upstream_flat, kv_heads):
    length = unrotated_query.shape[0]
    heads = unrotated_query.shape[1] // HEAD_SIZE
    group_size = heads // kv_heads
    cosine, sine_table = position_tables(length, HEAD_SIZE)
    query = rotate_forward(
        unrotated_query.reshape(length, heads, HEAD_SIZE), cosine, sine_table
    ).astype(jnp.bfloat16).reshape(length, heads * HEAD_SIZE)
    key = rotate_forward(
        unrotated_key.reshape(length, kv_heads, HEAD_SIZE), cosine, sine_table
    ).astype(jnp.bfloat16).reshape(length, kv_heads * HEAD_SIZE)
    value = projected_value.astype(jnp.bfloat16)
    group_cols = group_size * HEAD_SIZE
    pieces = [
        attention_kernel(
            query[:, g * group_cols : (g + 1) * group_cols],
            key[:, g * HEAD_SIZE : (g + 1) * HEAD_SIZE],
            value[:, g * HEAD_SIZE : (g + 1) * HEAD_SIZE],
            upstream_flat[:, g * group_cols : (g + 1) * group_cols],
        )
        for g in range(kv_heads)
    ]
    dquery = jnp.concatenate([p[0] for p in pieces], axis=1).reshape(length, heads, HEAD_SIZE)
    dkey = jnp.concatenate([p[1] for p in pieces], axis=1).reshape(length, kv_heads, HEAD_SIZE)
    dvalue = jnp.concatenate([p[2] for p in pieces], axis=1)
    query_gradient = (
        rotate_back(dquery, cosine, sine_table)
        .astype(jnp.bfloat16)
        .reshape(length, heads * HEAD_SIZE)
    )
    key_gradient = (
        rotate_back(dkey, cosine, sine_table)
        .astype(jnp.bfloat16)
        .reshape(length, kv_heads * HEAD_SIZE)
    )
    value_gradient = dvalue.astype(jnp.bfloat16)
    return (query_gradient, key_gradient, value_gradient)


DP_AXES = ("y", "zl", "x")
TP_AXES = ("zh", "c")


def _shift(x, axis, n, step):
    return lax.ppermute(x, axis, [(k, (k + step) % n) for k in range(n)])


def _place(parts, idx, n, dim):
    shape = list(parts[0].shape)
    size = shape[dim]
    shape[dim] = size * n
    out = jnp.zeros(shape, parts[0].dtype)
    for o, p in enumerate(parts):
        start = [0] * len(shape)
        start[dim] = ((idx + o) % n) * size
        out = lax.dynamic_update_slice(out, p, start)
    return out


def ring_gather(x, axis, n, dim):
    idx = lax.axis_index(axis)
    if n == 1:
        return x
    if n == 2:
        return _place([x, _shift(x, axis, 2, 1)], idx, 2, dim)
    assert n == 4
    from_left = _shift(x, axis, 4, 1)
    from_right = _shift(x, axis, 4, -1)
    half = x.shape[-1] // 2
    far_a = _shift(from_right[..., :half], axis, 4, -1)
    far_b = _shift(from_left[..., half:], axis, 4, 1)
    far = jnp.concatenate([far_a, far_b], axis=-1)
    return _place([x, from_right, far, from_left], idx, 4, dim)


def _take(x, pos, dim, n):
    size = x.shape[dim] // n
    return lax.dynamic_slice_in_dim(x, pos * size, size, dim)


def _add(a, b):
    return (a.astype(jnp.float32) + b.astype(jnp.float32)).astype(a.dtype)


def _halves(x, hdim):
    half = x.shape[hdim] // 2
    return (lax.slice_in_dim(x, 0, half, axis=hdim), lax.slice_in_dim(x, half, 2 * half, axis=hdim))


def ring_scatter(x, axis, n, take, hdim=0):
    idx = lax.axis_index(axis)
    if n == 2:
        return _add(take(x, idx), _shift(take(x, (idx + 1) % 2), axis, 2, 1))
    assert n == 4
    far_a, far_b = _halves(take(x, (idx + 2) % 4), hdim)
    right_a, right_b = _halves(take(x, (idx + 1) % 4), hdim)
    left_a, left_b = _halves(take(x, (idx + 3) % 4), hdim)
    got_a = _shift(far_a, axis, 4, 1)
    got_b = _shift(far_b, axis, 4, -1)
    to_right = jnp.concatenate([_add(right_a, got_a), right_b], axis=hdim)
    to_left = jnp.concatenate([left_a, _add(left_b, got_b)], axis=hdim)
    mine = take(x, idx)
    s = _add(mine, _shift(to_right, axis, 4, 1))
    return _add(s, _shift(to_left, axis, 4, -1))


def _cols(starts, width):
    def take(x, j):
        runs = [lax.dynamic_slice_in_dim(x, s(j), width, axis=1) for s in starts]
        return runs[0] if len(runs) == 1 else jnp.concatenate(runs, axis=1)

    return take


def dp_gather(w, sizes=(4, 2, 4)):
    ny, nz, nx = sizes
    r, c = w.shape
    a = w.reshape(1, 1, 1, r, c)
    a = ring_gather(a, "zl", nz, 1)
    h = c // 2
    s1 = ring_gather(ring_gather(a[..., :h], "x", nx, 2), "y", ny, 0)
    s2 = ring_gather(ring_gather(a[..., h:], "y", ny, 0), "x", nx, 2)
    return jnp.concatenate([s1, s2], axis=-1).reshape(ny * nz * nx * r, c)


def dp_scatter_t(g, sizes=(4, 2, 4)):
    ny, nz, nx = sizes
    c, R = g.shape
    r = R // (ny * nz * nx)
    h = c // 2
    zx = nz * nx * r
    s1 = ring_scatter(g[:h], "y", ny, _cols([lambda j: j * zx], zx))
    s1 = ring_scatter(s1, "x", nx, _cols([lambda j, z=z: z * nx * r + j * r for z in range(nz)], r))
    s2 = ring_scatter(
        g[h:], "x", nx,
        _cols([lambda j, k=k: k * nx * r + j * r for k in range(ny * nz)], r),
    )
    s2 = ring_scatter(s2, "y", ny, _cols([lambda j: j * nz * r], nz * r))
    a = jnp.concatenate([s1, s2], axis=0)
    a = ring_scatter(a, "zl", nz, _cols([lambda j: j * r], r))
    return a.T


def body(tokens, grad_out, w_query, w_key, value_matrix):
    query_cols = w_query.shape[1]
    key_value_columns = w_key.shape[1]
    kv_dev = key_value_columns // HEAD_SIZE
    weights_all = dp_gather(jnp.concatenate([w_query, w_key, value_matrix], axis=1))
    projected = jnp.dot(tokens, weights_all, preferred_element_type=jnp.float32)
    unrotated_query = projected[:, :query_cols]
    unrotated_key = projected[:, query_cols : query_cols + key_value_columns]
    projected_value = projected[:, query_cols + key_value_columns :]
    query_gradient, key_gradient, value_gradient = attention_backward(
        unrotated_query, unrotated_key, projected_value, grad_out, kv_dev
    )
    combined = jnp.concatenate([query_gradient, key_gradient, value_gradient], axis=1)
    partial_sum = lax.dot_general(
        combined, weights_all, (((1,), (1,)), ((), ())), preferred_element_type=jnp.float32
    )
    grad_tokens = lax.psum_scatter(
        partial_sum.astype(jnp.bfloat16), TP_AXES, scatter_dimension=1, tiled=True
    )
    grads_all = dp_scatter_t(
        lax.dot_general(
            combined, tokens, (((0,), (0,)), ((), ())), preferred_element_type=jnp.float32
        ).astype(jnp.bfloat16)
    )
    grad_query = grads_all[:, :query_cols]
    grad_key = grads_all[:, query_cols : query_cols + key_value_columns]
    grad_value = grads_all[:, query_cols + key_value_columns :]
    return (grad_tokens, grad_query, grad_key, grad_value)


def solution(mesh):
    view = Mesh(mesh.devices.reshape(4, 2, 4, 2, 2), DP_AXES + TP_AXES)
    rows = P(DP_AXES, None)
    split = P(DP_AXES, TP_AXES)
    in_specs = (rows, split, split, split, split)
    out_specs = (split, split, split, split)
    return jax.shard_map(body, mesh=view, in_specs=in_specs, out_specs=out_specs, check_vma=False)
```

```python
import jax
import jax.numpy as jnp
from jax import lax
from jax.experimental import pallas as pl
from jax.experimental.pallas import tpu as pltpu
from jax.sharding import Mesh
from jax.sharding import PartitionSpec as P

MODEL_WIDTH = 4096
HEAD_SIZE = 128


rope_base = 500000.0


def position_tables(length, head_dim):
    half_dim = head_dim // 2
    positions = jnp.arange(length, dtype=jnp.float32)
    inverse = jnp.power(
        jnp.float32(rope_base), -2.0 * jnp.arange(half_dim, dtype=jnp.float32) / head_dim
    )
    angles = positions[:, None] * inverse[None, :]
    cosine = jnp.concatenate([jnp.cos(angles), jnp.cos(angles)], axis=-1)[:, None, :]
    sine_table = jnp.concatenate([jnp.sin(angles), jnp.sin(angles)], axis=-1)[:, None, :]
    return (cosine, sine_table)


def half_turn(values):
    lower, upper = jnp.split(values, 2, axis=-1)
    return jnp.concatenate([-upper, lower], axis=-1)


def rotate_forward(values, cosine, sine_table):
    return values * cosine + half_turn(values) * sine_table


def rotate_back(grads, cosine, sine_table):
    return grads * cosine - half_turn(grads * sine_table)


def _attn_kernel(q_ref, k_ref, v_ref, do_ref, dq_ref, dk_ref, dv_ref):
    h = pl.program_id(0)
    scale = 1.0 / jnp.sqrt(jnp.float32(HEAD_SIZE))
    q = q_ref[...]
    k = k_ref[...]
    v = v_ref[...]
    do = do_ref[...]
    nt = (((1,), (1,)), ((), ()))
    tn = (((0,), (0,)), ((), ()))
    s = lax.dot_general(q, k, nt, preferred_element_type=jnp.float32) * scale
    rows = lax.broadcasted_iota(jnp.int32, s.shape, 0)
    cols = lax.broadcasted_iota(jnp.int32, s.shape, 1)
    s = jnp.where(rows >= cols, s, -jnp.inf)
    m = jnp.max(s, axis=1, keepdims=True)
    e = jnp.exp(s - m)
    w = e / jnp.sum(e, axis=1, keepdims=True)
    dp = lax.dot_general(do, v, nt, preferred_element_type=jnp.float32)
    rd = jnp.sum(w * dp, axis=1, keepdims=True)
    ds = (w * (dp - rd) * scale).astype(jnp.bfloat16)
    dq_ref[...] = jnp.dot(ds, k, preferred_element_type=jnp.float32)
    dk = lax.dot_general(ds, q, tn, preferred_element_type=jnp.float32)
    dv = lax.dot_general(w.astype(jnp.bfloat16), do, tn, preferred_element_type=jnp.float32)

    @pl.when(h == 0)
    def _():
        dk_ref[...] = dk
        dv_ref[...] = dv

    @pl.when(h > 0)
    def _():
        dk_ref[...] += dk
        dv_ref[...] += dv


def attention_kernel(query, key, value, upstream):
    length, width = query.shape
    heads = width // HEAD_SIZE
    per_head = pl.BlockSpec((length, HEAD_SIZE), lambda h: (0, h))
    shared = pl.BlockSpec((length, HEAD_SIZE), lambda h: (0, 0))
    return pl.pallas_call(
        _attn_kernel,
        grid=(heads,),
        in_specs=[per_head, shared, shared, per_head],
        out_specs=[per_head, shared, shared],
        out_shape=[
            jax.ShapeDtypeStruct((length, width), jnp.float32),
            jax.ShapeDtypeStruct((length, HEAD_SIZE), jnp.float32),
            jax.ShapeDtypeStruct((length, HEAD_SIZE), jnp.float32),
        ],
        compiler_params=pltpu.CompilerParams(dimension_semantics=("arbitrary",)),
    )(query, key, value, upstream)


def attention_backward(unrotated_query, unrotated_key, projected_value, upstream_flat, kv_heads):
    length = unrotated_query.shape[0]
    heads = unrotated_query.shape[1] // HEAD_SIZE
    group_size = heads // kv_heads
    cosine, sine_table = position_tables(length, HEAD_SIZE)
    query = rotate_forward(
        unrotated_query.reshape(length, heads, HEAD_SIZE), cosine, sine_table
    ).astype(jnp.bfloat16).reshape(length, heads * HEAD_SIZE)
    key = rotate_forward(
        unrotated_key.reshape(length, kv_heads, HEAD_SIZE), cosine, sine_table
    ).astype(jnp.bfloat16).reshape(length, kv_heads * HEAD_SIZE)
    value = projected_value.astype(jnp.bfloat16)
    group_cols = group_size * HEAD_SIZE
    pieces = [
        attention_kernel(
            query[:, g * group_cols : (g + 1) * group_cols],
            key[:, g * HEAD_SIZE : (g + 1) * HEAD_SIZE],
            value[:, g * HEAD_SIZE : (g + 1) * HEAD_SIZE],
            upstream_flat[:, g * group_cols : (g + 1) * group_cols],
        )
        for g in range(kv_heads)
    ]
    dquery = jnp.concatenate([p[0] for p in pieces], axis=1).reshape(length, heads, HEAD_SIZE)
    dkey = jnp.concatenate([p[1] for p in pieces], axis=1).reshape(length, kv_heads, HEAD_SIZE)
    dvalue = jnp.concatenate([p[2] for p in pieces], axis=1)
    query_gradient = (
        rotate_back(dquery, cosine, sine_table)
        .astype(jnp.bfloat16)
        .reshape(length, heads * HEAD_SIZE)
    )
    key_gradient = (
        rotate_back(dkey, cosine, sine_table)
        .astype(jnp.bfloat16)
        .reshape(length, kv_heads * HEAD_SIZE)
    )
    value_gradient = dvalue.astype(jnp.bfloat16)
    return (query_gradient, key_gradient, value_gradient)


DP_AXES = ("y", "zl", "x")
TP_AXES = ("zh", "c")


def _shift(x, axis, n, step):
    return lax.ppermute(x, axis, [(k, (k + step) % n) for k in range(n)])


def _place(parts, idx, n, dim):
    shape = list(parts[0].shape)
    size = shape[dim]
    shape[dim] = size * n
    out = jnp.zeros(shape, parts[0].dtype)
    for o, p in enumerate(parts):
        start = [0] * len(shape)
        start[dim] = ((idx + o) % n) * size
        out = lax.dynamic_update_slice(out, p, start)
    return out


def ring_gather(x, axis, n, dim):
    idx = lax.axis_index(axis)
    if n == 1:
        return x
    if n == 2:
        return _place([x, _shift(x, axis, 2, 1)], idx, 2, dim)
    assert n == 4
    from_left = _shift(x, axis, 4, 1)
    from_right = _shift(x, axis, 4, -1)
    half = x.shape[-1] // 2
    far_a = _shift(from_right[..., :half], axis, 4, -1)
    far_b = _shift(from_left[..., half:], axis, 4, 1)
    far = jnp.concatenate([far_a, far_b], axis=-1)
    return _place([x, from_right, far, from_left], idx, 4, dim)


def _take(x, pos, dim, n):
    size = x.shape[dim] // n
    return lax.dynamic_slice_in_dim(x, pos * size, size, dim)


def _add(a, b):
    return (a.astype(jnp.float32) + b.astype(jnp.float32)).astype(a.dtype)


def _halves(x, hdim):
    half = x.shape[hdim] // 2
    return (lax.slice_in_dim(x, 0, half, axis=hdim), lax.slice_in_dim(x, half, 2 * half, axis=hdim))


def ring_scatter(x, axis, n, take, hdim=0):
    idx = lax.axis_index(axis)
    if n == 2:
        return _add(take(x, idx), _shift(take(x, (idx + 1) % 2), axis, 2, 1))
    assert n == 4
    far_a, far_b = _halves(take(x, (idx + 2) % 4), hdim)
    right_a, right_b = _halves(take(x, (idx + 1) % 4), hdim)
    left_a, left_b = _halves(take(x, (idx + 3) % 4), hdim)
    got_a = _shift(far_a, axis, 4, 1)
    got_b = _shift(far_b, axis, 4, -1)
    to_right = jnp.concatenate([_add(right_a, got_a), right_b], axis=hdim)
    to_left = jnp.concatenate([left_a, _add(left_b, got_b)], axis=hdim)
    mine = take(x, idx)
    s = _add(mine, _shift(to_right, axis, 4, 1))
    return _add(s, _shift(to_left, axis, 4, -1))


def _cols(starts, width):
    def take(x, j):
        runs = [lax.dynamic_slice_in_dim(x, s(j), width, axis=1) for s in starts]
        return runs[0] if len(runs) == 1 else jnp.concatenate(runs, axis=1)

    return take


def dp_gather(w, sizes=(4, 2, 4)):
    ny, nz, nx = sizes
    r, c = w.shape
    a = w.reshape(1, 1, 1, r, c)
    a = ring_gather(a, "zl", nz, 1)
    h = c // 2
    s1 = ring_gather(ring_gather(a[..., :h], "x", nx, 2), "y", ny, 0)
    s2 = ring_gather(ring_gather(a[..., h:], "y", ny, 0), "x", nx, 2)
    return jnp.concatenate([s1, s2], axis=-1).reshape(ny * nz * nx * r, c)


def dp_scatter_t(g, sizes=(4, 2, 4)):
    ny, nz, nx = sizes
    c, R = g.shape
    r = R // (ny * nz * nx)
    h = c // 2
    zx = nz * nx * r
    s1 = ring_scatter(g[:h], "y", ny, _cols([lambda j: j * zx], zx))
    s1 = ring_scatter(s1, "x", nx, _cols([lambda j, z=z: z * nx * r + j * r for z in range(nz)], r))
    s2 = ring_scatter(
        g[h:], "x", nx,
        _cols([lambda j, k=k: k * nx * r + j * r for k in range(ny * nz)], r),
    )
    s2 = ring_scatter(s2, "y", ny, _cols([lambda j: j * nz * r], nz * r))
    a = jnp.concatenate([s1, s2], axis=0)
    a = ring_scatter(a, "zl", nz, _cols([lambda j: j * r], r))
    return a.T


def body(tokens, grad_out, w_query, w_key, value_matrix):
    query_cols = w_query.shape[1]
    key_value_columns = w_key.shape[1]
    kv_dev = key_value_columns // HEAD_SIZE
    weights_all = dp_gather(jnp.concatenate([w_query, w_key, value_matrix], axis=1))
    projected = jnp.dot(tokens, weights_all, preferred_element_type=jnp.float32)
    unrotated_query = projected[:, :query_cols]
    unrotated_key = projected[:, query_cols : query_cols + key_value_columns]
    projected_value = projected[:, query_cols + key_value_columns :]
    query_gradient, key_gradient, value_gradient = attention_backward(
        unrotated_query, unrotated_key, projected_value, grad_out, kv_dev
    )
    combined = jnp.concatenate([query_gradient, key_gradient, value_gradient], axis=1)
    n_tp = 4
    tp_index = lax.axis_index("zh") * 2 + lax.axis_index("c")
    share = weights_all.shape[0] // n_tp

    def shifted(x, s):
        return lax.ppermute(x, TP_AXES, [(k, (k + s) % n_tp) for k in range(n_tp)])

    total = None
    for s in range(n_tp):
        rows_for = lax.dynamic_slice_in_dim(weights_all, ((tp_index + s) % n_tp) * share, share, 0)
        w_rows = rows_for if s == 0 else shifted(rows_for, s)
        grads_from = combined if s == 0 else shifted(combined, s)
        part = lax.dot_general(
            grads_from, w_rows, (((1,), (1,)), ((), ())), preferred_element_type=jnp.float32
        ).astype(jnp.bfloat16).astype(jnp.float32)
        total = part if total is None else total + part
    grad_tokens = total.astype(jnp.bfloat16)
    grads_all = dp_scatter_t(
        lax.dot_general(
            combined, tokens, (((0,), (0,)), ((), ())), preferred_element_type=jnp.float32
        ).astype(jnp.bfloat16)
    )
    grad_query = grads_all[:, :query_cols]
    grad_key = grads_all[:, query_cols : query_cols + key_value_columns]
    grad_value = grads_all[:, query_cols + key_value_columns :]
    return (grad_tokens, grad_query, grad_key, grad_value)


def solution(mesh):
    view = Mesh(mesh.devices.reshape(4, 2, 4, 2, 2), DP_AXES + TP_AXES)
    rows = P(DP_AXES, None)
    split = P(DP_AXES, TP_AXES)
    in_specs = (rows, split, split, split, split)
    out_specs = (split, split, split, split)
    return jax.shard_map(body, mesh=view, in_specs=in_specs, out_specs=out_specs, check_vma=False)
```

```python
import jax
import jax.numpy as jnp
from jax import lax
from jax.experimental import pallas as pl
from jax.experimental.pallas import tpu as pltpu
from jax.sharding import Mesh
from jax.sharding import PartitionSpec as P

MODEL_WIDTH = 4096
HEAD_SIZE = 128


rope_base = 500000.0


def position_tables(length, head_dim):
    half_dim = head_dim // 2
    positions = jnp.arange(length, dtype=jnp.float32)
    inverse = jnp.power(
        jnp.float32(rope_base), -2.0 * jnp.arange(half_dim, dtype=jnp.float32) / head_dim
    )
    angles = positions[:, None] * inverse[None, :]
    cosine = jnp.concatenate([jnp.cos(angles), jnp.cos(angles)], axis=-1)[:, None, :]
    sine_table = jnp.concatenate([jnp.sin(angles), jnp.sin(angles)], axis=-1)[:, None, :]
    return (cosine, sine_table)


def half_turn(values):
    lower, upper = jnp.split(values, 2, axis=-1)
    return jnp.concatenate([-upper, lower], axis=-1)


def rotate_forward(values, cosine, sine_table):
    return values * cosine + half_turn(values) * sine_table


def rotate_back(grads, cosine, sine_table):
    return grads * cosine - half_turn(grads * sine_table)


def _attn_kernel(q_ref, k_ref, v_ref, do_ref, dq_ref, dk_ref, dv_ref):
    h = pl.program_id(0)
    scale = 1.0 / jnp.sqrt(jnp.float32(HEAD_SIZE))
    q = q_ref[...]
    k = k_ref[...]
    v = v_ref[...]
    do = do_ref[...]
    nt = (((1,), (1,)), ((), ()))
    tn = (((0,), (0,)), ((), ()))
    s = lax.dot_general(q, k, nt, preferred_element_type=jnp.float32) * scale
    rows = lax.broadcasted_iota(jnp.int32, s.shape, 0)
    cols = lax.broadcasted_iota(jnp.int32, s.shape, 1)
    s = jnp.where(rows >= cols, s, -jnp.inf)
    m = jnp.max(s, axis=1, keepdims=True)
    e = jnp.exp(s - m)
    w = e / jnp.sum(e, axis=1, keepdims=True)
    dp = lax.dot_general(do, v, nt, preferred_element_type=jnp.float32)
    rd = jnp.sum(w * dp, axis=1, keepdims=True)
    ds = (w * (dp - rd) * scale).astype(jnp.bfloat16)
    dq_ref[...] = jnp.dot(ds, k, preferred_element_type=jnp.float32)
    dk = lax.dot_general(ds, q, tn, preferred_element_type=jnp.float32)
    dv = lax.dot_general(w.astype(jnp.bfloat16), do, tn, preferred_element_type=jnp.float32)

    @pl.when(h == 0)
    def _():
        dk_ref[...] = dk
        dv_ref[...] = dv

    @pl.when(h > 0)
    def _():
        dk_ref[...] += dk
        dv_ref[...] += dv


def attention_kernel(query, key, value, upstream):
    length, width = query.shape
    heads = width // HEAD_SIZE
    per_head = pl.BlockSpec((length, HEAD_SIZE), lambda h: (0, h))
    shared = pl.BlockSpec((length, HEAD_SIZE), lambda h: (0, 0))
    return pl.pallas_call(
        _attn_kernel,
        grid=(heads,),
        in_specs=[per_head, shared, shared, per_head],
        out_specs=[per_head, shared, shared],
        out_shape=[
            jax.ShapeDtypeStruct((length, width), jnp.float32),
            jax.ShapeDtypeStruct((length, HEAD_SIZE), jnp.float32),
            jax.ShapeDtypeStruct((length, HEAD_SIZE), jnp.float32),
        ],
        compiler_params=pltpu.CompilerParams(dimension_semantics=("arbitrary",)),
    )(query, key, value, upstream)


def attention_backward(unrotated_query, unrotated_key, projected_value, upstream_flat, kv_heads):
    length = unrotated_query.shape[0]
    heads = unrotated_query.shape[1] // HEAD_SIZE
    group_size = heads // kv_heads
    cosine, sine_table = position_tables(length, HEAD_SIZE)
    query = rotate_forward(
        unrotated_query.reshape(length, heads, HEAD_SIZE), cosine, sine_table
    ).astype(jnp.bfloat16).reshape(length, heads * HEAD_SIZE)
    key = rotate_forward(
        unrotated_key.reshape(length, kv_heads, HEAD_SIZE), cosine, sine_table
    ).astype(jnp.bfloat16).reshape(length, kv_heads * HEAD_SIZE)
    value = projected_value.astype(jnp.bfloat16)
    group_cols = group_size * HEAD_SIZE
    pieces = [
        attention_kernel(
            query[:, g * group_cols : (g + 1) * group_cols],
            key[:, g * HEAD_SIZE : (g + 1) * HEAD_SIZE],
            value[:, g * HEAD_SIZE : (g + 1) * HEAD_SIZE],
            upstream_flat[:, g * group_cols : (g + 1) * group_cols],
        )
        for g in range(kv_heads)
    ]
    dquery = jnp.concatenate([p[0] for p in pieces], axis=1).reshape(length, heads, HEAD_SIZE)
    dkey = jnp.concatenate([p[1] for p in pieces], axis=1).reshape(length, kv_heads, HEAD_SIZE)
    dvalue = jnp.concatenate([p[2] for p in pieces], axis=1)
    query_gradient = (
        rotate_back(dquery, cosine, sine_table)
        .astype(jnp.bfloat16)
        .reshape(length, heads * HEAD_SIZE)
    )
    key_gradient = (
        rotate_back(dkey, cosine, sine_table)
        .astype(jnp.bfloat16)
        .reshape(length, kv_heads * HEAD_SIZE)
    )
    value_gradient = dvalue.astype(jnp.bfloat16)
    return (query_gradient, key_gradient, value_gradient)


DP_AXES = ("y", "zl", "x")
TP_AXES = ("zh", "c")


def _shift(x, axis, n, step):
    return lax.ppermute(x, axis, [(k, (k + step) % n) for k in range(n)])


def _place(parts, idx, n, dim):
    shape = list(parts[0].shape)
    size = shape[dim]
    shape[dim] = size * n
    out = jnp.zeros(shape, parts[0].dtype)
    for o, p in enumerate(parts):
        start = [0] * len(shape)
        start[dim] = ((idx + o) % n) * size
        out = lax.dynamic_update_slice(out, p, start)
    return out


def ring_gather(x, axis, n, dim):
    idx = lax.axis_index(axis)
    if n == 1:
        return x
    if n == 2:
        return _place([x, _shift(x, axis, 2, 1)], idx, 2, dim)
    assert n == 4
    from_left = _shift(x, axis, 4, 1)
    from_right = _shift(x, axis, 4, -1)
    half = x.shape[-1] // 2
    far_a = _shift(from_right[..., :half], axis, 4, -1)
    far_b = _shift(from_left[..., half:], axis, 4, 1)
    far = jnp.concatenate([far_a, far_b], axis=-1)
    return _place([x, from_right, far, from_left], idx, 4, dim)


def _take(x, pos, dim, n):
    size = x.shape[dim] // n
    return lax.dynamic_slice_in_dim(x, pos * size, size, dim)


def _add(a, b):
    return (a.astype(jnp.float32) + b.astype(jnp.float32)).astype(a.dtype)


def _halves(x, hdim):
    half = x.shape[hdim] // 2
    return (lax.slice_in_dim(x, 0, half, axis=hdim), lax.slice_in_dim(x, half, 2 * half, axis=hdim))


def ring_scatter(x, axis, n, take, hdim=0):
    idx = lax.axis_index(axis)
    if n == 2:
        return _add(take(x, idx), _shift(take(x, (idx + 1) % 2), axis, 2, 1))
    assert n == 4
    far_a, far_b = _halves(take(x, (idx + 2) % 4), hdim)
    right_a, right_b = _halves(take(x, (idx + 1) % 4), hdim)
    left_a, left_b = _halves(take(x, (idx + 3) % 4), hdim)
    got_a = _shift(far_a, axis, 4, 1)
    got_b = _shift(far_b, axis, 4, -1)
    to_right = jnp.concatenate([_add(right_a, got_a), right_b], axis=hdim)
    to_left = jnp.concatenate([left_a, _add(left_b, got_b)], axis=hdim)
    mine = take(x, idx)
    s = _add(mine, _shift(to_right, axis, 4, 1))
    return _add(s, _shift(to_left, axis, 4, -1))


def _cols(starts, width):
    def take(x, j):
        runs = [lax.dynamic_slice_in_dim(x, s(j), width, axis=1) for s in starts]
        return runs[0] if len(runs) == 1 else jnp.concatenate(runs, axis=1)

    return take


def dp_gather(w, sizes=(4, 2, 4)):
    ny, nz, nx = sizes
    r, c = w.shape
    a = w.reshape(1, 1, 1, r, c)
    a = ring_gather(a, "zl", nz, 1)
    h = c // 2
    s1 = ring_gather(ring_gather(a[..., :h], "x", nx, 2), "y", ny, 0)
    s2 = ring_gather(ring_gather(a[..., h:], "y", ny, 0), "x", nx, 2)
    return jnp.concatenate([s1, s2], axis=-1).reshape(ny * nz * nx * r, c)


def dp_scatter_t(g, sizes=(4, 2, 4)):
    ny, nz, nx = sizes
    c, R = g.shape
    r = R // (ny * nz * nx)
    h = c // 2
    zx = nz * nx * r
    s1 = ring_scatter(g[:h], "y", ny, _cols([lambda j: j * zx], zx))
    s1 = ring_scatter(s1, "x", nx, _cols([lambda j, z=z: z * nx * r + j * r for z in range(nz)], r))
    s2 = ring_scatter(
        g[h:], "x", nx,
        _cols([lambda j, k=k: k * nx * r + j * r for k in range(ny * nz)], r),
    )
    s2 = ring_scatter(s2, "y", ny, _cols([lambda j: j * nz * r], nz * r))
    a = jnp.concatenate([s1, s2], axis=0)
    a = ring_scatter(a, "zl", nz, _cols([lambda j: j * r], r))
    return a.T


def tp_scatter(t):
    w = t.shape[1] // 4
    t = ring_scatter(t, "c", 2, _cols([lambda j, z=z: z * 2 * w + j * w for z in range(2)], w))
    return ring_scatter(t, "zh", 2, _cols([lambda j: j * w], w))


def body(tokens, grad_out, w_query, w_key, value_matrix):
    query_cols = w_query.shape[1]
    key_value_columns = w_key.shape[1]
    kv_dev = key_value_columns // HEAD_SIZE
    weights_all = dp_gather(jnp.concatenate([w_query, w_key, value_matrix], axis=1))
    projected = jnp.dot(tokens, weights_all, preferred_element_type=jnp.float32)
    unrotated_query = projected[:, :query_cols]
    unrotated_key = projected[:, query_cols : query_cols + key_value_columns]
    projected_value = projected[:, query_cols + key_value_columns :]
    query_gradient, key_gradient, value_gradient = attention_backward(
        unrotated_query, unrotated_key, projected_value, grad_out, kv_dev
    )
    combined = jnp.concatenate([query_gradient, key_gradient, value_gradient], axis=1)
    partial_sum = lax.dot_general(
        combined, weights_all, (((1,), (1,)), ((), ())), preferred_element_type=jnp.float32
    )
    grad_tokens = tp_scatter(partial_sum.astype(jnp.bfloat16))
    grads_all = dp_scatter_t(
        lax.dot_general(
            combined, tokens, (((0,), (0,)), ((), ())), preferred_element_type=jnp.float32
        ).astype(jnp.bfloat16)
    )
    grad_query = grads_all[:, :query_cols]
    grad_key = grads_all[:, query_cols : query_cols + key_value_columns]
    grad_value = grads_all[:, query_cols + key_value_columns :]
    return (grad_tokens, grad_query, grad_key, grad_value)


def solution(mesh):
    view = Mesh(mesh.devices.reshape(4, 2, 4, 2, 2), DP_AXES + TP_AXES)
    rows = P(DP_AXES, None)
    split = P(DP_AXES, TP_AXES)
    in_specs = (rows, split, split, split, split)
    out_specs = (split, split, split, split)
    return jax.shard_map(body, mesh=view, in_specs=in_specs, out_specs=out_specs, check_vma=False)
```

```python
import jax
import jax.numpy as jnp
from jax import lax
from jax.experimental import pallas as pl
from jax.experimental.pallas import tpu as pltpu
from jax.sharding import Mesh
from jax.sharding import PartitionSpec as P

MODEL_WIDTH = 4096
HEAD_SIZE = 128


rope_base = 500000.0


def position_tables(length, head_dim):
    half_dim = head_dim // 2
    positions = jnp.arange(length, dtype=jnp.float32)
    inverse = jnp.power(
        jnp.float32(rope_base), -2.0 * jnp.arange(half_dim, dtype=jnp.float32) / head_dim
    )
    angles = positions[:, None] * inverse[None, :]
    cosine = jnp.concatenate([jnp.cos(angles), jnp.cos(angles)], axis=-1)[:, None, :]
    sine_table = jnp.concatenate([jnp.sin(angles), jnp.sin(angles)], axis=-1)[:, None, :]
    return (cosine, sine_table)


def half_turn(values):
    lower, upper = jnp.split(values, 2, axis=-1)
    return jnp.concatenate([-upper, lower], axis=-1)


def rotate_forward(values, cosine, sine_table):
    return values * cosine + half_turn(values) * sine_table


def rotate_back(grads, cosine, sine_table):
    return grads * cosine - half_turn(grads * sine_table)


def _turn(x):
    rolled = pltpu.roll(x, HEAD_SIZE // 2, 1)
    lane = lax.broadcasted_iota(jnp.int32, x.shape, 1)
    return jnp.where(lane < HEAD_SIZE // 2, -rolled, rolled)


def _fused_kernel(q_ref, k_ref, v_ref, do_ref, cos_ref, sin_ref, out_ref, dk_acc, dv_acc):
    h = pl.program_id(0)
    heads = pl.num_programs(0)
    scale = 1.0 / jnp.sqrt(jnp.float32(HEAD_SIZE))
    cosine = cos_ref[...]
    sine = sin_ref[...]
    q_raw = q_ref[...]
    k_raw = k_ref[...]
    q = (q_raw * cosine + _turn(q_raw) * sine).astype(jnp.bfloat16)
    k = (k_raw * cosine + _turn(k_raw) * sine).astype(jnp.bfloat16)
    v = v_ref[...].astype(jnp.bfloat16)
    do = do_ref[...]
    nt = (((1,), (1,)), ((), ()))
    tn = (((0,), (0,)), ((), ()))
    s = lax.dot_general(q, k, nt, preferred_element_type=jnp.float32) * scale
    rows = lax.broadcasted_iota(jnp.int32, s.shape, 0)
    cols = lax.broadcasted_iota(jnp.int32, s.shape, 1)
    s = jnp.where(rows >= cols, s, -jnp.inf)
    m = jnp.max(s, axis=1, keepdims=True)
    e = jnp.exp(s - m)
    w = e / jnp.sum(e, axis=1, keepdims=True)
    dp = lax.dot_general(do, v, nt, preferred_element_type=jnp.float32)
    rd = jnp.sum(w * dp, axis=1, keepdims=True)
    ds = (w * (dp - rd) * scale).astype(jnp.bfloat16)
    dq = jnp.dot(ds, k, preferred_element_type=jnp.float32)
    dq = dq * cosine - _turn(dq * sine)
    out_ref[:, pl.ds(pl.multiple_of(h * HEAD_SIZE, HEAD_SIZE), HEAD_SIZE)] = dq.astype(jnp.bfloat16)
    dk = lax.dot_general(ds, q, tn, preferred_element_type=jnp.float32)
    dv = lax.dot_general(w.astype(jnp.bfloat16), do, tn, preferred_element_type=jnp.float32)

    @pl.when(h == 0)
    def _():
        dk_acc[...] = dk
        dv_acc[...] = dv

    @pl.when(h > 0)
    def _():
        dk_acc[...] += dk
        dv_acc[...] += dv

    @pl.when(h == heads - 1)
    def _():
        g = dk_acc[...]
        g = g * cosine - _turn(g * sine)
        out_ref[:, pl.ds(heads * HEAD_SIZE, HEAD_SIZE)] = g.astype(jnp.bfloat16)
        out_ref[:, pl.ds((heads + 1) * HEAD_SIZE, HEAD_SIZE)] = dv_acc[...].astype(jnp.bfloat16)


def attention_fused(projected, upstream, cosine, sine):
    length, width = projected.shape
    heads = width // HEAD_SIZE - 2
    per_head = pl.BlockSpec((length, HEAD_SIZE), lambda h: (0, h))
    key_block = pl.BlockSpec((length, HEAD_SIZE), lambda h: (0, heads))
    value_block = pl.BlockSpec((length, HEAD_SIZE), lambda h: (0, heads + 1))
    table = pl.BlockSpec((length, HEAD_SIZE), lambda h: (0, 0))
    return pl.pallas_call(
        _fused_kernel,
        grid=(heads,),
        in_specs=[per_head, key_block, value_block, per_head, table, table],
        out_specs=pl.BlockSpec((length, width), lambda h: (0, 0)),
        out_shape=jax.ShapeDtypeStruct((length, width), jnp.bfloat16),
        scratch_shapes=[pltpu.VMEM((length, HEAD_SIZE), jnp.float32)] * 2,
        compiler_params=pltpu.CompilerParams(dimension_semantics=("arbitrary",)),
    )(projected, projected, projected, upstream, cosine, sine)


DP_AXES = ("y", "zl", "x")
TP_AXES = ("zh", "c")


def _shift(x, axis, n, step):
    return lax.ppermute(x, axis, [(k, (k + step) % n) for k in range(n)])


def _place(parts, idx, n, dim):
    shape = list(parts[0].shape)
    size = shape[dim]
    shape[dim] = size * n
    out = jnp.zeros(shape, parts[0].dtype)
    for o, p in enumerate(parts):
        start = [0] * len(shape)
        start[dim] = ((idx + o) % n) * size
        out = lax.dynamic_update_slice(out, p, start)
    return out


def ring_gather(x, axis, n, dim):
    idx = lax.axis_index(axis)
    if n == 1:
        return x
    if n == 2:
        return _place([x, _shift(x, axis, 2, 1)], idx, 2, dim)
    assert n == 4
    from_left = _shift(x, axis, 4, 1)
    from_right = _shift(x, axis, 4, -1)
    half = x.shape[-1] // 2
    far_a = _shift(from_right[..., :half], axis, 4, -1)
    far_b = _shift(from_left[..., half:], axis, 4, 1)
    far = jnp.concatenate([far_a, far_b], axis=-1)
    return _place([x, from_right, far, from_left], idx, 4, dim)


def _take(x, pos, dim, n):
    size = x.shape[dim] // n
    return lax.dynamic_slice_in_dim(x, pos * size, size, dim)


def _add(a, b):
    return (a.astype(jnp.float32) + b.astype(jnp.float32)).astype(a.dtype)


def _halves(x, hdim):
    half = x.shape[hdim] // 2
    return (lax.slice_in_dim(x, 0, half, axis=hdim), lax.slice_in_dim(x, half, 2 * half, axis=hdim))


def ring_scatter(x, axis, n, take, hdim=0):
    idx = lax.axis_index(axis)
    if n == 2:
        return _add(take(x, idx), _shift(take(x, (idx + 1) % 2), axis, 2, 1))
    assert n == 4
    far_a, far_b = _halves(take(x, (idx + 2) % 4), hdim)
    right_a, right_b = _halves(take(x, (idx + 1) % 4), hdim)
    left_a, left_b = _halves(take(x, (idx + 3) % 4), hdim)
    got_a = _shift(far_a, axis, 4, 1)
    got_b = _shift(far_b, axis, 4, -1)
    to_right = jnp.concatenate([_add(right_a, got_a), right_b], axis=hdim)
    to_left = jnp.concatenate([left_a, _add(left_b, got_b)], axis=hdim)
    mine = take(x, idx)
    s = _add(mine, _shift(to_right, axis, 4, 1))
    return _add(s, _shift(to_left, axis, 4, -1))


def _cols(starts, width):
    def take(x, j):
        runs = [lax.dynamic_slice_in_dim(x, s(j), width, axis=1) for s in starts]
        return runs[0] if len(runs) == 1 else jnp.concatenate(runs, axis=1)

    return take


def dp_gather(w, sizes=(4, 2, 4)):
    ny, nz, nx = sizes
    r, c = w.shape
    a = w.reshape(1, 1, 1, r, c)
    a = ring_gather(a, "zl", nz, 1)
    h = c // 2
    s1 = ring_gather(ring_gather(a[..., :h], "x", nx, 2), "y", ny, 0)
    s2 = ring_gather(ring_gather(a[..., h:], "y", ny, 0), "x", nx, 2)
    return jnp.concatenate([s1, s2], axis=-1).reshape(ny * nz * nx * r, c)


def dp_scatter_t(g, sizes=(4, 2, 4)):
    ny, nz, nx = sizes
    c, R = g.shape
    r = R // (ny * nz * nx)
    h = c // 2
    zx = nz * nx * r
    s1 = ring_scatter(g[:h], "y", ny, _cols([lambda j: j * zx], zx))
    s1 = ring_scatter(s1, "x", nx, _cols([lambda j, z=z: z * nx * r + j * r for z in range(nz)], r))
    s2 = ring_scatter(
        g[h:], "x", nx,
        _cols([lambda j, k=k: k * nx * r + j * r for k in range(ny * nz)], r),
    )
    s2 = ring_scatter(s2, "y", ny, _cols([lambda j: j * nz * r], nz * r))
    a = jnp.concatenate([s1, s2], axis=0)
    a = ring_scatter(a, "zl", nz, _cols([lambda j: j * r], r))
    return a.T


def body(tokens, grad_out, w_query, w_key, value_matrix):
    query_cols = w_query.shape[1]
    key_value_columns = w_key.shape[1]
    kv_dev = key_value_columns // HEAD_SIZE
    weights_all = dp_gather(jnp.concatenate([w_query, w_key, value_matrix], axis=1))
    projected = jnp.dot(tokens, weights_all, preferred_element_type=jnp.float32)
    cosine, sine_table = position_tables(tokens.shape[0], HEAD_SIZE)
    combined = attention_fused(projected, grad_out, cosine[:, 0, :], sine_table[:, 0, :])
    partial_sum = lax.dot_general(
        combined, weights_all, (((1,), (1,)), ((), ())), preferred_element_type=jnp.float32
    )
    grad_tokens = lax.psum_scatter(
        partial_sum.astype(jnp.bfloat16), TP_AXES, scatter_dimension=1, tiled=True
    )
    grads_all = dp_scatter_t(
        lax.dot_general(
            combined, tokens, (((0,), (0,)), ((), ())), preferred_element_type=jnp.float32
        ).astype(jnp.bfloat16)
    )
    grad_query = grads_all[:, :query_cols]
    grad_key = grads_all[:, query_cols : query_cols + key_value_columns]
    grad_value = grads_all[:, query_cols + key_value_columns :]
    return (grad_tokens, grad_query, grad_key, grad_value)


def solution(mesh):
    view = Mesh(mesh.devices.reshape(4, 2, 4, 2, 2), DP_AXES + TP_AXES)
    rows = P(DP_AXES, None)
    split = P(DP_AXES, TP_AXES)
    in_specs = (rows, split, split, split, split)
    out_specs = (split, split, split, split)
    return jax.shard_map(body, mesh=view, in_specs=in_specs, out_specs=out_specs, check_vma=False)
```

```python
import jax
import jax.numpy as jnp
from jax import lax
from jax.experimental import pallas as pl
from jax.experimental.pallas import tpu as pltpu
from jax.sharding import Mesh
from jax.sharding import PartitionSpec as P

MODEL_WIDTH = 4096
HEAD_SIZE = 128


rope_base = 500000.0


def position_tables(length, head_dim):
    half_dim = head_dim // 2
    positions = jnp.arange(length, dtype=jnp.float32)
    inverse = jnp.power(
        jnp.float32(rope_base), -2.0 * jnp.arange(half_dim, dtype=jnp.float32) / head_dim
    )
    angles = positions[:, None] * inverse[None, :]
    cosine = jnp.concatenate([jnp.cos(angles), jnp.cos(angles)], axis=-1)[:, None, :]
    sine_table = jnp.concatenate([jnp.sin(angles), jnp.sin(angles)], axis=-1)[:, None, :]
    return (cosine, sine_table)


def half_turn(values):
    lower, upper = jnp.split(values, 2, axis=-1)
    return jnp.concatenate([-upper, lower], axis=-1)


def rotate_forward(values, cosine, sine_table):
    return values * cosine + half_turn(values) * sine_table


def rotate_back(grads, cosine, sine_table):
    return grads * cosine - half_turn(grads * sine_table)


def _turn(x):
    rolled = pltpu.roll(x, HEAD_SIZE // 2, 1)
    lane = lax.broadcasted_iota(jnp.int32, x.shape, 1)
    return jnp.where(lane < HEAD_SIZE // 2, -rolled, rolled)


def _fused_kernel(proj_ref, do_ref, cos_ref, sin_ref, out_ref, dk_acc, dv_acc):
    h = pl.program_id(0)
    heads = pl.num_programs(0)
    scale = 1.0 / jnp.sqrt(jnp.float32(HEAD_SIZE))
    cosine = cos_ref[...]
    sine = sin_ref[...]
    q_raw = proj_ref[:, pl.ds(pl.multiple_of(h * HEAD_SIZE, HEAD_SIZE), HEAD_SIZE)]
    k_raw = proj_ref[:, pl.ds(heads * HEAD_SIZE, HEAD_SIZE)]
    q = (q_raw * cosine + _turn(q_raw) * sine).astype(jnp.bfloat16)
    k = (k_raw * cosine + _turn(k_raw) * sine).astype(jnp.bfloat16)
    v = proj_ref[:, pl.ds((heads + 1) * HEAD_SIZE, HEAD_SIZE)].astype(jnp.bfloat16)
    do = do_ref[...]
    nt = (((1,), (1,)), ((), ()))
    tn = (((0,), (0,)), ((), ()))
    s = lax.dot_general(q, k, nt, preferred_element_type=jnp.float32) * scale
    rows = lax.broadcasted_iota(jnp.int32, s.shape, 0)
    cols = lax.broadcasted_iota(jnp.int32, s.shape, 1)
    s = jnp.where(rows >= cols, s, -jnp.inf)
    m = jnp.max(s, axis=1, keepdims=True)
    e = jnp.exp(s - m)
    w = e / jnp.sum(e, axis=1, keepdims=True)
    dp = lax.dot_general(do, v, nt, preferred_element_type=jnp.float32)
    rd = jnp.sum(w * dp, axis=1, keepdims=True)
    ds = (w * (dp - rd) * scale).astype(jnp.bfloat16)
    dq = jnp.dot(ds, k, preferred_element_type=jnp.float32)
    dq = dq * cosine - _turn(dq * sine)
    out_ref[:, pl.ds(pl.multiple_of(h * HEAD_SIZE, HEAD_SIZE), HEAD_SIZE)] = dq.astype(jnp.bfloat16)
    dk = lax.dot_general(ds, q, tn, preferred_element_type=jnp.float32)
    dv = lax.dot_general(w.astype(jnp.bfloat16), do, tn, preferred_element_type=jnp.float32)

    @pl.when(h == 0)
    def _():
        dk_acc[...] = dk
        dv_acc[...] = dv

    @pl.when(h > 0)
    def _():
        dk_acc[...] += dk
        dv_acc[...] += dv

    @pl.when(h == heads - 1)
    def _():
        g = dk_acc[...]
        g = g * cosine - _turn(g * sine)
        out_ref[:, pl.ds(heads * HEAD_SIZE, HEAD_SIZE)] = g.astype(jnp.bfloat16)
        out_ref[:, pl.ds((heads + 1) * HEAD_SIZE, HEAD_SIZE)] = dv_acc[...].astype(jnp.bfloat16)


def attention_fused(projected, upstream, cosine, sine):
    length, width = projected.shape
    heads = width // HEAD_SIZE - 2
    per_head = pl.BlockSpec((length, HEAD_SIZE), lambda h: (0, h))
    whole = pl.BlockSpec((length, width), lambda h: (0, 0))
    table = pl.BlockSpec((length, HEAD_SIZE), lambda h: (0, 0))
    return pl.pallas_call(
        _fused_kernel,
        grid=(heads,),
        in_specs=[whole, per_head, table, table],
        out_specs=pl.BlockSpec((length, width), lambda h: (0, 0)),
        out_shape=jax.ShapeDtypeStruct((length, width), jnp.bfloat16),
        scratch_shapes=[pltpu.VMEM((length, HEAD_SIZE), jnp.float32)] * 2,
        compiler_params=pltpu.CompilerParams(dimension_semantics=("arbitrary",)),
    )(projected, upstream, cosine, sine)


DP_AXES = ("y", "zl", "x")
TP_AXES = ("zh", "c")


def _shift(x, axis, n, step):
    return lax.ppermute(x, axis, [(k, (k + step) % n) for k in range(n)])


def _place(parts, idx, n, dim):
    shape = list(parts[0].shape)
    size = shape[dim]
    shape[dim] = size * n
    out = jnp.zeros(shape, parts[0].dtype)
    for o, p in enumerate(parts):
        start = [0] * len(shape)
        start[dim] = ((idx + o) % n) * size
        out = lax.dynamic_update_slice(out, p, start)
    return out


def ring_gather(x, axis, n, dim):
    idx = lax.axis_index(axis)
    if n == 1:
        return x
    if n == 2:
        return _place([x, _shift(x, axis, 2, 1)], idx, 2, dim)
    assert n == 4
    from_left = _shift(x, axis, 4, 1)
    from_right = _shift(x, axis, 4, -1)
    half = x.shape[-1] // 2
    far_a = _shift(from_right[..., :half], axis, 4, -1)
    far_b = _shift(from_left[..., half:], axis, 4, 1)
    far = jnp.concatenate([far_a, far_b], axis=-1)
    return _place([x, from_right, far, from_left], idx, 4, dim)


def _take(x, pos, dim, n):
    size = x.shape[dim] // n
    return lax.dynamic_slice_in_dim(x, pos * size, size, dim)


def _add(a, b):
    return (a.astype(jnp.float32) + b.astype(jnp.float32)).astype(a.dtype)


def _halves(x, hdim):
    half = x.shape[hdim] // 2
    return (lax.slice_in_dim(x, 0, half, axis=hdim), lax.slice_in_dim(x, half, 2 * half, axis=hdim))


def ring_scatter(x, axis, n, take, hdim=0):
    idx = lax.axis_index(axis)
    if n == 2:
        return _add(take(x, idx), _shift(take(x, (idx + 1) % 2), axis, 2, 1))
    assert n == 4
    far_a, far_b = _halves(take(x, (idx + 2) % 4), hdim)
    right_a, right_b = _halves(take(x, (idx + 1) % 4), hdim)
    left_a, left_b = _halves(take(x, (idx + 3) % 4), hdim)
    got_a = _shift(far_a, axis, 4, 1)
    got_b = _shift(far_b, axis, 4, -1)
    to_right = jnp.concatenate([_add(right_a, got_a), right_b], axis=hdim)
    to_left = jnp.concatenate([left_a, _add(left_b, got_b)], axis=hdim)
    mine = take(x, idx)
    s = _add(mine, _shift(to_right, axis, 4, 1))
    return _add(s, _shift(to_left, axis, 4, -1))


def _cols(starts, width):
    def take(x, j):
        runs = [lax.dynamic_slice_in_dim(x, s(j), width, axis=1) for s in starts]
        return runs[0] if len(runs) == 1 else jnp.concatenate(runs, axis=1)

    return take


def dp_gather(w, sizes=(4, 2, 4)):
    ny, nz, nx = sizes
    r, c = w.shape
    a = w.reshape(1, 1, 1, r, c)
    a = ring_gather(a, "zl", nz, 1)
    h = c // 2
    s1 = ring_gather(ring_gather(a[..., :h], "x", nx, 2), "y", ny, 0)
    s2 = ring_gather(ring_gather(a[..., h:], "y", ny, 0), "x", nx, 2)
    return jnp.concatenate([s1, s2], axis=-1).reshape(ny * nz * nx * r, c)


def dp_scatter_t(g, sizes=(4, 2, 4)):
    ny, nz, nx = sizes
    c, R = g.shape
    r = R // (ny * nz * nx)
    h = c // 2
    zx = nz * nx * r
    s1 = ring_scatter(g[:h], "y", ny, _cols([lambda j: j * zx], zx))
    s1 = ring_scatter(s1, "x", nx, _cols([lambda j, z=z: z * nx * r + j * r for z in range(nz)], r))
    s2 = ring_scatter(
        g[h:], "x", nx,
        _cols([lambda j, k=k: k * nx * r + j * r for k in range(ny * nz)], r),
    )
    s2 = ring_scatter(s2, "y", ny, _cols([lambda j: j * nz * r], nz * r))
    a = jnp.concatenate([s1, s2], axis=0)
    a = ring_scatter(a, "zl", nz, _cols([lambda j: j * r], r))
    return a.T


def body(tokens, grad_out, w_query, w_key, value_matrix):
    query_cols = w_query.shape[1]
    key_value_columns = w_key.shape[1]
    kv_dev = key_value_columns // HEAD_SIZE
    weights_all = dp_gather(jnp.concatenate([w_query, w_key, value_matrix], axis=1))
    projected = jnp.dot(tokens, weights_all, preferred_element_type=jnp.float32)
    cosine, sine_table = position_tables(tokens.shape[0], HEAD_SIZE)
    combined = attention_fused(projected, grad_out, cosine[:, 0, :], sine_table[:, 0, :])
    partial_sum = lax.dot_general(
        combined, weights_all, (((1,), (1,)), ((), ())), preferred_element_type=jnp.float32
    )
    grad_tokens = lax.psum_scatter(
        partial_sum.astype(jnp.bfloat16), TP_AXES, scatter_dimension=1, tiled=True
    )
    grads_all = dp_scatter_t(
        lax.dot_general(
            combined, tokens, (((0,), (0,)), ((), ())), preferred_element_type=jnp.float32
        ).astype(jnp.bfloat16)
    )
    grad_query = grads_all[:, :query_cols]
    grad_key = grads_all[:, query_cols : query_cols + key_value_columns]
    grad_value = grads_all[:, query_cols + key_value_columns :]
    return (grad_tokens, grad_query, grad_key, grad_value)


def solution(mesh):
    view = Mesh(mesh.devices.reshape(4, 2, 4, 2, 2), DP_AXES + TP_AXES)
    rows = P(DP_AXES, None)
    split = P(DP_AXES, TP_AXES)
    in_specs = (rows, split, split, split, split)
    out_specs = (split, split, split, split)
    return jax.shard_map(body, mesh=view, in_specs=in_specs, out_specs=out_specs, check_vma=False)
```

```python
import jax
import jax.numpy as jnp
from jax import lax
from jax.experimental import pallas as pl
from jax.experimental.pallas import tpu as pltpu
from jax.sharding import Mesh
from jax.sharding import PartitionSpec as P

MODEL_WIDTH = 4096
HEAD_SIZE = 128


rope_base = 500000.0


def position_tables(length, head_dim):
    half_dim = head_dim // 2
    positions = jnp.arange(length, dtype=jnp.float32)
    inverse = jnp.power(
        jnp.float32(rope_base), -2.0 * jnp.arange(half_dim, dtype=jnp.float32) / head_dim
    )
    angles = positions[:, None] * inverse[None, :]
    cosine = jnp.concatenate([jnp.cos(angles), jnp.cos(angles)], axis=-1)[:, None, :]
    sine_table = jnp.concatenate([jnp.sin(angles), jnp.sin(angles)], axis=-1)[:, None, :]
    return (cosine, sine_table)


def half_turn(values):
    lower, upper = jnp.split(values, 2, axis=-1)
    return jnp.concatenate([-upper, lower], axis=-1)


def rotate_forward(values, cosine, sine_table):
    return values * cosine + half_turn(values) * sine_table


def rotate_back(grads, cosine, sine_table):
    return grads * cosine - half_turn(grads * sine_table)


def _turn(x):
    rolled = pltpu.roll(x, HEAD_SIZE // 2, 1)
    lane = lax.broadcasted_iota(jnp.int32, x.shape, 1)
    return jnp.where(lane < HEAD_SIZE // 2, -rolled, rolled)


def _fused_kernel(q_ref, k_ref, v_ref, do_ref, cos_ref, sin_ref, out_ref, dk_acc, dv_acc):
    h = pl.program_id(0)
    heads = pl.num_programs(0)
    scale = 1.0 / jnp.sqrt(jnp.float32(HEAD_SIZE))
    cosine = cos_ref[...]
    sine = sin_ref[...]
    q_raw = q_ref[...]
    k_raw = k_ref[...]
    q = (q_raw * cosine + _turn(q_raw) * sine).astype(jnp.bfloat16)
    k = (k_raw * cosine + _turn(k_raw) * sine).astype(jnp.bfloat16)
    v = v_ref[...].astype(jnp.bfloat16)
    do = do_ref[...]
    nt = (((1,), (1,)), ((), ()))
    tn = (((0,), (0,)), ((), ()))
    s = lax.dot_general(q, k, nt, preferred_element_type=jnp.float32) * scale
    rows = lax.broadcasted_iota(jnp.int32, s.shape, 0)
    cols = lax.broadcasted_iota(jnp.int32, s.shape, 1)
    s = jnp.where(rows >= cols, s, -jnp.inf)
    m = jnp.max(s, axis=1, keepdims=True)
    e = jnp.exp(s - m)
    w = e / jnp.sum(e, axis=1, keepdims=True)
    dp = lax.dot_general(do, v, nt, preferred_element_type=jnp.float32)
    rd = jnp.sum(w * dp, axis=1, keepdims=True)
    ds = (w * (dp - rd) * scale).astype(jnp.bfloat16)
    dq = jnp.dot(ds, k, preferred_element_type=jnp.float32)
    dq = dq * cosine - _turn(dq * sine)
    out_ref[:, pl.ds(pl.multiple_of(h * HEAD_SIZE, HEAD_SIZE), HEAD_SIZE)] = dq.astype(jnp.bfloat16)
    dk = lax.dot_general(ds, q, tn, preferred_element_type=jnp.float32)
    dv = lax.dot_general(w.astype(jnp.bfloat16), do, tn, preferred_element_type=jnp.float32)

    @pl.when(h == 0)
    def _():
        dk_acc[...] = dk
        dv_acc[...] = dv

    @pl.when(h > 0)
    def _():
        dk_acc[...] += dk
        dv_acc[...] += dv

    @pl.when(h == heads - 1)
    def _():
        g = dk_acc[...]
        g = g * cosine - _turn(g * sine)
        out_ref[:, pl.ds(heads * HEAD_SIZE, HEAD_SIZE)] = g.astype(jnp.bfloat16)
        out_ref[:, pl.ds((heads + 1) * HEAD_SIZE, HEAD_SIZE)] = dv_acc[...].astype(jnp.bfloat16)


def attention_fused(projected, upstream, cosine, sine):
    length, width = projected.shape
    heads = width // HEAD_SIZE - 2
    per_head = pl.BlockSpec((length, HEAD_SIZE), lambda h: (0, h))
    key_block = pl.BlockSpec((length, HEAD_SIZE), lambda h: (0, heads))
    value_block = pl.BlockSpec((length, HEAD_SIZE), lambda h: (0, heads + 1))
    table = pl.BlockSpec((length, HEAD_SIZE), lambda h: (0, 0))
    return pl.pallas_call(
        _fused_kernel,
        grid=(heads,),
        in_specs=[per_head, key_block, value_block, per_head, table, table],
        out_specs=pl.BlockSpec((length, width), lambda h: (0, 0)),
        out_shape=jax.ShapeDtypeStruct((length, width), jnp.bfloat16),
        scratch_shapes=[pltpu.VMEM((length, HEAD_SIZE), jnp.float32)] * 2,
        compiler_params=pltpu.CompilerParams(dimension_semantics=("arbitrary",)),
    )(projected, projected, projected, upstream, cosine, sine)


DP_AXES = ("y", "zl", "x")
TP_AXES = ("zh", "c")


def _shift(x, axis, n, step):
    return lax.ppermute(x, axis, [(k, (k + step) % n) for k in range(n)])


def _place(parts, idx, n, dim):
    shape = list(parts[0].shape)
    size = shape[dim]
    shape[dim] = size * n
    out = jnp.zeros(shape, parts[0].dtype)
    for o, p in enumerate(parts):
        start = [0] * len(shape)
        start[dim] = ((idx + o) % n) * size
        out = lax.dynamic_update_slice(out, p, start)
    return out


def ring_gather(x, axis, n, dim):
    idx = lax.axis_index(axis)
    if n == 1:
        return x
    if n == 2:
        return _place([x, _shift(x, axis, 2, 1)], idx, 2, dim)
    assert n == 4
    from_left = _shift(x, axis, 4, 1)
    from_right = _shift(x, axis, 4, -1)
    half = x.shape[-1] // 2
    far_a = _shift(from_right[..., :half], axis, 4, -1)
    far_b = _shift(from_left[..., half:], axis, 4, 1)
    far = jnp.concatenate([far_a, far_b], axis=-1)
    return _place([x, from_right, far, from_left], idx, 4, dim)


def _take(x, pos, dim, n):
    size = x.shape[dim] // n
    return lax.dynamic_slice_in_dim(x, pos * size, size, dim)


def _add(a, b):
    return (a.astype(jnp.float32) + b.astype(jnp.float32)).astype(a.dtype)


def _halves(x, hdim):
    half = x.shape[hdim] // 2
    return (lax.slice_in_dim(x, 0, half, axis=hdim), lax.slice_in_dim(x, half, 2 * half, axis=hdim))


def ring_scatter(x, axis, n, take, hdim=0):
    idx = lax.axis_index(axis)
    if n == 2:
        return _add(take(x, idx), _shift(take(x, (idx + 1) % 2), axis, 2, 1))
    assert n == 4
    far_a, far_b = _halves(take(x, (idx + 2) % 4), hdim)
    right_a, right_b = _halves(take(x, (idx + 1) % 4), hdim)
    left_a, left_b = _halves(take(x, (idx + 3) % 4), hdim)
    got_a = _shift(far_a, axis, 4, 1)
    got_b = _shift(far_b, axis, 4, -1)
    to_right = jnp.concatenate([_add(right_a, got_a), right_b], axis=hdim)
    to_left = jnp.concatenate([left_a, _add(left_b, got_b)], axis=hdim)
    mine = take(x, idx)
    s = _add(mine, _shift(to_right, axis, 4, 1))
    return _add(s, _shift(to_left, axis, 4, -1))


def _cols(starts, width):
    def take(x, j):
        runs = [lax.dynamic_slice_in_dim(x, s(j), width, axis=1) for s in starts]
        return runs[0] if len(runs) == 1 else jnp.concatenate(runs, axis=1)

    return take


def dp_gather(w, sizes=(4, 2, 4)):
    ny, nz, nx = sizes
    r, c = w.shape
    a = w.reshape(1, 1, 1, r, c)
    a = ring_gather(a, "zl", nz, 1)
    h = c // 2
    s1 = ring_gather(ring_gather(a[..., :h], "x", nx, 2), "y", ny, 0)
    s2 = ring_gather(ring_gather(a[..., h:], "y", ny, 0), "x", nx, 2)
    return jnp.concatenate([s1, s2], axis=-1).reshape(ny * nz * nx * r, c)


def dp_scatter_t(g, sizes=(4, 2, 4)):
    ny, nz, nx = sizes
    c, R = g.shape
    r = R // (ny * nz * nx)
    h = c // 2
    zx = nz * nx * r
    s1 = ring_scatter(g[:h], "y", ny, _cols([lambda j: j * zx], zx))
    s1 = ring_scatter(s1, "x", nx, _cols([lambda j, z=z: z * nx * r + j * r for z in range(nz)], r))
    s2 = ring_scatter(
        g[h:], "x", nx,
        _cols([lambda j, k=k: k * nx * r + j * r for k in range(ny * nz)], r),
    )
    s2 = ring_scatter(s2, "y", ny, _cols([lambda j: j * nz * r], nz * r))
    a = jnp.concatenate([s1, s2], axis=0)
    a = ring_scatter(a, "zl", nz, _cols([lambda j: j * r], r))
    return a.T


def tp_scatter(t):
    w = t.shape[1] // 4
    t = ring_scatter(t, "c", 2, _cols([lambda j, z=z: z * 2 * w + j * w for z in range(2)], w))
    return ring_scatter(t, "zh", 2, _cols([lambda j: j * w], w))


def body(tokens, grad_out, w_query, w_key, value_matrix):
    query_cols = w_query.shape[1]
    key_value_columns = w_key.shape[1]
    kv_dev = key_value_columns // HEAD_SIZE
    weights_all = dp_gather(jnp.concatenate([w_query, w_key, value_matrix], axis=1))
    projected = jnp.dot(tokens, weights_all, preferred_element_type=jnp.float32)
    cosine, sine_table = position_tables(tokens.shape[0], HEAD_SIZE)
    combined = attention_fused(projected, grad_out, cosine[:, 0, :], sine_table[:, 0, :])
    partial_sum = lax.dot_general(
        combined, weights_all, (((1,), (1,)), ((), ())), preferred_element_type=jnp.float32
    )
    part = partial_sum.astype(jnp.bfloat16)
    native_rows = part.shape[0] * 3 // 4
    grad_tokens = jnp.concatenate(
        [
            lax.psum_scatter(part[:native_rows], TP_AXES, scatter_dimension=1, tiled=True),
            tp_scatter(part[native_rows:]),
        ],
        axis=0,
    )
    grads_all = dp_scatter_t(
        lax.dot_general(
            combined, tokens, (((0,), (0,)), ((), ())), preferred_element_type=jnp.float32
        ).astype(jnp.bfloat16)
    )
    grad_query = grads_all[:, :query_cols]
    grad_key = grads_all[:, query_cols : query_cols + key_value_columns]
    grad_value = grads_all[:, query_cols + key_value_columns :]
    return (grad_tokens, grad_query, grad_key, grad_value)


def solution(mesh):
    view = Mesh(mesh.devices.reshape(4, 2, 4, 2, 2), DP_AXES + TP_AXES)
    rows = P(DP_AXES, None)
    split = P(DP_AXES, TP_AXES)
    in_specs = (rows, split, split, split, split)
    out_specs = (split, split, split, split)
    return jax.shard_map(body, mesh=view, in_specs=in_specs, out_specs=out_specs, check_vma=False)
```

```python
import jax
import jax.numpy as jnp
from jax import lax
from jax.experimental import pallas as pl
from jax.experimental.pallas import tpu as pltpu
from jax.sharding import Mesh
from jax.sharding import PartitionSpec as P

MODEL_WIDTH = 4096
HEAD_SIZE = 128


rope_base = 500000.0


def position_tables(length, head_dim):
    half_dim = head_dim // 2
    positions = jnp.arange(length, dtype=jnp.float32)
    inverse = jnp.power(
        jnp.float32(rope_base), -2.0 * jnp.arange(half_dim, dtype=jnp.float32) / head_dim
    )
    angles = positions[:, None] * inverse[None, :]
    cosine = jnp.concatenate([jnp.cos(angles), jnp.cos(angles)], axis=-1)[:, None, :]
    sine_table = jnp.concatenate([jnp.sin(angles), jnp.sin(angles)], axis=-1)[:, None, :]
    return (cosine, sine_table)


def half_turn(values):
    lower, upper = jnp.split(values, 2, axis=-1)
    return jnp.concatenate([-upper, lower], axis=-1)


def rotate_forward(values, cosine, sine_table):
    return values * cosine + half_turn(values) * sine_table


def rotate_back(grads, cosine, sine_table):
    return grads * cosine - half_turn(grads * sine_table)


def _turn(x):
    rolled = pltpu.roll(x, HEAD_SIZE // 2, 1)
    lane = lax.broadcasted_iota(jnp.int32, x.shape, 1)
    return jnp.where(lane < HEAD_SIZE // 2, -rolled, rolled)


def _fused_kernel(q_ref, k_ref, v_ref, do_ref, cos_ref, sin_ref, out_ref, dk_acc, dv_acc):
    h = pl.program_id(0)
    heads = pl.num_programs(0)
    scale = 1.0 / jnp.sqrt(jnp.float32(HEAD_SIZE))
    cosine = cos_ref[...]
    sine = sin_ref[...]
    q_raw = q_ref[...]
    k_raw = k_ref[...]
    q = (q_raw * cosine + _turn(q_raw) * sine).astype(jnp.bfloat16)
    k = (k_raw * cosine + _turn(k_raw) * sine).astype(jnp.bfloat16)
    v = v_ref[...].astype(jnp.bfloat16)
    do = do_ref[...]
    nt = (((1,), (1,)), ((), ()))
    tn = (((0,), (0,)), ((), ()))
    s = lax.dot_general(q, k, nt, preferred_element_type=jnp.float32) * scale
    rows = lax.broadcasted_iota(jnp.int32, s.shape, 0)
    cols = lax.broadcasted_iota(jnp.int32, s.shape, 1)
    s = jnp.where(rows >= cols, s, -jnp.inf)
    m = jnp.max(s, axis=1, keepdims=True)
    e = jnp.exp(s - m)
    w = e / jnp.sum(e, axis=1, keepdims=True)
    dp = lax.dot_general(do, v, nt, preferred_element_type=jnp.float32)
    rd = jnp.sum(w * dp, axis=1, keepdims=True)
    ds = (w * (dp - rd) * scale).astype(jnp.bfloat16)
    dq = jnp.dot(ds, k, preferred_element_type=jnp.float32)
    dq = dq * cosine - _turn(dq * sine)
    out_ref[:, pl.ds(pl.multiple_of(h * HEAD_SIZE, HEAD_SIZE), HEAD_SIZE)] = dq.astype(jnp.bfloat16)
    dk = lax.dot_general(ds, q, tn, preferred_element_type=jnp.float32)
    dv = lax.dot_general(w.astype(jnp.bfloat16), do, tn, preferred_element_type=jnp.float32)

    @pl.when(h == 0)
    def _():
        dk_acc[...] = dk
        dv_acc[...] = dv

    @pl.when(h > 0)
    def _():
        dk_acc[...] += dk
        dv_acc[...] += dv

    @pl.when(h == heads - 1)
    def _():
        g = dk_acc[...]
        g = g * cosine - _turn(g * sine)
        out_ref[:, pl.ds(heads * HEAD_SIZE, HEAD_SIZE)] = g.astype(jnp.bfloat16)
        out_ref[:, pl.ds((heads + 1) * HEAD_SIZE, HEAD_SIZE)] = dv_acc[...].astype(jnp.bfloat16)


def attention_fused(projected, upstream, cosine, sine):
    length, width = projected.shape
    heads = width // HEAD_SIZE - 2
    per_head = pl.BlockSpec((length, HEAD_SIZE), lambda h: (0, h))
    key_block = pl.BlockSpec((length, HEAD_SIZE), lambda h: (0, heads))
    value_block = pl.BlockSpec((length, HEAD_SIZE), lambda h: (0, heads + 1))
    table = pl.BlockSpec((length, HEAD_SIZE), lambda h: (0, 0))
    return pl.pallas_call(
        _fused_kernel,
        grid=(heads,),
        in_specs=[per_head, key_block, value_block, per_head, table, table],
        out_specs=pl.BlockSpec((length, width), lambda h: (0, 0)),
        out_shape=jax.ShapeDtypeStruct((length, width), jnp.bfloat16),
        scratch_shapes=[pltpu.VMEM((length, HEAD_SIZE), jnp.float32)] * 2,
        compiler_params=pltpu.CompilerParams(dimension_semantics=("arbitrary",)),
    )(projected, projected, projected, upstream, cosine, sine)


DP_AXES = ("y", "zl", "x")
TP_AXES = ("zh", "c")


def _shift(x, axis, n, step):
    return lax.ppermute(x, axis, [(k, (k + step) % n) for k in range(n)])


def _place(parts, idx, n, dim):
    shape = list(parts[0].shape)
    size = shape[dim]
    shape[dim] = size * n
    out = jnp.zeros(shape, parts[0].dtype)
    for o, p in enumerate(parts):
        start = [0] * len(shape)
        start[dim] = ((idx + o) % n) * size
        out = lax.dynamic_update_slice(out, p, start)
    return out


def ring_gather(x, axis, n, dim):
    idx = lax.axis_index(axis)
    if n == 1:
        return x
    if n == 2:
        return _place([x, _shift(x, axis, 2, 1)], idx, 2, dim)
    assert n == 4
    from_left = _shift(x, axis, 4, 1)
    from_right = _shift(x, axis, 4, -1)
    half = x.shape[-1] // 2
    far_a = _shift(from_right[..., :half], axis, 4, -1)
    far_b = _shift(from_left[..., half:], axis, 4, 1)
    far = jnp.concatenate([far_a, far_b], axis=-1)
    return _place([x, from_right, far, from_left], idx, 4, dim)


def _take(x, pos, dim, n):
    size = x.shape[dim] // n
    return lax.dynamic_slice_in_dim(x, pos * size, size, dim)


def _add(a, b):
    return (a.astype(jnp.float32) + b.astype(jnp.float32)).astype(a.dtype)


def _halves(x, hdim):
    half = x.shape[hdim] // 2
    return (lax.slice_in_dim(x, 0, half, axis=hdim), lax.slice_in_dim(x, half, 2 * half, axis=hdim))


def ring_scatter(x, axis, n, take, hdim=0):
    idx = lax.axis_index(axis)
    if n == 2:
        return _add(take(x, idx), _shift(take(x, (idx + 1) % 2), axis, 2, 1))
    assert n == 4
    far_a, far_b = _halves(take(x, (idx + 2) % 4), hdim)
    right_a, right_b = _halves(take(x, (idx + 1) % 4), hdim)
    left_a, left_b = _halves(take(x, (idx + 3) % 4), hdim)
    got_a = _shift(far_a, axis, 4, 1)
    got_b = _shift(far_b, axis, 4, -1)
    to_right = jnp.concatenate([_add(right_a, got_a), right_b], axis=hdim)
    to_left = jnp.concatenate([left_a, _add(left_b, got_b)], axis=hdim)
    mine = take(x, idx)
    s = _add(mine, _shift(to_right, axis, 4, 1))
    return _add(s, _shift(to_left, axis, 4, -1))


def _cols(starts, width):
    def take(x, j):
        runs = [lax.dynamic_slice_in_dim(x, s(j), width, axis=1) for s in starts]
        return runs[0] if len(runs) == 1 else jnp.concatenate(runs, axis=1)

    return take


def dp_gather(w, sizes=(4, 2, 4)):
    ny, nz, nx = sizes
    r, c = w.shape
    a = w.reshape(1, 1, 1, r, c)
    a = ring_gather(a, "zl", nz, 1)
    h = c // 2
    s1 = ring_gather(ring_gather(a[..., :h], "x", nx, 2), "y", ny, 0)
    s2 = ring_gather(ring_gather(a[..., h:], "y", ny, 0), "x", nx, 2)
    return jnp.concatenate([s1, s2], axis=-1).reshape(ny * nz * nx * r, c)


def dp_scatter_t(g_a, g_b, sizes=(4, 2, 4)):
    ny, nz, nx = sizes
    h, R = g_a.shape
    r = R // (ny * nz * nx)
    zx = nz * nx * r
    s1 = ring_scatter(g_a, "y", ny, _cols([lambda j: j * zx], zx))
    s1 = ring_scatter(s1, "x", nx, _cols([lambda j, z=z: z * nx * r + j * r for z in range(nz)], r))
    s2 = ring_scatter(
        g_b, "x", nx,
        _cols([lambda j, k=k: k * nx * r + j * r for k in range(ny * nz)], r),
    )
    s2 = ring_scatter(s2, "y", ny, _cols([lambda j: j * nz * r], nz * r))
    a = jnp.concatenate([s1, s2], axis=0)
    a = ring_scatter(a, "zl", nz, _cols([lambda j: j * r], r))
    return a.T


def tp_scatter(t):
    w = t.shape[1] // 4
    t = ring_scatter(t, "c", 2, _cols([lambda j, z=z: z * 2 * w + j * w for z in range(2)], w))
    return ring_scatter(t, "zh", 2, _cols([lambda j: j * w], w))


def body(tokens, grad_out, w_query, w_key, value_matrix):
    query_cols = w_query.shape[1]
    key_value_columns = w_key.shape[1]
    kv_dev = key_value_columns // HEAD_SIZE
    weights_all = dp_gather(jnp.concatenate([w_query, w_key, value_matrix], axis=1))
    projected = jnp.dot(tokens, weights_all, preferred_element_type=jnp.float32)
    cosine, sine_table = position_tables(tokens.shape[0], HEAD_SIZE)
    combined = attention_fused(projected, grad_out, cosine[:, 0, :], sine_table[:, 0, :])
    partial_sum = lax.dot_general(
        combined, weights_all, (((1,), (1,)), ((), ())), preferred_element_type=jnp.float32
    )
    part = partial_sum.astype(jnp.bfloat16)
    native_rows = part.shape[0] * 3 // 4
    grad_tokens = jnp.concatenate(
        [
            lax.psum_scatter(part[:native_rows], TP_AXES, scatter_dimension=1, tiled=True),
            tp_scatter(part[native_rows:]),
        ],
        axis=0,
    )
    half = combined.shape[1] // 2

    def weight_grads(cols):
        return lax.dot_general(
            cols, tokens, (((0,), (0,)), ((), ())), preferred_element_type=jnp.float32
        ).astype(jnp.bfloat16)

    grads_all = dp_scatter_t(weight_grads(combined[:, :half]), weight_grads(combined[:, half:]))
    grad_query = grads_all[:, :query_cols]
    grad_key = grads_all[:, query_cols : query_cols + key_value_columns]
    grad_value = grads_all[:, query_cols + key_value_columns :]
    return (grad_tokens, grad_query, grad_key, grad_value)


def solution(mesh):
    view = Mesh(mesh.devices.reshape(4, 2, 4, 2, 2), DP_AXES + TP_AXES)
    rows = P(DP_AXES, None)
    split = P(DP_AXES, TP_AXES)
    in_specs = (rows, split, split, split, split)
    out_specs = (split, split, split, split)
    return jax.shard_map(body, mesh=view, in_specs=in_specs, out_specs=out_specs, check_vma=False)
```

```python
import jax
import jax.numpy as jnp
from jax import lax
from jax.experimental import pallas as pl
from jax.experimental.pallas import tpu as pltpu
from jax.sharding import Mesh
from jax.sharding import PartitionSpec as P

MODEL_WIDTH = 4096
HEAD_SIZE = 128


rope_base = 500000.0


def position_tables(length, head_dim):
    half_dim = head_dim // 2
    positions = jnp.arange(length, dtype=jnp.float32)
    inverse = jnp.power(
        jnp.float32(rope_base), -2.0 * jnp.arange(half_dim, dtype=jnp.float32) / head_dim
    )
    angles = positions[:, None] * inverse[None, :]
    cosine = jnp.concatenate([jnp.cos(angles), jnp.cos(angles)], axis=-1)[:, None, :]
    sine_table = jnp.concatenate([jnp.sin(angles), jnp.sin(angles)], axis=-1)[:, None, :]
    return (cosine, sine_table)


def half_turn(values):
    lower, upper = jnp.split(values, 2, axis=-1)
    return jnp.concatenate([-upper, lower], axis=-1)


def rotate_forward(values, cosine, sine_table):
    return values * cosine + half_turn(values) * sine_table


def rotate_back(grads, cosine, sine_table):
    return grads * cosine - half_turn(grads * sine_table)


def _turn(x):
    rolled = pltpu.roll(x, HEAD_SIZE // 2, 1)
    lane = lax.broadcasted_iota(jnp.int32, x.shape, 1)
    return jnp.where(lane < HEAD_SIZE // 2, -rolled, rolled)


def _fused_kernel(q_ref, k_ref, v_ref, do_ref, cos_ref, sin_ref, out_ref, dk_acc, dv_acc):
    h = pl.program_id(0)
    heads = pl.num_programs(0)
    scale = 1.0 / jnp.sqrt(jnp.float32(HEAD_SIZE))
    cosine = cos_ref[...]
    sine = sin_ref[...]
    q_raw = q_ref[...]
    k_raw = k_ref[...]
    q = (q_raw * cosine + _turn(q_raw) * sine).astype(jnp.bfloat16)
    k = (k_raw * cosine + _turn(k_raw) * sine).astype(jnp.bfloat16)
    v = v_ref[...].astype(jnp.bfloat16)
    do = do_ref[...]
    nt = (((1,), (1,)), ((), ()))
    tn = (((0,), (0,)), ((), ()))
    s = lax.dot_general(q, k, nt, preferred_element_type=jnp.float32) * scale
    rows = lax.broadcasted_iota(jnp.int32, s.shape, 0)
    cols = lax.broadcasted_iota(jnp.int32, s.shape, 1)
    s = jnp.where(rows >= cols, s, -jnp.inf)
    m = jnp.max(s, axis=1, keepdims=True)
    e = jnp.exp(s - m)
    w = e / jnp.sum(e, axis=1, keepdims=True)
    dp = lax.dot_general(do, v, nt, preferred_element_type=jnp.float32)
    rd = jnp.sum(w * dp, axis=1, keepdims=True)
    ds = (w * (dp - rd) * scale).astype(jnp.bfloat16)
    dq = jnp.dot(ds, k, preferred_element_type=jnp.float32)
    dq = dq * cosine - _turn(dq * sine)
    out_ref[:, pl.ds(pl.multiple_of(h * HEAD_SIZE, HEAD_SIZE), HEAD_SIZE)] = dq.astype(jnp.bfloat16)
    dk = lax.dot_general(ds, q, tn, preferred_element_type=jnp.float32)
    dv = lax.dot_general(w.astype(jnp.bfloat16), do, tn, preferred_element_type=jnp.float32)

    @pl.when(h == 0)
    def _():
        dk_acc[...] = dk
        dv_acc[...] = dv

    @pl.when(h > 0)
    def _():
        dk_acc[...] += dk
        dv_acc[...] += dv

    @pl.when(h == heads - 1)
    def _():
        g = dk_acc[...]
        g = g * cosine - _turn(g * sine)
        out_ref[:, pl.ds(heads * HEAD_SIZE, HEAD_SIZE)] = g.astype(jnp.bfloat16)
        out_ref[:, pl.ds((heads + 1) * HEAD_SIZE, HEAD_SIZE)] = dv_acc[...].astype(jnp.bfloat16)


def attention_fused(projected, upstream, cosine, sine):
    length, width = projected.shape
    heads = width // HEAD_SIZE - 2
    per_head = pl.BlockSpec((length, HEAD_SIZE), lambda h: (0, h))
    key_block = pl.BlockSpec((length, HEAD_SIZE), lambda h: (0, heads))
    value_block = pl.BlockSpec((length, HEAD_SIZE), lambda h: (0, heads + 1))
    table = pl.BlockSpec((length, HEAD_SIZE), lambda h: (0, 0))
    return pl.pallas_call(
        _fused_kernel,
        grid=(heads,),
        in_specs=[per_head, key_block, value_block, per_head, table, table],
        out_specs=pl.BlockSpec((length, width), lambda h: (0, 0)),
        out_shape=jax.ShapeDtypeStruct((length, width), jnp.bfloat16),
        scratch_shapes=[pltpu.VMEM((length, HEAD_SIZE), jnp.float32)] * 2,
        compiler_params=pltpu.CompilerParams(dimension_semantics=("arbitrary",)),
    )(projected, projected, projected, upstream, cosine, sine)


DP_AXES = ("y", "zl", "x")
TP_AXES = ("zh", "c")


def _shift(x, axis, n, step):
    return lax.ppermute(x, axis, [(k, (k + step) % n) for k in range(n)])


def _place(parts, idx, n, dim):
    shape = list(parts[0].shape)
    size = shape[dim]
    shape[dim] = size * n
    out = jnp.zeros(shape, parts[0].dtype)
    for o, p in enumerate(parts):
        start = [0] * len(shape)
        start[dim] = ((idx + o) % n) * size
        out = lax.dynamic_update_slice(out, p, start)
    return out


def ring_gather(x, axis, n, dim):
    idx = lax.axis_index(axis)
    if n == 1:
        return x
    if n == 2:
        return _place([x, _shift(x, axis, 2, 1)], idx, 2, dim)
    assert n == 4
    from_left = _shift(x, axis, 4, 1)
    from_right = _shift(x, axis, 4, -1)
    half = x.shape[-1] // 2
    far_a = _shift(from_right[..., :half], axis, 4, -1)
    far_b = _shift(from_left[..., half:], axis, 4, 1)
    far = jnp.concatenate([far_a, far_b], axis=-1)
    return _place([x, from_right, far, from_left], idx, 4, dim)


def _take(x, pos, dim, n):
    size = x.shape[dim] // n
    return lax.dynamic_slice_in_dim(x, pos * size, size, dim)


def _add(a, b):
    return (a.astype(jnp.float32) + b.astype(jnp.float32)).astype(a.dtype)


def _halves(x, hdim):
    half = x.shape[hdim] // 2
    return (lax.slice_in_dim(x, 0, half, axis=hdim), lax.slice_in_dim(x, half, 2 * half, axis=hdim))


def ring_scatter(x, axis, n, take, hdim=0):
    idx = lax.axis_index(axis)
    if n == 2:
        return _add(take(x, idx), _shift(take(x, (idx + 1) % 2), axis, 2, 1))
    assert n == 4
    far_a, far_b = _halves(take(x, (idx + 2) % 4), hdim)
    right_a, right_b = _halves(take(x, (idx + 1) % 4), hdim)
    left_a, left_b = _halves(take(x, (idx + 3) % 4), hdim)
    got_a = _shift(far_a, axis, 4, 1)
    got_b = _shift(far_b, axis, 4, -1)
    to_right = jnp.concatenate([_add(right_a, got_a), right_b], axis=hdim)
    to_left = jnp.concatenate([left_a, _add(left_b, got_b)], axis=hdim)
    mine = take(x, idx)
    s = _add(mine, _shift(to_right, axis, 4, 1))
    return _add(s, _shift(to_left, axis, 4, -1))


def _cols(starts, width):
    def take(x, j):
        runs = [lax.dynamic_slice_in_dim(x, s(j), width, axis=1) for s in starts]
        return runs[0] if len(runs) == 1 else jnp.concatenate(runs, axis=1)

    return take


def dp_gather(w, sizes=(4, 2, 4)):
    ny, nz, nx = sizes
    r, c = w.shape
    a = w.reshape(1, 1, 1, r, c)
    a = ring_gather(a, "zl", nz, 1)
    h = c // 2
    s1 = ring_gather(ring_gather(a[..., :h], "x", nx, 2), "y", ny, 0)
    s2 = ring_gather(ring_gather(a[..., h:], "y", ny, 0), "x", nx, 2)
    return jnp.concatenate([s1, s2], axis=-1).reshape(ny * nz * nx * r, c)


def dp_scatter_t(g, sizes=(4, 2, 4)):
    ny, nz, nx = sizes
    c, R = g.shape
    r = R // (ny * nz * nx)
    h = c // 2
    zx = nz * nx * r
    s1 = ring_scatter(g[:h], "y", ny, _cols([lambda j: j * zx], zx))
    s1 = ring_scatter(s1, "x", nx, _cols([lambda j, z=z: z * nx * r + j * r for z in range(nz)], r))
    s2 = ring_scatter(
        g[h:], "x", nx,
        _cols([lambda j, k=k: k * nx * r + j * r for k in range(ny * nz)], r),
    )
    s2 = ring_scatter(s2, "y", ny, _cols([lambda j: j * nz * r], nz * r))
    a = jnp.concatenate([s1, s2], axis=0)
    a = ring_scatter(a, "zl", nz, _cols([lambda j: j * r], r))
    return a.T


def tp_scatter(t):
    w = t.shape[1] // 4
    t = ring_scatter(t, "c", 2, _cols([lambda j, z=z: z * 2 * w + j * w for z in range(2)], w))
    return ring_scatter(t, "zh", 2, _cols([lambda j: j * w], w))


def body(tokens, grad_out, w_query, w_key, value_matrix):
    query_cols = w_query.shape[1]
    key_value_columns = w_key.shape[1]
    kv_dev = key_value_columns // HEAD_SIZE
    weights_all = dp_gather(jnp.concatenate([w_query, w_key, value_matrix], axis=1))
    projected = jnp.dot(tokens, weights_all, preferred_element_type=jnp.float32)
    cosine, sine_table = position_tables(tokens.shape[0], HEAD_SIZE)
    combined = attention_fused(projected, grad_out, cosine[:, 0, :], sine_table[:, 0, :])
    native_rows = combined.shape[0] * 3 // 4

    def token_grads(rows):
        return lax.dot_general(
            rows, weights_all, (((1,), (1,)), ((), ())), preferred_element_type=jnp.float32
        ).astype(jnp.bfloat16)

    grad_tokens = jnp.concatenate(
        [
            lax.psum_scatter(
                token_grads(combined[:native_rows]), TP_AXES, scatter_dimension=1, tiled=True
            ),
            tp_scatter(token_grads(combined[native_rows:])),
        ],
        axis=0,
    )
    grads_all = dp_scatter_t(
        lax.dot_general(
            combined, tokens, (((0,), (0,)), ((), ())), preferred_element_type=jnp.float32
        ).astype(jnp.bfloat16)
    )
    grad_query = grads_all[:, :query_cols]
    grad_key = grads_all[:, query_cols : query_cols + key_value_columns]
    grad_value = grads_all[:, query_cols + key_value_columns :]
    return (grad_tokens, grad_query, grad_key, grad_value)


def solution(mesh):
    view = Mesh(mesh.devices.reshape(4, 2, 4, 2, 2), DP_AXES + TP_AXES)
    rows = P(DP_AXES, None)
    split = P(DP_AXES, TP_AXES)
    in_specs = (rows, split, split, split, split)
    out_specs = (split, split, split, split)
    return jax.shard_map(body, mesh=view, in_specs=in_specs, out_specs=out_specs, check_vma=False)
```

```python
import jax
import jax.numpy as jnp
from jax import lax
from jax.experimental import pallas as pl
from jax.experimental.pallas import tpu as pltpu
from jax.sharding import Mesh
from jax.sharding import PartitionSpec as P

MODEL_WIDTH = 4096
HEAD_SIZE = 128


rope_base = 500000.0


def position_tables(length, head_dim):
    half_dim = head_dim // 2
    positions = jnp.arange(length, dtype=jnp.float32)
    inverse = jnp.power(
        jnp.float32(rope_base), -2.0 * jnp.arange(half_dim, dtype=jnp.float32) / head_dim
    )
    angles = positions[:, None] * inverse[None, :]
    cosine = jnp.concatenate([jnp.cos(angles), jnp.cos(angles)], axis=-1)[:, None, :]
    sine_table = jnp.concatenate([jnp.sin(angles), jnp.sin(angles)], axis=-1)[:, None, :]
    return (cosine, sine_table)


def half_turn(values):
    lower, upper = jnp.split(values, 2, axis=-1)
    return jnp.concatenate([-upper, lower], axis=-1)


def rotate_forward(values, cosine, sine_table):
    return values * cosine + half_turn(values) * sine_table


def rotate_back(grads, cosine, sine_table):
    return grads * cosine - half_turn(grads * sine_table)


def _turn(x):
    rolled = pltpu.roll(x, HEAD_SIZE // 2, 1)
    lane = lax.broadcasted_iota(jnp.int32, x.shape, 1)
    return jnp.where(lane < HEAD_SIZE // 2, -rolled, rolled)


def _fused_kernel(q_ref, k_ref, v_ref, do_ref, cos_ref, sin_ref, out_ref, dk_acc, dv_acc):
    h = pl.program_id(0)
    heads = pl.num_programs(0)
    scale = 1.0 / jnp.sqrt(jnp.float32(HEAD_SIZE))
    cosine = cos_ref[...]
    sine = sin_ref[...]
    q_raw = q_ref[...]
    k_raw = k_ref[...]
    q = (q_raw * cosine + _turn(q_raw) * sine).astype(jnp.bfloat16)
    k = (k_raw * cosine + _turn(k_raw) * sine).astype(jnp.bfloat16)
    v = v_ref[...].astype(jnp.bfloat16)
    nt = (((1,), (1,)), ((), ()))
    tn = (((0,), (0,)), ((), ()))
    length = q.shape[0]
    step = length // 4
    dq_rows = []
    dk = jnp.zeros((length, HEAD_SIZE), jnp.float32)
    dv = jnp.zeros((length, HEAD_SIZE), jnp.float32)
    for i in range(4):
        lo, hi = i * step, (i + 1) * step
        q_i = q[lo:hi]
        k_i = k[:hi]
        do_i = do_ref[lo:hi, :]
        s = lax.dot_general(q_i, k_i, nt, preferred_element_type=jnp.float32) * scale
        rows = lax.broadcasted_iota(jnp.int32, s.shape, 0) + lo
        cols = lax.broadcasted_iota(jnp.int32, s.shape, 1)
        s = jnp.where(rows >= cols, s, -jnp.inf)
        m = jnp.max(s, axis=1, keepdims=True)
        e = jnp.exp(s - m)
        w = e / jnp.sum(e, axis=1, keepdims=True)
        dp = lax.dot_general(do_i, v[:hi], nt, preferred_element_type=jnp.float32)
        rd = jnp.sum(w * dp, axis=1, keepdims=True)
        ds = (w * (dp - rd) * scale).astype(jnp.bfloat16)
        dq_rows.append(jnp.dot(ds, k_i, preferred_element_type=jnp.float32))
        dk_i = lax.dot_general(ds, q_i, tn, preferred_element_type=jnp.float32)
        dv_i = lax.dot_general(w.astype(jnp.bfloat16), do_i, tn, preferred_element_type=jnp.float32)
        if hi < length:
            pad = jnp.zeros((length - hi, HEAD_SIZE), jnp.float32)
            dk_i = jnp.concatenate([dk_i, pad], axis=0)
            dv_i = jnp.concatenate([dv_i, pad], axis=0)
        dk = dk + dk_i
        dv = dv + dv_i
    dq = jnp.concatenate(dq_rows, axis=0)
    dq = dq * cosine - _turn(dq * sine)
    out_ref[:, pl.ds(pl.multiple_of(h * HEAD_SIZE, HEAD_SIZE), HEAD_SIZE)] = dq.astype(jnp.bfloat16)

    @pl.when(h == 0)
    def _():
        dk_acc[...] = dk
        dv_acc[...] = dv

    @pl.when(h > 0)
    def _():
        dk_acc[...] += dk
        dv_acc[...] += dv

    @pl.when(h == heads - 1)
    def _():
        g = dk_acc[...]
        g = g * cosine - _turn(g * sine)
        out_ref[:, pl.ds(heads * HEAD_SIZE, HEAD_SIZE)] = g.astype(jnp.bfloat16)
        out_ref[:, pl.ds((heads + 1) * HEAD_SIZE, HEAD_SIZE)] = dv_acc[...].astype(jnp.bfloat16)


def attention_fused(projected, upstream, cosine, sine):
    length, width = projected.shape
    heads = width // HEAD_SIZE - 2
    per_head = pl.BlockSpec((length, HEAD_SIZE), lambda h: (0, h))
    key_block = pl.BlockSpec((length, HEAD_SIZE), lambda h: (0, heads))
    value_block = pl.BlockSpec((length, HEAD_SIZE), lambda h: (0, heads + 1))
    table = pl.BlockSpec((length, HEAD_SIZE), lambda h: (0, 0))
    return pl.pallas_call(
        _fused_kernel,
        grid=(heads,),
        in_specs=[per_head, key_block, value_block, per_head, table, table],
        out_specs=pl.BlockSpec((length, width), lambda h: (0, 0)),
        out_shape=jax.ShapeDtypeStruct((length, width), jnp.bfloat16),
        scratch_shapes=[pltpu.VMEM((length, HEAD_SIZE), jnp.float32)] * 2,
        compiler_params=pltpu.CompilerParams(dimension_semantics=("arbitrary",)),
    )(projected, projected, projected, upstream, cosine, sine)


DP_AXES = ("y", "zl", "x")
TP_AXES = ("zh", "c")


def _shift(x, axis, n, step):
    return lax.ppermute(x, axis, [(k, (k + step) % n) for k in range(n)])


def _place(parts, idx, n, dim):
    shape = list(parts[0].shape)
    size = shape[dim]
    shape[dim] = size * n
    out = jnp.zeros(shape, parts[0].dtype)
    for o, p in enumerate(parts):
        start = [0] * len(shape)
        start[dim] = ((idx + o) % n) * size
        out = lax.dynamic_update_slice(out, p, start)
    return out


def ring_gather(x, axis, n, dim):
    idx = lax.axis_index(axis)
    if n == 1:
        return x
    if n == 2:
        return _place([x, _shift(x, axis, 2, 1)], idx, 2, dim)
    assert n == 4
    from_left = _shift(x, axis, 4, 1)
    from_right = _shift(x, axis, 4, -1)
    half = x.shape[-1] // 2
    far_a = _shift(from_right[..., :half], axis, 4, -1)
    far_b = _shift(from_left[..., half:], axis, 4, 1)
    far = jnp.concatenate([far_a, far_b], axis=-1)
    return _place([x, from_right, far, from_left], idx, 4, dim)


def _take(x, pos, dim, n):
    size = x.shape[dim] // n
    return lax.dynamic_slice_in_dim(x, pos * size, size, dim)


def _add(a, b):
    return (a.astype(jnp.float32) + b.astype(jnp.float32)).astype(a.dtype)


def _halves(x, hdim):
    half = x.shape[hdim] // 2
    return (lax.slice_in_dim(x, 0, half, axis=hdim), lax.slice_in_dim(x, half, 2 * half, axis=hdim))


def ring_scatter(x, axis, n, take, hdim=0):
    idx = lax.axis_index(axis)
    if n == 2:
        return _add(take(x, idx), _shift(take(x, (idx + 1) % 2), axis, 2, 1))
    assert n == 4
    far_a, far_b = _halves(take(x, (idx + 2) % 4), hdim)
    right_a, right_b = _halves(take(x, (idx + 1) % 4), hdim)
    left_a, left_b = _halves(take(x, (idx + 3) % 4), hdim)
    got_a = _shift(far_a, axis, 4, 1)
    got_b = _shift(far_b, axis, 4, -1)
    to_right = jnp.concatenate([_add(right_a, got_a), right_b], axis=hdim)
    to_left = jnp.concatenate([left_a, _add(left_b, got_b)], axis=hdim)
    mine = take(x, idx)
    s = _add(mine, _shift(to_right, axis, 4, 1))
    return _add(s, _shift(to_left, axis, 4, -1))


def _cols(starts, width):
    def take(x, j):
        runs = [lax.dynamic_slice_in_dim(x, s(j), width, axis=1) for s in starts]
        return runs[0] if len(runs) == 1 else jnp.concatenate(runs, axis=1)

    return take


def dp_gather(w, sizes=(4, 2, 4)):
    ny, nz, nx = sizes
    r, c = w.shape
    a = w.reshape(1, 1, 1, r, c)
    a = ring_gather(a, "zl", nz, 1)
    h = c // 2
    s1 = ring_gather(ring_gather(a[..., :h], "x", nx, 2), "y", ny, 0)
    s2 = ring_gather(ring_gather(a[..., h:], "y", ny, 0), "x", nx, 2)
    return jnp.concatenate([s1, s2], axis=-1).reshape(ny * nz * nx * r, c)


def dp_scatter_t(g, sizes=(4, 2, 4)):
    ny, nz, nx = sizes
    c, R = g.shape
    r = R // (ny * nz * nx)
    h = c // 2
    zx = nz * nx * r
    s1 = ring_scatter(g[:h], "y", ny, _cols([lambda j: j * zx], zx))
    s1 = ring_scatter(s1, "x", nx, _cols([lambda j, z=z: z * nx * r + j * r for z in range(nz)], r))
    s2 = ring_scatter(
        g[h:], "x", nx,
        _cols([lambda j, k=k: k * nx * r + j * r for k in range(ny * nz)], r),
    )
    s2 = ring_scatter(s2, "y", ny, _cols([lambda j: j * nz * r], nz * r))
    a = jnp.concatenate([s1, s2], axis=0)
    a = ring_scatter(a, "zl", nz, _cols([lambda j: j * r], r))
    return a.T


def tp_scatter(t):
    w = t.shape[1] // 4
    t = ring_scatter(t, "c", 2, _cols([lambda j, z=z: z * 2 * w + j * w for z in range(2)], w))
    return ring_scatter(t, "zh", 2, _cols([lambda j: j * w], w))


def body(tokens, grad_out, w_query, w_key, value_matrix):
    query_cols = w_query.shape[1]
    key_value_columns = w_key.shape[1]
    kv_dev = key_value_columns // HEAD_SIZE
    weights_all = dp_gather(jnp.concatenate([w_query, w_key, value_matrix], axis=1))
    projected = jnp.dot(tokens, weights_all, preferred_element_type=jnp.float32)
    cosine, sine_table = position_tables(tokens.shape[0], HEAD_SIZE)
    combined = attention_fused(projected, grad_out, cosine[:, 0, :], sine_table[:, 0, :])
    native_rows = combined.shape[0] * 3 // 4

    def token_grads(rows):
        return lax.dot_general(
            rows, weights_all, (((1,), (1,)), ((), ())), preferred_element_type=jnp.float32
        ).astype(jnp.bfloat16)

    grad_tokens = jnp.concatenate(
        [
            lax.psum_scatter(
                token_grads(combined[:native_rows]), TP_AXES, scatter_dimension=1, tiled=True
            ),
            tp_scatter(token_grads(combined[native_rows:])),
        ],
        axis=0,
    )
    grads_all = dp_scatter_t(
        lax.dot_general(
            combined, tokens, (((0,), (0,)), ((), ())), preferred_element_type=jnp.float32
        ).astype(jnp.bfloat16)
    )
    grad_query = grads_all[:, :query_cols]
    grad_key = grads_all[:, query_cols : query_cols + key_value_columns]
    grad_value = grads_all[:, query_cols + key_value_columns :]
    return (grad_tokens, grad_query, grad_key, grad_value)


def solution(mesh):
    view = Mesh(mesh.devices.reshape(4, 2, 4, 2, 2), DP_AXES + TP_AXES)
    rows = P(DP_AXES, None)
    split = P(DP_AXES, TP_AXES)
    in_specs = (rows, split, split, split, split)
    out_specs = (split, split, split, split)
    return jax.shard_map(body, mesh=view, in_specs=in_specs, out_specs=out_specs, check_vma=False)
```

```python
import jax
import jax.numpy as jnp
from jax import lax
from jax.experimental import pallas as pl
from jax.experimental.pallas import tpu as pltpu
from jax.sharding import Mesh
from jax.sharding import PartitionSpec as P

MODEL_WIDTH = 4096
HEAD_SIZE = 128


rope_base = 500000.0


def position_tables(length, head_dim):
    half_dim = head_dim // 2
    positions = jnp.arange(length, dtype=jnp.float32)
    inverse = jnp.power(
        jnp.float32(rope_base), -2.0 * jnp.arange(half_dim, dtype=jnp.float32) / head_dim
    )
    angles = positions[:, None] * inverse[None, :]
    cosine = jnp.concatenate([jnp.cos(angles), jnp.cos(angles)], axis=-1)[:, None, :]
    sine_table = jnp.concatenate([jnp.sin(angles), jnp.sin(angles)], axis=-1)[:, None, :]
    return (cosine, sine_table)


def half_turn(values):
    lower, upper = jnp.split(values, 2, axis=-1)
    return jnp.concatenate([-upper, lower], axis=-1)


def rotate_forward(values, cosine, sine_table):
    return values * cosine + half_turn(values) * sine_table


def rotate_back(grads, cosine, sine_table):
    return grads * cosine - half_turn(grads * sine_table)


def _turn(x):
    rolled = pltpu.roll(x, HEAD_SIZE // 2, 1)
    lane = lax.broadcasted_iota(jnp.int32, x.shape, 1)
    return jnp.where(lane < HEAD_SIZE // 2, -rolled, rolled)


def _fused_kernel(q_ref, k_ref, v_ref, do_ref, cos_ref, sin_ref, out_ref, dk_acc, dv_acc):
    h = pl.program_id(0)
    heads = pl.num_programs(0)
    scale = 1.0 / jnp.sqrt(jnp.float32(HEAD_SIZE))
    cosine = cos_ref[...]
    sine = sin_ref[...]
    q_raw = q_ref[...]
    k_raw = k_ref[...]
    q = (q_raw * cosine + _turn(q_raw) * sine).astype(jnp.bfloat16)
    k = (k_raw * cosine + _turn(k_raw) * sine).astype(jnp.bfloat16)
    v = v_ref[...].astype(jnp.bfloat16)
    nt = (((1,), (1,)), ((), ()))
    tn = (((0,), (0,)), ((), ()))
    length = q.shape[0]
    blocks = 8
    step = length // blocks
    dq_rows = []
    dk = jnp.zeros((length, HEAD_SIZE), jnp.float32)
    dv = jnp.zeros((length, HEAD_SIZE), jnp.float32)
    for i in range(blocks):
        lo, hi = i * step, (i + 1) * step
        q_i = q[lo:hi]
        k_i = k[:hi]
        do_i = do_ref[lo:hi, :]
        s = lax.dot_general(q_i, k_i, nt, preferred_element_type=jnp.float32) * scale
        rows = lax.broadcasted_iota(jnp.int32, s.shape, 0) + lo
        cols = lax.broadcasted_iota(jnp.int32, s.shape, 1)
        s = jnp.where(rows >= cols, s, -jnp.inf)
        m = jnp.max(s, axis=1, keepdims=True)
        e = jnp.exp(s - m)
        w = e / jnp.sum(e, axis=1, keepdims=True)
        dp = lax.dot_general(do_i, v[:hi], nt, preferred_element_type=jnp.float32)
        rd = jnp.sum(w * dp, axis=1, keepdims=True)
        ds = (w * (dp - rd) * scale).astype(jnp.bfloat16)
        dq_rows.append(jnp.dot(ds, k_i, preferred_element_type=jnp.float32))
        dk_i = lax.dot_general(ds, q_i, tn, preferred_element_type=jnp.float32)
        dv_i = lax.dot_general(w.astype(jnp.bfloat16), do_i, tn, preferred_element_type=jnp.float32)
        if hi < length:
            pad = jnp.zeros((length - hi, HEAD_SIZE), jnp.float32)
            dk_i = jnp.concatenate([dk_i, pad], axis=0)
            dv_i = jnp.concatenate([dv_i, pad], axis=0)
        dk = dk + dk_i
        dv = dv + dv_i
    dq = jnp.concatenate(dq_rows, axis=0)
    dq = dq * cosine - _turn(dq * sine)
    out_ref[:, pl.ds(pl.multiple_of(h * HEAD_SIZE, HEAD_SIZE), HEAD_SIZE)] = dq.astype(jnp.bfloat16)

    @pl.when(h == 0)
    def _():
        dk_acc[...] = dk
        dv_acc[...] = dv

    @pl.when(h > 0)
    def _():
        dk_acc[...] += dk
        dv_acc[...] += dv

    @pl.when(h == heads - 1)
    def _():
        g = dk_acc[...]
        g = g * cosine - _turn(g * sine)
        out_ref[:, pl.ds(heads * HEAD_SIZE, HEAD_SIZE)] = g.astype(jnp.bfloat16)
        out_ref[:, pl.ds((heads + 1) * HEAD_SIZE, HEAD_SIZE)] = dv_acc[...].astype(jnp.bfloat16)


def attention_fused(projected, upstream, cosine, sine):
    length, width = projected.shape
    heads = width // HEAD_SIZE - 2
    per_head = pl.BlockSpec((length, HEAD_SIZE), lambda h: (0, h))
    key_block = pl.BlockSpec((length, HEAD_SIZE), lambda h: (0, heads))
    value_block = pl.BlockSpec((length, HEAD_SIZE), lambda h: (0, heads + 1))
    table = pl.BlockSpec((length, HEAD_SIZE), lambda h: (0, 0))
    return pl.pallas_call(
        _fused_kernel,
        grid=(heads,),
        in_specs=[per_head, key_block, value_block, per_head, table, table],
        out_specs=pl.BlockSpec((length, width), lambda h: (0, 0)),
        out_shape=jax.ShapeDtypeStruct((length, width), jnp.bfloat16),
        scratch_shapes=[pltpu.VMEM((length, HEAD_SIZE), jnp.float32)] * 2,
        compiler_params=pltpu.CompilerParams(dimension_semantics=("arbitrary",)),
    )(projected, projected, projected, upstream, cosine, sine)


DP_AXES = ("y", "zl", "x")
TP_AXES = ("zh", "c")


def _shift(x, axis, n, step):
    return lax.ppermute(x, axis, [(k, (k + step) % n) for k in range(n)])


def _place(parts, idx, n, dim):
    shape = list(parts[0].shape)
    size = shape[dim]
    shape[dim] = size * n
    out = jnp.zeros(shape, parts[0].dtype)
    for o, p in enumerate(parts):
        start = [0] * len(shape)
        start[dim] = ((idx + o) % n) * size
        out = lax.dynamic_update_slice(out, p, start)
    return out


def ring_gather(x, axis, n, dim):
    idx = lax.axis_index(axis)
    if n == 1:
        return x
    if n == 2:
        return _place([x, _shift(x, axis, 2, 1)], idx, 2, dim)
    assert n == 4
    from_left = _shift(x, axis, 4, 1)
    from_right = _shift(x, axis, 4, -1)
    half = x.shape[-1] // 2
    far_a = _shift(from_right[..., :half], axis, 4, -1)
    far_b = _shift(from_left[..., half:], axis, 4, 1)
    far = jnp.concatenate([far_a, far_b], axis=-1)
    return _place([x, from_right, far, from_left], idx, 4, dim)


def _take(x, pos, dim, n):
    size = x.shape[dim] // n
    return lax.dynamic_slice_in_dim(x, pos * size, size, dim)


def _add(a, b):
    return (a.astype(jnp.float32) + b.astype(jnp.float32)).astype(a.dtype)


def _halves(x, hdim):
    half = x.shape[hdim] // 2
    return (lax.slice_in_dim(x, 0, half, axis=hdim), lax.slice_in_dim(x, half, 2 * half, axis=hdim))


def ring_scatter(x, axis, n, take, hdim=0):
    idx = lax.axis_index(axis)
    if n == 2:
        return _add(take(x, idx), _shift(take(x, (idx + 1) % 2), axis, 2, 1))
    assert n == 4
    far_a, far_b = _halves(take(x, (idx + 2) % 4), hdim)
    right_a, right_b = _halves(take(x, (idx + 1) % 4), hdim)
    left_a, left_b = _halves(take(x, (idx + 3) % 4), hdim)
    got_a = _shift(far_a, axis, 4, 1)
    got_b = _shift(far_b, axis, 4, -1)
    to_right = jnp.concatenate([_add(right_a, got_a), right_b], axis=hdim)
    to_left = jnp.concatenate([left_a, _add(left_b, got_b)], axis=hdim)
    mine = take(x, idx)
    s = _add(mine, _shift(to_right, axis, 4, 1))
    return _add(s, _shift(to_left, axis, 4, -1))


def _cols(starts, width):
    def take(x, j):
        runs = [lax.dynamic_slice_in_dim(x, s(j), width, axis=1) for s in starts]
        return runs[0] if len(runs) == 1 else jnp.concatenate(runs, axis=1)

    return take


def dp_gather(w, sizes=(4, 2, 4)):
    ny, nz, nx = sizes
    r, c = w.shape
    a = w.reshape(1, 1, 1, r, c)
    a = ring_gather(a, "zl", nz, 1)
    h = c // 2
    s1 = ring_gather(ring_gather(a[..., :h], "x", nx, 2), "y", ny, 0)
    s2 = ring_gather(ring_gather(a[..., h:], "y", ny, 0), "x", nx, 2)
    return jnp.concatenate([s1, s2], axis=-1).reshape(ny * nz * nx * r, c)


def dp_scatter_t(g, sizes=(4, 2, 4)):
    ny, nz, nx = sizes
    c, R = g.shape
    r = R // (ny * nz * nx)
    h = c // 2
    zx = nz * nx * r
    s1 = ring_scatter(g[:h], "y", ny, _cols([lambda j: j * zx], zx))
    s1 = ring_scatter(s1, "x", nx, _cols([lambda j, z=z: z * nx * r + j * r for z in range(nz)], r))
    s2 = ring_scatter(
        g[h:], "x", nx,
        _cols([lambda j, k=k: k * nx * r + j * r for k in range(ny * nz)], r),
    )
    s2 = ring_scatter(s2, "y", ny, _cols([lambda j: j * nz * r], nz * r))
    a = jnp.concatenate([s1, s2], axis=0)
    a = ring_scatter(a, "zl", nz, _cols([lambda j: j * r], r))
    return a.T


def tp_scatter(t):
    w = t.shape[1] // 4
    t = ring_scatter(t, "c", 2, _cols([lambda j, z=z: z * 2 * w + j * w for z in range(2)], w))
    return ring_scatter(t, "zh", 2, _cols([lambda j: j * w], w))


def body(tokens, grad_out, w_query, w_key, value_matrix):
    query_cols = w_query.shape[1]
    key_value_columns = w_key.shape[1]
    kv_dev = key_value_columns // HEAD_SIZE
    weights_all = dp_gather(jnp.concatenate([w_query, w_key, value_matrix], axis=1))
    projected = jnp.dot(tokens, weights_all, preferred_element_type=jnp.float32)
    cosine, sine_table = position_tables(tokens.shape[0], HEAD_SIZE)
    combined = attention_fused(projected, grad_out, cosine[:, 0, :], sine_table[:, 0, :])
    native_rows = combined.shape[0] * 3 // 4

    def token_grads(rows):
        return lax.dot_general(
            rows, weights_all, (((1,), (1,)), ((), ())), preferred_element_type=jnp.float32
        ).astype(jnp.bfloat16)

    grad_tokens = jnp.concatenate(
        [
            lax.psum_scatter(
                token_grads(combined[:native_rows]), TP_AXES, scatter_dimension=1, tiled=True
            ),
            tp_scatter(token_grads(combined[native_rows:])),
        ],
        axis=0,
    )
    grads_all = dp_scatter_t(
        lax.dot_general(
            combined, tokens, (((0,), (0,)), ((), ())), preferred_element_type=jnp.float32
        ).astype(jnp.bfloat16)
    )
    grad_query = grads_all[:, :query_cols]
    grad_key = grads_all[:, query_cols : query_cols + key_value_columns]
    grad_value = grads_all[:, query_cols + key_value_columns :]
    return (grad_tokens, grad_query, grad_key, grad_value)


def solution(mesh):
    view = Mesh(mesh.devices.reshape(4, 2, 4, 2, 2), DP_AXES + TP_AXES)
    rows = P(DP_AXES, None)
    split = P(DP_AXES, TP_AXES)
    in_specs = (rows, split, split, split, split)
    out_specs = (split, split, split, split)
    return jax.shard_map(body, mesh=view, in_specs=in_specs, out_specs=out_specs, check_vma=False)
```

```python
import jax
import jax.numpy as jnp
from jax import lax
from jax.experimental import pallas as pl
from jax.experimental.pallas import tpu as pltpu
from jax.sharding import Mesh
from jax.sharding import PartitionSpec as P

MODEL_WIDTH = 4096
HEAD_SIZE = 128


rope_base = 500000.0


def position_tables(length, head_dim):
    half_dim = head_dim // 2
    positions = jnp.arange(length, dtype=jnp.float32)
    inverse = jnp.power(
        jnp.float32(rope_base), -2.0 * jnp.arange(half_dim, dtype=jnp.float32) / head_dim
    )
    angles = positions[:, None] * inverse[None, :]
    cosine = jnp.concatenate([jnp.cos(angles), jnp.cos(angles)], axis=-1)[:, None, :]
    sine_table = jnp.concatenate([jnp.sin(angles), jnp.sin(angles)], axis=-1)[:, None, :]
    return (cosine, sine_table)


def half_turn(values):
    lower, upper = jnp.split(values, 2, axis=-1)
    return jnp.concatenate([-upper, lower], axis=-1)


def rotate_forward(values, cosine, sine_table):
    return values * cosine + half_turn(values) * sine_table


def rotate_back(grads, cosine, sine_table):
    return grads * cosine - half_turn(grads * sine_table)


def _turn(x):
    rolled = pltpu.roll(x, HEAD_SIZE // 2, 1)
    lane = lax.broadcasted_iota(jnp.int32, x.shape, 1)
    return jnp.where(lane < HEAD_SIZE // 2, -rolled, rolled)


def _fused_kernel(q_ref, k_ref, v_ref, do_ref, cos_ref, sin_ref, out_ref, dk_acc, dv_acc):
    h = pl.program_id(0)
    heads = pl.num_programs(0)
    scale = 1.0 / jnp.sqrt(jnp.float32(HEAD_SIZE))
    cosine = cos_ref[...]
    sine = sin_ref[...]
    q_raw = q_ref[...]
    k_raw = k_ref[...]
    q = (q_raw * cosine + _turn(q_raw) * sine).astype(jnp.bfloat16)
    k = (k_raw * cosine + _turn(k_raw) * sine).astype(jnp.bfloat16)
    v = v_ref[...].astype(jnp.bfloat16)
    nt = (((1,), (1,)), ((), ()))
    tn = (((0,), (0,)), ((), ()))
    length = q.shape[0]
    blocks = 2
    step = length // blocks
    dq_rows = []
    dk = jnp.zeros((length, HEAD_SIZE), jnp.float32)
    dv = jnp.zeros((length, HEAD_SIZE), jnp.float32)
    for i in range(blocks):
        lo, hi = i * step, (i + 1) * step
        q_i = q[lo:hi]
        k_i = k[:hi]
        do_i = do_ref[lo:hi, :]
        s = lax.dot_general(q_i, k_i, nt, preferred_element_type=jnp.float32) * scale
        rows = lax.broadcasted_iota(jnp.int32, s.shape, 0) + lo
        cols = lax.broadcasted_iota(jnp.int32, s.shape, 1)
        s = jnp.where(rows >= cols, s, -jnp.inf)
        m = jnp.max(s, axis=1, keepdims=True)
        e = jnp.exp(s - m)
        w = e / jnp.sum(e, axis=1, keepdims=True)
        dp = lax.dot_general(do_i, v[:hi], nt, preferred_element_type=jnp.float32)
        rd = jnp.sum(w * dp, axis=1, keepdims=True)
        ds = (w * (dp - rd) * scale).astype(jnp.bfloat16)
        dq_rows.append(jnp.dot(ds, k_i, preferred_element_type=jnp.float32))
        dk_i = lax.dot_general(ds, q_i, tn, preferred_element_type=jnp.float32)
        dv_i = lax.dot_general(w.astype(jnp.bfloat16), do_i, tn, preferred_element_type=jnp.float32)
        if hi < length:
            pad = jnp.zeros((length - hi, HEAD_SIZE), jnp.float32)
            dk_i = jnp.concatenate([dk_i, pad], axis=0)
            dv_i = jnp.concatenate([dv_i, pad], axis=0)
        dk = dk + dk_i
        dv = dv + dv_i
    dq = jnp.concatenate(dq_rows, axis=0)
    dq = dq * cosine - _turn(dq * sine)
    out_ref[:, pl.ds(pl.multiple_of(h * HEAD_SIZE, HEAD_SIZE), HEAD_SIZE)] = dq.astype(jnp.bfloat16)

    @pl.when(h == 0)
    def _():
        dk_acc[...] = dk
        dv_acc[...] = dv

    @pl.when(h > 0)
    def _():
        dk_acc[...] += dk
        dv_acc[...] += dv

    @pl.when(h == heads - 1)
    def _():
        g = dk_acc[...]
        g = g * cosine - _turn(g * sine)
        out_ref[:, pl.ds(heads * HEAD_SIZE, HEAD_SIZE)] = g.astype(jnp.bfloat16)
        out_ref[:, pl.ds((heads + 1) * HEAD_SIZE, HEAD_SIZE)] = dv_acc[...].astype(jnp.bfloat16)


def attention_fused(projected, upstream, cosine, sine):
    length, width = projected.shape
    heads = width // HEAD_SIZE - 2
    per_head = pl.BlockSpec((length, HEAD_SIZE), lambda h: (0, h))
    key_block = pl.BlockSpec((length, HEAD_SIZE), lambda h: (0, heads))
    value_block = pl.BlockSpec((length, HEAD_SIZE), lambda h: (0, heads + 1))
    table = pl.BlockSpec((length, HEAD_SIZE), lambda h: (0, 0))
    return pl.pallas_call(
        _fused_kernel,
        grid=(heads,),
        in_specs=[per_head, key_block, value_block, per_head, table, table],
        out_specs=pl.BlockSpec((length, width), lambda h: (0, 0)),
        out_shape=jax.ShapeDtypeStruct((length, width), jnp.bfloat16),
        scratch_shapes=[pltpu.VMEM((length, HEAD_SIZE), jnp.float32)] * 2,
        compiler_params=pltpu.CompilerParams(dimension_semantics=("arbitrary",)),
    )(projected, projected, projected, upstream, cosine, sine)


DP_AXES = ("y", "zl", "x")
TP_AXES = ("zh", "c")


def _shift(x, axis, n, step):
    return lax.ppermute(x, axis, [(k, (k + step) % n) for k in range(n)])


def _place(parts, idx, n, dim):
    shape = list(parts[0].shape)
    size = shape[dim]
    shape[dim] = size * n
    out = jnp.zeros(shape, parts[0].dtype)
    for o, p in enumerate(parts):
        start = [0] * len(shape)
        start[dim] = ((idx + o) % n) * size
        out = lax.dynamic_update_slice(out, p, start)
    return out


def ring_gather(x, axis, n, dim):
    idx = lax.axis_index(axis)
    if n == 1:
        return x
    if n == 2:
        return _place([x, _shift(x, axis, 2, 1)], idx, 2, dim)
    assert n == 4
    from_left = _shift(x, axis, 4, 1)
    from_right = _shift(x, axis, 4, -1)
    half = x.shape[-1] // 2
    far_a = _shift(from_right[..., :half], axis, 4, -1)
    far_b = _shift(from_left[..., half:], axis, 4, 1)
    far = jnp.concatenate([far_a, far_b], axis=-1)
    return _place([x, from_right, far, from_left], idx, 4, dim)


def _take(x, pos, dim, n):
    size = x.shape[dim] // n
    return lax.dynamic_slice_in_dim(x, pos * size, size, dim)


def _add(a, b):
    return (a.astype(jnp.float32) + b.astype(jnp.float32)).astype(a.dtype)


def _halves(x, hdim):
    half = x.shape[hdim] // 2
    return (lax.slice_in_dim(x, 0, half, axis=hdim), lax.slice_in_dim(x, half, 2 * half, axis=hdim))


def ring_scatter(x, axis, n, take, hdim=0):
    idx = lax.axis_index(axis)
    if n == 2:
        return _add(take(x, idx), _shift(take(x, (idx + 1) % 2), axis, 2, 1))
    assert n == 4
    far_a, far_b = _halves(take(x, (idx + 2) % 4), hdim)
    right_a, right_b = _halves(take(x, (idx + 1) % 4), hdim)
    left_a, left_b = _halves(take(x, (idx + 3) % 4), hdim)
    got_a = _shift(far_a, axis, 4, 1)
    got_b = _shift(far_b, axis, 4, -1)
    to_right = jnp.concatenate([_add(right_a, got_a), right_b], axis=hdim)
    to_left = jnp.concatenate([left_a, _add(left_b, got_b)], axis=hdim)
    mine = take(x, idx)
    s = _add(mine, _shift(to_right, axis, 4, 1))
    return _add(s, _shift(to_left, axis, 4, -1))


def _cols(starts, width):
    def take(x, j):
        runs = [lax.dynamic_slice_in_dim(x, s(j), width, axis=1) for s in starts]
        return runs[0] if len(runs) == 1 else jnp.concatenate(runs, axis=1)

    return take


def dp_gather(w, sizes=(4, 2, 4)):
    ny, nz, nx = sizes
    r, c = w.shape
    a = w.reshape(1, 1, 1, r, c)
    a = ring_gather(a, "zl", nz, 1)
    h = c // 2
    s1 = ring_gather(ring_gather(a[..., :h], "x", nx, 2), "y", ny, 0)
    s2 = ring_gather(ring_gather(a[..., h:], "y", ny, 0), "x", nx, 2)
    return jnp.concatenate([s1, s2], axis=-1).reshape(ny * nz * nx * r, c)


def dp_scatter_t(g, sizes=(4, 2, 4)):
    ny, nz, nx = sizes
    c, R = g.shape
    r = R // (ny * nz * nx)
    h = c // 2
    zx = nz * nx * r
    s1 = ring_scatter(g[:h], "y", ny, _cols([lambda j: j * zx], zx))
    s1 = ring_scatter(s1, "x", nx, _cols([lambda j, z=z: z * nx * r + j * r for z in range(nz)], r))
    s2 = ring_scatter(
        g[h:], "x", nx,
        _cols([lambda j, k=k: k * nx * r + j * r for k in range(ny * nz)], r),
    )
    s2 = ring_scatter(s2, "y", ny, _cols([lambda j: j * nz * r], nz * r))
    a = jnp.concatenate([s1, s2], axis=0)
    a = ring_scatter(a, "zl", nz, _cols([lambda j: j * r], r))
    return a.T


def tp_scatter(t):
    w = t.shape[1] // 4
    t = ring_scatter(t, "c", 2, _cols([lambda j, z=z: z * 2 * w + j * w for z in range(2)], w))
    return ring_scatter(t, "zh", 2, _cols([lambda j: j * w], w))


def body(tokens, grad_out, w_query, w_key, value_matrix):
    query_cols = w_query.shape[1]
    key_value_columns = w_key.shape[1]
    kv_dev = key_value_columns // HEAD_SIZE
    weights_all = dp_gather(jnp.concatenate([w_query, w_key, value_matrix], axis=1))
    projected = jnp.dot(tokens, weights_all, preferred_element_type=jnp.float32)
    cosine, sine_table = position_tables(tokens.shape[0], HEAD_SIZE)
    combined = attention_fused(projected, grad_out, cosine[:, 0, :], sine_table[:, 0, :])
    native_rows = combined.shape[0] * 3 // 4

    def token_grads(rows):
        return lax.dot_general(
            rows, weights_all, (((1,), (1,)), ((), ())), preferred_element_type=jnp.float32
        ).astype(jnp.bfloat16)

    grad_tokens = jnp.concatenate(
        [
            lax.psum_scatter(
                token_grads(combined[:native_rows]), TP_AXES, scatter_dimension=1, tiled=True
            ),
            tp_scatter(token_grads(combined[native_rows:])),
        ],
        axis=0,
    )
    grads_all = dp_scatter_t(
        lax.dot_general(
            combined, tokens, (((0,), (0,)), ((), ())), preferred_element_type=jnp.float32
        ).astype(jnp.bfloat16)
    )
    grad_query = grads_all[:, :query_cols]
    grad_key = grads_all[:, query_cols : query_cols + key_value_columns]
    grad_value = grads_all[:, query_cols + key_value_columns :]
    return (grad_tokens, grad_query, grad_key, grad_value)


def solution(mesh):
    view = Mesh(mesh.devices.reshape(4, 2, 4, 2, 2), DP_AXES + TP_AXES)
    rows = P(DP_AXES, None)
    split = P(DP_AXES, TP_AXES)
    in_specs = (rows, split, split, split, split)
    out_specs = (split, split, split, split)
    return jax.shard_map(body, mesh=view, in_specs=in_specs, out_specs=out_specs, check_vma=False)
```

```python
import jax
import jax.numpy as jnp
from jax import lax
from jax.experimental import pallas as pl
from jax.experimental.pallas import tpu as pltpu
from jax.sharding import Mesh
from jax.sharding import PartitionSpec as P

MODEL_WIDTH = 4096
HEAD_SIZE = 128


rope_base = 500000.0


def position_tables(length, head_dim):
    half_dim = head_dim // 2
    positions = jnp.arange(length, dtype=jnp.float32)
    inverse = jnp.power(
        jnp.float32(rope_base), -2.0 * jnp.arange(half_dim, dtype=jnp.float32) / head_dim
    )
    angles = positions[:, None] * inverse[None, :]
    cosine = jnp.concatenate([jnp.cos(angles), jnp.cos(angles)], axis=-1)[:, None, :]
    sine_table = jnp.concatenate([jnp.sin(angles), jnp.sin(angles)], axis=-1)[:, None, :]
    return (cosine, sine_table)


def half_turn(values):
    lower, upper = jnp.split(values, 2, axis=-1)
    return jnp.concatenate([-upper, lower], axis=-1)


def rotate_forward(values, cosine, sine_table):
    return values * cosine + half_turn(values) * sine_table


def rotate_back(grads, cosine, sine_table):
    return grads * cosine - half_turn(grads * sine_table)


def _turn(x):
    rolled = pltpu.roll(x, HEAD_SIZE // 2, 1)
    lane = lax.broadcasted_iota(jnp.int32, x.shape, 1)
    return jnp.where(lane < HEAD_SIZE // 2, -rolled, rolled)


def _fused_kernel(q_ref, k_ref, v_ref, do_ref, cos_ref, sin_ref, out_ref, dk_acc, dv_acc):
    h = pl.program_id(0)
    heads = pl.num_programs(0)
    scale = 1.0 / jnp.sqrt(jnp.float32(HEAD_SIZE))
    cosine = cos_ref[...]
    sine = sin_ref[...]
    q_raw = q_ref[...]
    k_raw = k_ref[...]
    q = (q_raw * cosine + _turn(q_raw) * sine).astype(jnp.bfloat16)
    k = (k_raw * cosine + _turn(k_raw) * sine).astype(jnp.bfloat16)
    v = v_ref[...].astype(jnp.bfloat16)
    nt = (((1,), (1,)), ((), ()))
    tn = (((0,), (0,)), ((), ()))
    length = q.shape[0]
    step = length // 4
    dq_rows = []
    dk = jnp.zeros((length, HEAD_SIZE), jnp.float32)
    dv = jnp.zeros((length, HEAD_SIZE), jnp.float32)
    for i in range(4):
        lo, hi = i * step, (i + 1) * step
        q_i = q[lo:hi]
        k_i = k[:hi]
        do_i = do_ref[lo:hi, :]
        s = lax.dot_general(q_i, k_i, nt, preferred_element_type=jnp.float32) * scale
        rows = lax.broadcasted_iota(jnp.int32, s.shape, 0) + lo
        cols = lax.broadcasted_iota(jnp.int32, s.shape, 1)
        s = jnp.where(rows >= cols, s, -jnp.inf)
        m = jnp.max(s, axis=1, keepdims=True)
        e = jnp.exp(s - m)
        w = e / jnp.sum(e, axis=1, keepdims=True)
        dp = lax.dot_general(do_i, v[:hi], nt, preferred_element_type=jnp.float32)
        rd = jnp.sum(w * dp, axis=1, keepdims=True)
        ds = (w * (dp - rd) * scale).astype(jnp.bfloat16)
        dq_rows.append(jnp.dot(ds, k_i, preferred_element_type=jnp.float32))
        dk_i = lax.dot_general(ds, q_i, tn, preferred_element_type=jnp.float32)
        dv_i = lax.dot_general(w.astype(jnp.bfloat16), do_i, tn, preferred_element_type=jnp.float32)
        if hi < length:
            pad = jnp.zeros((length - hi, HEAD_SIZE), jnp.float32)
            dk_i = jnp.concatenate([dk_i, pad], axis=0)
            dv_i = jnp.concatenate([dv_i, pad], axis=0)
        dk = dk + dk_i
        dv = dv + dv_i
    dq = jnp.concatenate(dq_rows, axis=0)
    dq = dq * cosine - _turn(dq * sine)
    out_ref[:, pl.ds(pl.multiple_of(h * HEAD_SIZE, HEAD_SIZE), HEAD_SIZE)] = dq.astype(jnp.bfloat16)

    @pl.when(h == 0)
    def _():
        dk_acc[...] = dk
        dv_acc[...] = dv

    @pl.when(h > 0)
    def _():
        dk_acc[...] += dk
        dv_acc[...] += dv

    @pl.when(h == heads - 1)
    def _():
        g = dk_acc[...]
        g = g * cosine - _turn(g * sine)
        out_ref[:, pl.ds(heads * HEAD_SIZE, HEAD_SIZE)] = g.astype(jnp.bfloat16)
        out_ref[:, pl.ds((heads + 1) * HEAD_SIZE, HEAD_SIZE)] = dv_acc[...].astype(jnp.bfloat16)


def attention_fused(projected, upstream, cosine, sine):
    length, width = projected.shape
    heads = width // HEAD_SIZE - 2
    per_head = pl.BlockSpec((length, HEAD_SIZE), lambda h: (0, h))
    key_block = pl.BlockSpec((length, HEAD_SIZE), lambda h: (0, heads))
    value_block = pl.BlockSpec((length, HEAD_SIZE), lambda h: (0, heads + 1))
    table = pl.BlockSpec((length, HEAD_SIZE), lambda h: (0, 0))
    return pl.pallas_call(
        _fused_kernel,
        grid=(heads,),
        in_specs=[per_head, key_block, value_block, per_head, table, table],
        out_specs=pl.BlockSpec((length, width), lambda h: (0, 0)),
        out_shape=jax.ShapeDtypeStruct((length, width), jnp.bfloat16),
        scratch_shapes=[pltpu.VMEM((length, HEAD_SIZE), jnp.float32)] * 2,
        compiler_params=pltpu.CompilerParams(dimension_semantics=("arbitrary",)),
    )(projected, projected, projected, upstream, cosine, sine)


DP_AXES = ("y", "zl", "x")
TP_AXES = ("zh", "c")


def _shift(x, axis, n, step):
    return lax.ppermute(x, axis, [(k, (k + step) % n) for k in range(n)])


def _place(parts, idx, n, dim):
    shape = list(parts[0].shape)
    size = shape[dim]
    shape[dim] = size * n
    out = jnp.zeros(shape, parts[0].dtype)
    for o, p in enumerate(parts):
        start = [0] * len(shape)
        start[dim] = ((idx + o) % n) * size
        out = lax.dynamic_update_slice(out, p, start)
    return out


def ring_gather(x, axis, n, dim):
    idx = lax.axis_index(axis)
    if n == 1:
        return x
    if n == 2:
        return _place([x, _shift(x, axis, 2, 1)], idx, 2, dim)
    assert n == 4
    from_left = _shift(x, axis, 4, 1)
    from_right = _shift(x, axis, 4, -1)
    half = x.shape[-1] // 2
    far_a = _shift(from_right[..., :half], axis, 4, -1)
    far_b = _shift(from_left[..., half:], axis, 4, 1)
    far = jnp.concatenate([far_a, far_b], axis=-1)
    return _place([x, from_right, far, from_left], idx, 4, dim)


def _take(x, pos, dim, n):
    size = x.shape[dim] // n
    return lax.dynamic_slice_in_dim(x, pos * size, size, dim)


def _add(a, b):
    return (a.astype(jnp.float32) + b.astype(jnp.float32)).astype(a.dtype)


def _halves(x, hdim):
    half = x.shape[hdim] // 2
    return (lax.slice_in_dim(x, 0, half, axis=hdim), lax.slice_in_dim(x, half, 2 * half, axis=hdim))


def ring_scatter(x, axis, n, take, hdim=0):
    idx = lax.axis_index(axis)
    if n == 2:
        return _add(take(x, idx), _shift(take(x, (idx + 1) % 2), axis, 2, 1))
    assert n == 4
    far_a, far_b = _halves(take(x, (idx + 2) % 4), hdim)
    right_a, right_b = _halves(take(x, (idx + 1) % 4), hdim)
    left_a, left_b = _halves(take(x, (idx + 3) % 4), hdim)
    got_a = _shift(far_a, axis, 4, 1)
    got_b = _shift(far_b, axis, 4, -1)
    to_right = jnp.concatenate([_add(right_a, got_a), right_b], axis=hdim)
    to_left = jnp.concatenate([left_a, _add(left_b, got_b)], axis=hdim)
    mine = take(x, idx)
    s = _add(mine, _shift(to_right, axis, 4, 1))
    return _add(s, _shift(to_left, axis, 4, -1))


def _cols(starts, width):
    def take(x, j):
        runs = [lax.dynamic_slice_in_dim(x, s(j), width, axis=1) for s in starts]
        return runs[0] if len(runs) == 1 else jnp.concatenate(runs, axis=1)

    return take


def dp_gather(w, sizes=(4, 2, 4)):
    ny, nz, nx = sizes
    r, c = w.shape
    a = w.reshape(1, 1, 1, r, c)
    a = ring_gather(a, "zl", nz, 1)
    h = c // 2
    s1 = ring_gather(ring_gather(a[..., :h], "x", nx, 2), "y", ny, 0)
    s2 = ring_gather(ring_gather(a[..., h:], "y", ny, 0), "x", nx, 2)
    return jnp.concatenate([s1, s2], axis=-1).reshape(ny * nz * nx * r, c)


def dp_scatter_t(g, sizes=(4, 2, 4)):
    ny, nz, nx = sizes
    c, R = g.shape
    r = R // (ny * nz * nx)
    h = c // 2
    zx = nz * nx * r
    s1 = ring_scatter(g[:h], "y", ny, _cols([lambda j: j * zx], zx))
    s1 = ring_scatter(s1, "x", nx, _cols([lambda j, z=z: z * nx * r + j * r for z in range(nz)], r))
    s2 = ring_scatter(
        g[h:], "x", nx,
        _cols([lambda j, k=k: k * nx * r + j * r for k in range(ny * nz)], r),
    )
    s2 = ring_scatter(s2, "y", ny, _cols([lambda j: j * nz * r], nz * r))
    a = jnp.concatenate([s1, s2], axis=0)
    a = ring_scatter(a, "zl", nz, _cols([lambda j: j * r], r))
    return a.T


def tp_scatter(t):
    w = t.shape[1] // 4
    t = ring_scatter(t, "c", 2, _cols([lambda j, z=z: z * 2 * w + j * w for z in range(2)], w))
    return ring_scatter(t, "zh", 2, _cols([lambda j: j * w], w))


def body(tokens, grad_out, w_query, w_key, value_matrix):
    query_cols = w_query.shape[1]
    key_value_columns = w_key.shape[1]
    kv_dev = key_value_columns // HEAD_SIZE
    weights_all = dp_gather(jnp.concatenate([w_query, w_key, value_matrix], axis=1))
    projected = jnp.dot(tokens, weights_all, preferred_element_type=jnp.float32)
    cosine, sine_table = position_tables(tokens.shape[0], HEAD_SIZE)
    combined = attention_fused(projected, grad_out, cosine[:, 0, :], sine_table[:, 0, :])
    native_rows = combined.shape[0] // 2

    def token_grads(rows):
        return lax.dot_general(
            rows, weights_all, (((1,), (1,)), ((), ())), preferred_element_type=jnp.float32
        ).astype(jnp.bfloat16)

    grad_tokens = jnp.concatenate(
        [
            lax.psum_scatter(
                token_grads(combined[:native_rows]), TP_AXES, scatter_dimension=1, tiled=True
            ),
            tp_scatter(token_grads(combined[native_rows:])),
        ],
        axis=0,
    )
    grads_all = dp_scatter_t(
        lax.dot_general(
            combined, tokens, (((0,), (0,)), ((), ())), preferred_element_type=jnp.float32
        ).astype(jnp.bfloat16)
    )
    grad_query = grads_all[:, :query_cols]
    grad_key = grads_all[:, query_cols : query_cols + key_value_columns]
    grad_value = grads_all[:, query_cols + key_value_columns :]
    return (grad_tokens, grad_query, grad_key, grad_value)


def solution(mesh):
    view = Mesh(mesh.devices.reshape(4, 2, 4, 2, 2), DP_AXES + TP_AXES)
    rows = P(DP_AXES, None)
    split = P(DP_AXES, TP_AXES)
    in_specs = (rows, split, split, split, split)
    out_specs = (split, split, split, split)
    return jax.shard_map(body, mesh=view, in_specs=in_specs, out_specs=out_specs, check_vma=False)
```

```python
import jax
import jax.numpy as jnp
from jax import lax
from jax.experimental import pallas as pl
from jax.experimental.pallas import tpu as pltpu
from jax.sharding import Mesh
from jax.sharding import PartitionSpec as P

MODEL_WIDTH = 4096
HEAD_SIZE = 128


rope_base = 500000.0


def position_tables(length, head_dim):
    half_dim = head_dim // 2
    positions = jnp.arange(length, dtype=jnp.float32)
    inverse = jnp.power(
        jnp.float32(rope_base), -2.0 * jnp.arange(half_dim, dtype=jnp.float32) / head_dim
    )
    angles = positions[:, None] * inverse[None, :]
    cosine = jnp.concatenate([jnp.cos(angles), jnp.cos(angles)], axis=-1)[:, None, :]
    sine_table = jnp.concatenate([jnp.sin(angles), jnp.sin(angles)], axis=-1)[:, None, :]
    return (cosine, sine_table)


def half_turn(values):
    lower, upper = jnp.split(values, 2, axis=-1)
    return jnp.concatenate([-upper, lower], axis=-1)


def rotate_forward(values, cosine, sine_table):
    return values * cosine + half_turn(values) * sine_table


def rotate_back(grads, cosine, sine_table):
    return grads * cosine - half_turn(grads * sine_table)


def _turn(x):
    rolled = pltpu.roll(x, HEAD_SIZE // 2, 1)
    lane = lax.broadcasted_iota(jnp.int32, x.shape, 1)
    return jnp.where(lane < HEAD_SIZE // 2, -rolled, rolled)


def _fused_kernel(q_ref, k_ref, v_ref, do_ref, cos_ref, sin_ref, out_ref, dk_acc, dv_acc):
    h = pl.program_id(0)
    heads = pl.num_programs(0)
    scale = 1.0 / jnp.sqrt(jnp.float32(HEAD_SIZE))
    cosine = cos_ref[...]
    sine = sin_ref[...]
    q_raw = q_ref[...]
    k_raw = k_ref[...]
    q = (q_raw * cosine + _turn(q_raw) * sine).astype(jnp.bfloat16)
    k = (k_raw * cosine + _turn(k_raw) * sine).astype(jnp.bfloat16)
    v = v_ref[...].astype(jnp.bfloat16)
    nt = (((1,), (1,)), ((), ()))
    tn = (((0,), (0,)), ((), ()))
    length = q.shape[0]
    step = length // 4
    dq_rows = []
    dk = jnp.zeros((length, HEAD_SIZE), jnp.float32)
    dv = jnp.zeros((length, HEAD_SIZE), jnp.float32)
    for i in range(4):
        lo, hi = i * step, (i + 1) * step
        q_i = q[lo:hi]
        k_i = k[:hi]
        do_i = do_ref[lo:hi, :]
        s = lax.dot_general(q_i, k_i, nt, preferred_element_type=jnp.float32) * scale
        rows = lax.broadcasted_iota(jnp.int32, s.shape, 0) + lo
        cols = lax.broadcasted_iota(jnp.int32, s.shape, 1)
        s = jnp.where(rows >= cols, s, -jnp.inf)
        m = jnp.max(s, axis=1, keepdims=True)
        e = jnp.exp(s - m)
        w = e / jnp.sum(e, axis=1, keepdims=True)
        dp = lax.dot_general(do_i, v[:hi], nt, preferred_element_type=jnp.float32)
        rd = jnp.sum(w * dp, axis=1, keepdims=True)
        ds = (w * (dp - rd) * scale).astype(jnp.bfloat16)
        dq_rows.append(jnp.dot(ds, k_i, preferred_element_type=jnp.float32))
        dk_i = lax.dot_general(ds, q_i, tn, preferred_element_type=jnp.float32)
        dv_i = lax.dot_general(w.astype(jnp.bfloat16), do_i, tn, preferred_element_type=jnp.float32)
        if hi < length:
            pad = jnp.zeros((length - hi, HEAD_SIZE), jnp.float32)
            dk_i = jnp.concatenate([dk_i, pad], axis=0)
            dv_i = jnp.concatenate([dv_i, pad], axis=0)
        dk = dk + dk_i
        dv = dv + dv_i
    dq = jnp.concatenate(dq_rows, axis=0)
    dq = dq * cosine - _turn(dq * sine)
    out_ref[:, pl.ds(pl.multiple_of(h * HEAD_SIZE, HEAD_SIZE), HEAD_SIZE)] = dq.astype(jnp.bfloat16)

    @pl.when(h == 0)
    def _():
        dk_acc[...] = dk
        dv_acc[...] = dv

    @pl.when(h > 0)
    def _():
        dk_acc[...] += dk
        dv_acc[...] += dv

    @pl.when(h == heads - 1)
    def _():
        g = dk_acc[...]
        g = g * cosine - _turn(g * sine)
        out_ref[:, pl.ds(heads * HEAD_SIZE, HEAD_SIZE)] = g.astype(jnp.bfloat16)
        out_ref[:, pl.ds((heads + 1) * HEAD_SIZE, HEAD_SIZE)] = dv_acc[...].astype(jnp.bfloat16)


def attention_fused(projected, upstream, cosine, sine):
    length, width = projected.shape
    heads = width // HEAD_SIZE - 2
    per_head = pl.BlockSpec((length, HEAD_SIZE), lambda h: (0, h))
    key_block = pl.BlockSpec((length, HEAD_SIZE), lambda h: (0, heads))
    value_block = pl.BlockSpec((length, HEAD_SIZE), lambda h: (0, heads + 1))
    table = pl.BlockSpec((length, HEAD_SIZE), lambda h: (0, 0))
    return pl.pallas_call(
        _fused_kernel,
        grid=(heads,),
        in_specs=[per_head, key_block, value_block, per_head, table, table],
        out_specs=pl.BlockSpec((length, width), lambda h: (0, 0)),
        out_shape=jax.ShapeDtypeStruct((length, width), jnp.bfloat16),
        scratch_shapes=[pltpu.VMEM((length, HEAD_SIZE), jnp.float32)] * 2,
        compiler_params=pltpu.CompilerParams(dimension_semantics=("arbitrary",)),
    )(projected, projected, projected, upstream, cosine, sine)


DP_AXES = ("y", "zl", "x")
TP_AXES = ("zh", "c")


def _shift(x, axis, n, step):
    return lax.ppermute(x, axis, [(k, (k + step) % n) for k in range(n)])


def _place(parts, idx, n, dim):
    shape = list(parts[0].shape)
    size = shape[dim]
    shape[dim] = size * n
    out = jnp.zeros(shape, parts[0].dtype)
    for o, p in enumerate(parts):
        start = [0] * len(shape)
        start[dim] = ((idx + o) % n) * size
        out = lax.dynamic_update_slice(out, p, start)
    return out


def ring_gather(x, axis, n, dim):
    idx = lax.axis_index(axis)
    if n == 1:
        return x
    if n == 2:
        return _place([x, _shift(x, axis, 2, 1)], idx, 2, dim)
    assert n == 4
    from_left = _shift(x, axis, 4, 1)
    from_right = _shift(x, axis, 4, -1)
    half = x.shape[-1] // 2
    far_a = _shift(from_right[..., :half], axis, 4, -1)
    far_b = _shift(from_left[..., half:], axis, 4, 1)
    far = jnp.concatenate([far_a, far_b], axis=-1)
    return _place([x, from_right, far, from_left], idx, 4, dim)


def _take(x, pos, dim, n):
    size = x.shape[dim] // n
    return lax.dynamic_slice_in_dim(x, pos * size, size, dim)


def _add(a, b):
    return (a.astype(jnp.float32) + b.astype(jnp.float32)).astype(a.dtype)


def _halves(x, hdim):
    half = x.shape[hdim] // 2
    return (lax.slice_in_dim(x, 0, half, axis=hdim), lax.slice_in_dim(x, half, 2 * half, axis=hdim))


def ring_scatter(x, axis, n, take, hdim=0):
    idx = lax.axis_index(axis)
    if n == 2:
        return _add(take(x, idx), _shift(take(x, (idx + 1) % 2), axis, 2, 1))
    assert n == 4
    far_a, far_b = _halves(take(x, (idx + 2) % 4), hdim)
    right_a, right_b = _halves(take(x, (idx + 1) % 4), hdim)
    left_a, left_b = _halves(take(x, (idx + 3) % 4), hdim)
    got_a = _shift(far_a, axis, 4, 1)
    got_b = _shift(far_b, axis, 4, -1)
    to_right = jnp.concatenate([_add(right_a, got_a), right_b], axis=hdim)
    to_left = jnp.concatenate([left_a, _add(left_b, got_b)], axis=hdim)
    mine = take(x, idx)
    s = _add(mine, _shift(to_right, axis, 4, 1))
    return _add(s, _shift(to_left, axis, 4, -1))


def _cols(starts, width):
    def take(x, j):
        runs = [lax.dynamic_slice_in_dim(x, s(j), width, axis=1) for s in starts]
        return runs[0] if len(runs) == 1 else jnp.concatenate(runs, axis=1)

    return take


def dp_gather(w, sizes=(4, 2, 4)):
    ny, nz, nx = sizes
    r, c = w.shape
    a = w.reshape(1, 1, 1, r, c)
    a = ring_gather(a, "zl", nz, 1)
    h = c // 2
    s1 = ring_gather(ring_gather(a[..., :h], "x", nx, 2), "y", ny, 0)
    s2 = ring_gather(ring_gather(a[..., h:], "y", ny, 0), "x", nx, 2)
    return jnp.concatenate([s1, s2], axis=-1).reshape(ny * nz * nx * r, c)


def dp_scatter_t(g, sizes=(4, 2, 4)):
    ny, nz, nx = sizes
    c, R = g.shape
    r = R // (ny * nz * nx)
    h = c // 2
    zx = nz * nx * r
    s1 = ring_scatter(g[:h], "y", ny, _cols([lambda j: j * zx], zx))
    s1 = ring_scatter(s1, "x", nx, _cols([lambda j, z=z: z * nx * r + j * r for z in range(nz)], r))
    s2 = ring_scatter(
        g[h:], "x", nx,
        _cols([lambda j, k=k: k * nx * r + j * r for k in range(ny * nz)], r),
    )
    s2 = ring_scatter(s2, "y", ny, _cols([lambda j: j * nz * r], nz * r))
    a = jnp.concatenate([s1, s2], axis=0)
    a = ring_scatter(a, "zl", nz, _cols([lambda j: j * r], r))
    return a.T


def tp_scatter(t):
    w = t.shape[1] // 4
    t = ring_scatter(t, "c", 2, _cols([lambda j, z=z: z * 2 * w + j * w for z in range(2)], w))
    return ring_scatter(t, "zh", 2, _cols([lambda j: j * w], w))


def body(tokens, grad_out, w_query, w_key, value_matrix):
    query_cols = w_query.shape[1]
    key_value_columns = w_key.shape[1]
    kv_dev = key_value_columns // HEAD_SIZE
    weights_all = dp_gather(jnp.concatenate([w_query, w_key, value_matrix], axis=1))
    projected = jnp.dot(tokens, weights_all, preferred_element_type=jnp.float32)
    cosine, sine_table = position_tables(tokens.shape[0], HEAD_SIZE)
    combined = attention_fused(projected, grad_out, cosine[:, 0, :], sine_table[:, 0, :])
    native_rows = combined.shape[0] * 7 // 8

    def token_grads(rows):
        return lax.dot_general(
            rows, weights_all, (((1,), (1,)), ((), ())), preferred_element_type=jnp.float32
        ).astype(jnp.bfloat16)

    grad_tokens = jnp.concatenate(
        [
            lax.psum_scatter(
                token_grads(combined[:native_rows]), TP_AXES, scatter_dimension=1, tiled=True
            ),
            tp_scatter(token_grads(combined[native_rows:])),
        ],
        axis=0,
    )
    grads_all = dp_scatter_t(
        lax.dot_general(
            combined, tokens, (((0,), (0,)), ((), ())), preferred_element_type=jnp.float32
        ).astype(jnp.bfloat16)
    )
    grad_query = grads_all[:, :query_cols]
    grad_key = grads_all[:, query_cols : query_cols + key_value_columns]
    grad_value = grads_all[:, query_cols + key_value_columns :]
    return (grad_tokens, grad_query, grad_key, grad_value)


def solution(mesh):
    view = Mesh(mesh.devices.reshape(4, 2, 4, 2, 2), DP_AXES + TP_AXES)
    rows = P(DP_AXES, None)
    split = P(DP_AXES, TP_AXES)
    in_specs = (rows, split, split, split, split)
    out_specs = (split, split, split, split)
    return jax.shard_map(body, mesh=view, in_specs=in_specs, out_specs=out_specs, check_vma=False)
```
